32 devices in a mesh: sec: 4 (over z), blk: 8 (over y, x, core).
Axes of the slice: x: 2, y: 2, z: 4, core: 2. Of those that a mesh axis runs over, the one named last changes fastest.
Arguments:
- receptor: bfloat16 [16384, 1024], P(('sec', 'blk')), may hold values from -6 to 6
- poses: bfloat16 [4096, 1024], P(('sec', 'blk')), may hold values from -6 to 6
- pairs: int32 [8192, 2], P(('sec', 'blk')), may hold values from 0 to 127
- block_complex: int32 [32], replicated, may hold values from 0 to 15, never falling along the last dimension, each value on 1 to 4 neighbouring positions
- w_key: bfloat16 [1024, 1024], P('blk'), may hold values from -0.1875 to 0.1875
- w_value: bfloat16 [1024, 1024], P('blk'), may hold values from -0.1875 to 0.1875
- w_query: bfloat16 [1024, 1024], replicated, may hold values from -0.1875 to 0.1875
- score_weight: float32 [1024], replicated, may hold values from -24 to 24
Outputs:
- pair_loss: float32 [8192], P(('sec', 'blk'))
- pose_grad: bfloat16 [4096, 1024], P(('sec', 'blk'))
- receptor_grad: bfloat16 [16384, 1024], P(('sec', 'blk'))
The draws below stay inside these ranges and needn't reach their ends.
Inputs may be any that keep to these rules, and one draw needn't show every extreme that they name: `block_complex`: never falls from one block to the next; each complex holds 1 to 4 consecutive blocks, and some complex holds exactly 4. `pairs`: indices among the 128 poses beside the pair's block.
All inputs are finite; a program needn't handle non-finite values.
Results may differ from the reference program's by a relative error of at most 0.014.
Values may be sent and summed in bfloat16 or wider, within the bound.
No kernel may reach another device: no remote copies, remote signals or barrier semaphores. Data moves between devices by JAX's collectives and lax.ppermute only.
A program may use at most 64 MiB of HBM per device.

```python
import math
import jax
import jax.numpy as jnp
import numpy as np
from jax import lax

D = 1024
H = 16
DH = 64
RES_DEV = 512
POSE_DEV = 128
PAIR_DEV = 256
MOSTB = 4
NBLK = 32
NCPLX = 16
RES = 16384
POSES = 4096
NPAIRS = 8192


def plant(values, own_key, low, top_value):
    place = [jax.random.randint(jax.random.fold_in(own_key, axis), (), 0, length) for axis, length in enumerate(values.shape)]
    main_axis = values.shape.index(max(values.shape))
    beside = place[:main_axis] + [(place[main_axis] + 1) % values.shape[main_axis]] + place[main_axis + 1:]
    return values.at[tuple(place)].set(low).at[tuple(beside)].set(top_value)


def block_scale(own_key, dims, pieces, least, high):
    loudness = 1.0
    for dim, blocks in pieces:
        draws = jax.random.uniform(jax.random.fold_in(jax.random.fold_in(own_key, 6), dim), (blocks,), jnp.float32, least / len(pieces), high / len(pieces))
        loudness = loudness * jnp.repeat(jnp.exp(draws), dims[dim] // blocks).reshape((-1,) + (1,) * (len(dims) - 1 - dim))
    return loudness


def split_up(count, total, most, lean):
    weights = [(1 << 20) // math.isqrt(grade ** lean) + 1 for grade in range(2, count + 1)]
    spare, holding = total - most - (count - 1), [1] * (count - 1)
    while spare > 0:
        candidates = [i for i in range(count - 1) if holding[i] < most]
        mass, remaining = sum([weights[i] for i in candidates]), spare
        for i in candidates:
            more = min(most - holding[i], max(1, remaining * weights[i] // mass), spare)
            holding[i] = holding[i] + more
            spare = spare - more
    return np.array([most] + holding)


def uneven(rng, count, total, most, skew):
    if count == 2:
        one = jax.random.randint(rng, (), max(1, total - most), min(most, total - 1) + 1)
        return jnp.stack([one, total - one])
    lengths = jnp.asarray(split_up(count, total, most, skew), jnp.int32)
    couples = (count - 1) // 2
    source_of, sink = lengths[1:1 + 2 * couples:2], lengths[2:2 + 2 * couples:2]
    slack = jnp.minimum(source_of - 1, most - sink)
    passed = jax.random.randint(jax.random.fold_in(rng, 1), (couples,), 0, 1 << 20) % (slack + 1)
    lengths = lengths.at[1:1 + 2 * couples:2].set(source_of - passed).at[2:2 + 2 * couples:2].set(sink + passed)
    return lengths[jax.random.permutation(jax.random.fold_in(rng, 2), count)]


def centred(key, dims, deviation, most, pieces=(), kind=jnp.bfloat16):
    values = jax.random.normal(key, dims, jnp.float32) * deviation
    if len(pieces) > 0:
        values = block_scale(key, dims, pieces, -0.22, 0.18) * values
    return jnp.clip(values, min=-most, max=most).astype(kind)


def setup_inputs(seed: int = 0) -> dict:
    seeds = jax.random.split(jax.random.key(seed), 9)
    return {
        "receptor": centred(seeds[0], (RES, D), 1.0, 6.0, ((0, 32),)),
        "poses": centred(seeds[1], (POSES, D), 1.0, 6.0, ((0, 32),)),
        "pairs": plant(jax.random.randint(seeds[2], (NPAIRS, 2), 0, POSE_DEV), jax.random.fold_in(seeds[2], 1), 0, POSE_DEV - 1).astype(jnp.int32),
        "block_complex": jnp.searchsorted(jnp.cumsum(uneven(seeds[3], NCPLX, NBLK, MOSTB, 1)), jnp.arange(NBLK), side="right").astype(jnp.int32),
        "w_key": centred(seeds[4], (D, D), D ** -0.5, 0.1875, ((0, 8),)),
        "w_value": centred(seeds[5], (D, D), D ** -0.5, 0.1875, ((0, 8),)),
        "w_query": centred(seeds[6], (D, D), D ** -0.5, 0.1875),
        "score_weight": centred(seeds[7], (D,), 4.0, 24.0, (), jnp.float32),
    }


highest = lax.Precision.HIGHEST


def features(values):
    return jnp.where(values > 0, values + 1.0, jnp.exp(jnp.minimum(values, 0.0)))


def slope(values):
    return jnp.where(values > 0, jnp.ones_like(values), jnp.exp(jnp.minimum(values, 0.0)))


def block_state(key_feat, val_round):
    rows = key_feat.shape[0]
    key_heads = key_feat.astype(jnp.float32).reshape(rows, H, DH)
    val_heads = val_round.astype(jnp.float32).reshape(rows, H, DH)
    outer = jnp.einsum("thd,the->dhe", key_heads, val_heads, precision=highest).reshape(DH, H * DH)
    norm_row = jnp.sum(key_feat.astype(jnp.float32), axis=0)
    return jnp.concatenate([outer, norm_row[None, :]], axis=0)


def pose_side(pose_rows, pair_rows, state, w_query, score_weight):
    count = pose_rows.shape[0]
    queries = jnp.dot(pose_rows, w_query, preferred_element_type=jnp.float32)
    query_heads = features(queries).reshape(count, H, DH)
    state_heads = state[:DH].reshape(DH, H, DH)
    norm_heads = state[DH].reshape(H, DH)
    numer = jnp.einsum("phd,dhe->phe", query_heads, state_heads, precision=highest)
    denom = jnp.sum(query_heads * norm_heads[None], axis=2)
    attended = numer / denom[:, :, None]
    weight_heads = score_weight.reshape(H, DH)
    scores = jnp.sum(attended * weight_heads[None], axis=(1, 2))
    better = jnp.take(scores, pair_rows[:, 0])
    worse = jnp.take(scores, pair_rows[:, 1])
    delta = worse - better
    pair_loss = jax.nn.softplus(delta)
    push = jax.nn.sigmoid(delta)
    slots = lax.broadcasted_iota(jnp.int32, (pair_rows.shape[0], count), 1)
    score_grad = jnp.sum(jnp.where(slots == pair_rows[:, 1:2], push[:, None], 0.0)
                         - jnp.where(slots == pair_rows[:, 0:1], push[:, None], 0.0), axis=0)
    attended_grad = score_grad[:, None, None] * weight_heads[None]
    numer_grad = attended_grad / denom[:, :, None]
    denom_grad = -jnp.sum(attended_grad * attended, axis=2) / denom
    outer_grad = jnp.einsum("phd,phe->dhe", query_heads, numer_grad, precision=highest).reshape(DH, H * DH)
    norm_grad = jnp.sum(query_heads * denom_grad[:, :, None], axis=0).reshape(H * DH)
    pose_state = jnp.concatenate([outer_grad, norm_grad[None, :]], axis=0)
    feat_grad = jnp.einsum("phe,dhe->phd", numer_grad, state_heads, precision=highest) + denom_grad[:, :, None] * norm_heads[None]
    query_grad = (feat_grad.reshape(count, H * DH) * slope(queries)).astype(jnp.bfloat16)
    pose_grad = lax.dot_general(query_grad, w_query, (((1,), (1,)), ((), ())), preferred_element_type=jnp.float32)
    return pair_loss, pose_grad.astype(jnp.bfloat16), pose_state


def receptor_back(key_feat, val_round, keys, grad, w_key, w_value):
    rows = key_feat.shape[0]
    key_heads = key_feat.astype(jnp.float32).reshape(rows, H, DH)
    val_heads = val_round.astype(jnp.float32).reshape(rows, H, DH)
    grad_heads = grad[:DH].astype(jnp.float32).reshape(DH, H, DH)
    norm_back = grad[DH].astype(jnp.float32).reshape(H, DH)
    feat_grad = jnp.einsum("the,dhe->thd", val_heads, grad_heads, precision=highest) + norm_back[None]
    key_grad = (feat_grad.reshape(rows, H * DH) * slope(keys)).astype(jnp.bfloat16)
    value_grad = jnp.einsum("thd,dhe->the", key_heads, grad_heads, precision=highest).reshape(rows, H * DH).astype(jnp.bfloat16)
    total = lax.dot_general(key_grad, w_key, (((1,), (1,)), ((), ())), preferred_element_type=jnp.float32)
    total = total + lax.dot_general(value_grad, w_value, (((1,), (1,)), ((), ())), preferred_element_type=jnp.float32)
    return total.astype(jnp.bfloat16)


def reference(receptor, poses, pairs, block_complex, w_key, w_value, w_query, score_weight):
    blocks = receptor.reshape(NBLK, RES_DEV, D)

    def forward_block(block):
        keys = jnp.dot(block, w_key, preferred_element_type=jnp.float32)
        values = jnp.dot(block, w_value, preferred_element_type=jnp.float32)
        return block_state(features(keys).astype(jnp.bfloat16), values.astype(jnp.bfloat16))

    states = lax.map(forward_block, blocks)
    totals = jax.ops.segment_sum(states, block_complex, num_segments=NCPLX)
    complex_state = jnp.take(totals, block_complex, axis=0)

    def pose_block(items):
        return pose_side(items[0], items[1], items[2], w_query, score_weight)

    pair_loss, pose_grad, pose_states = lax.map(
        pose_block, (poses.reshape(NBLK, POSE_DEV, D), pairs.reshape(NBLK, PAIR_DEV, 2), complex_state))
    grad_totals = jax.ops.segment_sum(pose_states, block_complex, num_segments=NCPLX)
    state_grad = jnp.take(grad_totals, block_complex, axis=0).astype(jnp.bfloat16)

    def backward_block(items):
        block, grad = items
        keys = jnp.dot(block, w_key, preferred_element_type=jnp.float32)
        values = jnp.dot(block, w_value, preferred_element_type=jnp.float32)
        key_feat = features(keys).astype(jnp.bfloat16)
        val_round = values.astype(jnp.bfloat16)
        return receptor_back(key_feat, val_round, keys, grad, w_key, w_value)

    receptor_grad = lax.map(backward_block, (blocks, state_grad))
    return (pair_loss.reshape(NPAIRS), pose_grad.reshape(POSES, D), receptor_grad.reshape(RES, D))
```

```python
import jax
import jax.numpy as jnp
from jax import lax
from jax.sharding import PartitionSpec as P

H = 16
DH = 64
MOSTB = 4


highest = lax.Precision.HIGHEST


def from_behind(value, axis, steps):
    count = lax.axis_size(axis)
    initial, last = (max(0, -steps), min(count, count - steps))
    return lax.ppermute(value, axis, [(source, source + steps) for source in range(initial, last)])


def features(values):
    return jnp.where(values > 0, values + 1.0, jnp.exp(jnp.minimum(values, 0.0)))


def slope(values):
    return jnp.where(values > 0, jnp.ones_like(values), jnp.exp(jnp.minimum(values, 0.0)))


def local_state(key_feat, val_round):
    rows = key_feat.shape[0]
    key_heads = key_feat.reshape(rows, H, DH)
    val_heads = val_round.reshape(rows, H, DH)
    outer = jnp.einsum(
        "thd,the->dhe", key_heads, val_heads, preferred_element_type=jnp.float32
    ).reshape(DH, H * DH)
    norm_row = jnp.sum(key_feat, axis=0, dtype=jnp.float32)
    return jnp.concatenate([outer, norm_row[None, :]], axis=0)


def complex_total(own, block_complex):
    position = lax.axis_index(("sec", "blk"))
    blocks = block_complex.shape[0]
    mine = jnp.take(block_complex, position)
    total = own
    for reach in range(1, MOSTB):
        lower = from_behind(own.astype(jnp.bfloat16), ("sec", "blk"), reach).astype(own.dtype)
        upper = from_behind(own.astype(jnp.bfloat16), ("sec", "blk"), -reach).astype(own.dtype)
        below = jnp.take(block_complex, jnp.maximum(position - reach, 0))
        above = jnp.take(block_complex, jnp.minimum(position + reach, blocks - 1))
        take_lower = jnp.logical_and(position - reach >= 0, below == mine)
        take_upper = jnp.logical_and(position + reach < blocks, above == mine)
        total = total + jnp.where(take_lower, lower, 0.0) + jnp.where(take_upper, upper, 0.0)
    return total


def pose_side(pose_rows, pair_rows, state, w_query, score_weight):
    count = pose_rows.shape[0]
    queries = jnp.dot(pose_rows, w_query, preferred_element_type=jnp.float32)
    query_heads = features(queries).reshape(count, H, DH)
    state_heads = state[:DH].reshape(DH, H, DH)
    norm_heads = state[DH].reshape(H, DH)
    numer = jnp.einsum("phd,dhe->phe", query_heads, state_heads, precision=highest)
    denom = jnp.sum(query_heads * norm_heads[None], axis=2)
    attended = numer / denom[:, :, None]
    weight_heads = score_weight.reshape(H, DH)
    scores = jnp.sum(attended * weight_heads[None], axis=(1, 2))
    better = jnp.take(scores, pair_rows[:, 0])
    worse = jnp.take(scores, pair_rows[:, 1])
    delta = worse - better
    pair_loss = jax.nn.softplus(delta)
    push = jax.nn.sigmoid(delta)
    slots = lax.broadcasted_iota(jnp.int32, (pair_rows.shape[0], count), 1)
    score_grad = jnp.sum(
        jnp.where(slots == pair_rows[:, 1:2], push[:, None], 0.0)
        - jnp.where(slots == pair_rows[:, 0:1], push[:, None], 0.0),
        axis=0,
    )
    attended_grad = score_grad[:, None, None] * weight_heads[None]
    numer_grad = attended_grad / denom[:, :, None]
    denom_grad = -jnp.sum(attended_grad * attended, axis=2) / denom
    outer_grad = jnp.einsum("phd,phe->dhe", query_heads, numer_grad, precision=highest).reshape(
        DH, H * DH
    )
    norm_grad = jnp.sum(query_heads * denom_grad[:, :, None], axis=0).reshape(H * DH)
    pose_state = jnp.concatenate([outer_grad, norm_grad[None, :]], axis=0)
    feat_grad = (
        jnp.einsum("phe,dhe->phd", numer_grad, state_heads, precision=highest)
        + denom_grad[:, :, None] * norm_heads[None]
    )
    query_grad = (feat_grad.reshape(count, H * DH) * slope(queries)).astype(jnp.bfloat16)
    pose_grad = lax.dot_general(
        query_grad, w_query, (((1,), (1,)), ((), ())), preferred_element_type=jnp.float32
    )
    return (pair_loss, pose_grad.astype(jnp.bfloat16), pose_state)


def gather_rows(shard):
    count = lax.axis_size("blk")
    if count > 16 or count % 2:
        return lax.all_gather(shard, "blk", axis=0, tiled=True)
    position = lax.axis_index("blk")
    rows = shard.shape[0]
    got = [shard] + [
        lax.ppermute(shard, "blk", [(s, (s + 2 * k) % count) for s in range(count)])
        for k in range(1, count // 2)
    ]
    mine = jnp.stack(got)
    sibling = lax.ppermute(mine, "blk", [(s, s ^ 1) for s in range(count)])
    full = jnp.zeros((count,) + shard.shape, shard.dtype)
    for k in range(count // 2):
        full = lax.dynamic_update_slice(full, mine[k][None], ((position - 2 * k) % count, 0, 0))
        full = lax.dynamic_update_slice(
            full, sibling[k][None], (((position ^ 1) - 2 * k) % count, 0, 0)
        )
    return full.reshape(count * rows, shard.shape[1])


def shards(receptor, poses, pairs, block_complex, w_key, w_value, w_query, score_weight):
    rows = receptor.shape[0]
    width = receptor.shape[1]
    contract = (((1,), (1,)), ((), ()))
    full_both = gather_rows(jnp.concatenate([w_key, w_value], axis=1))
    both = jnp.dot(receptor, full_both, preferred_element_type=jnp.float32)
    keys = both[:, :width]
    values = both[:, width:]
    key_feat = features(keys).astype(jnp.bfloat16)
    val_round = values.astype(jnp.bfloat16)
    state = complex_total(local_state(key_feat, val_round), block_complex)
    pair_loss, pose_grad, pose_state = pose_side(poses, pairs, state, w_query, score_weight)
    state_grad = complex_total(pose_state, block_complex).astype(jnp.bfloat16)
    key_heads = key_feat.reshape(rows, H, DH)
    val_heads = val_round.reshape(rows, H, DH)
    grad_heads = state_grad[:DH].reshape(DH, H, DH)
    norm_back = state_grad[DH].astype(jnp.float32).reshape(H, DH)
    feat_grad = (
        jnp.einsum("the,dhe->thd", val_heads, grad_heads, preferred_element_type=jnp.float32)
        + norm_back[None]
    )
    key_grad = (feat_grad.reshape(rows, width) * slope(keys)).astype(jnp.bfloat16)
    value_grad = (
        jnp.einsum("thd,dhe->the", key_heads, grad_heads, preferred_element_type=jnp.float32)
        .reshape(rows, width)
        .astype(jnp.bfloat16)
    )
    both_grad = jnp.concatenate([key_grad, value_grad], axis=1)
    total = lax.dot_general(both_grad, full_both, contract, preferred_element_type=jnp.float32)
    return (pair_loss, pose_grad, total.astype(jnp.bfloat16))


def solution(mesh):
    placed = (
        P(("sec", "blk"), None),
        P(("sec", "blk"), None),
        P(("sec", "blk"), None),
        P(),
        P("blk", None),
        P("blk", None),
        P(),
        P(),
    )
    return jax.shard_map(
        shards,
        mesh=mesh,
        in_specs=placed,
        out_specs=(P(("sec", "blk")), P(("sec", "blk"), None), P(("sec", "blk"), None)),
        check_vma=False,
    )
```

```python
import jax
import jax.numpy as jnp
from jax import lax
from jax.sharding import PartitionSpec as P

H = 16
DH = 64
MOSTB = 4


highest = lax.Precision.HIGHEST


def from_behind(value, axis, steps):
    count = lax.axis_size(axis)
    initial, last = (max(0, -steps), min(count, count - steps))
    return lax.ppermute(value, axis, [(source, source + steps) for source in range(initial, last)])


def features(values):
    return jnp.where(values > 0, values + 1.0, jnp.exp(jnp.minimum(values, 0.0)))


def slope(values):
    return jnp.where(values > 0, jnp.ones_like(values), jnp.exp(jnp.minimum(values, 0.0)))


def local_state(key_feat, val_round):
    rows = key_feat.shape[0]
    key_heads = key_feat.reshape(rows, H, DH)
    val_heads = val_round.reshape(rows, H, DH)
    outer = jnp.einsum(
        "thd,the->dhe", key_heads, val_heads, preferred_element_type=jnp.float32
    ).reshape(DH, H * DH)
    norm_row = jnp.sum(key_feat, axis=0, dtype=jnp.float32)
    return jnp.concatenate([outer, norm_row[None, :]], axis=0)


def complex_total(own, block_complex):
    position = lax.axis_index(("sec", "blk"))
    blocks = block_complex.shape[0]
    mine = jnp.take(block_complex, position)
    total = own
    for reach in range(1, MOSTB):
        lower = from_behind(own.astype(jnp.bfloat16), ("sec", "blk"), reach).astype(own.dtype)
        upper = from_behind(own.astype(jnp.bfloat16), ("sec", "blk"), -reach).astype(own.dtype)
        below = jnp.take(block_complex, jnp.maximum(position - reach, 0))
        above = jnp.take(block_complex, jnp.minimum(position + reach, blocks - 1))
        take_lower = jnp.logical_and(position - reach >= 0, below == mine)
        take_upper = jnp.logical_and(position + reach < blocks, above == mine)
        total = total + jnp.where(take_lower, lower, 0.0) + jnp.where(take_upper, upper, 0.0)
    return total


def pose_side(pose_rows, pair_rows, state, w_query, score_weight):
    count = pose_rows.shape[0]
    queries = jnp.dot(pose_rows, w_query, preferred_element_type=jnp.float32)
    query_heads = features(queries).reshape(count, H, DH)
    state_heads = state[:DH].reshape(DH, H, DH)
    norm_heads = state[DH].reshape(H, DH)
    numer = jnp.einsum("phd,dhe->phe", query_heads, state_heads, precision=highest)
    denom = jnp.sum(query_heads * norm_heads[None], axis=2)
    attended = numer / denom[:, :, None]
    weight_heads = score_weight.reshape(H, DH)
    scores = jnp.sum(attended * weight_heads[None], axis=(1, 2))
    slots = lax.broadcasted_iota(jnp.int32, (pair_rows.shape[0], count), 1)
    is_better = slots == pair_rows[:, 0:1]
    is_worse = slots == pair_rows[:, 1:2]
    better = jnp.sum(jnp.where(is_better, scores[None, :], 0.0), axis=1)
    worse = jnp.sum(jnp.where(is_worse, scores[None, :], 0.0), axis=1)
    delta = worse - better
    pair_loss = jax.nn.softplus(delta)
    push = jax.nn.sigmoid(delta)
    score_grad = jnp.sum(
        jnp.where(is_worse, push[:, None], 0.0) - jnp.where(is_better, push[:, None], 0.0),
        axis=0,
    )
    attended_grad = score_grad[:, None, None] * weight_heads[None]
    numer_grad = attended_grad / denom[:, :, None]
    denom_grad = -jnp.sum(attended_grad * attended, axis=2) / denom
    outer_grad = jnp.einsum("phd,phe->dhe", query_heads, numer_grad, precision=highest).reshape(
        DH, H * DH
    )
    norm_grad = jnp.sum(query_heads * denom_grad[:, :, None], axis=0).reshape(H * DH)
    pose_state = jnp.concatenate([outer_grad, norm_grad[None, :]], axis=0)
    feat_grad = (
        jnp.einsum("phe,dhe->phd", numer_grad, state_heads, precision=highest)
        + denom_grad[:, :, None] * norm_heads[None]
    )
    query_grad = (feat_grad.reshape(count, H * DH) * slope(queries)).astype(jnp.bfloat16)
    pose_grad = lax.dot_general(
        query_grad, w_query, (((1,), (1,)), ((), ())), preferred_element_type=jnp.float32
    )
    return (pair_loss, pose_grad.astype(jnp.bfloat16), pose_state)


def gather_rows(shards):
    count = lax.axis_size("blk")
    rows = shards[0].shape[0]
    if count > 16 or count % 2 or rows % 128:
        full = tuple(lax.all_gather(part, "blk", axis=0, tiled=True) for part in shards)
        return full, None
    position = lax.axis_index("blk")
    got = [shards] + [
        lax.ppermute(shards, "blk", [(s, (s + 2 * k) % count) for s in range(count)])
        for k in range(1, count // 2)
    ]
    sibling = lax.ppermute(got, "blk", [(s, s ^ 1) for s in range(count)])
    pieces = got + sibling
    full = tuple(
        jnp.concatenate([piece[i] for piece in pieces], axis=0) for i in range(len(shards))
    )
    half = count // 2
    source = [(position - 2 * k) % count for k in range(half)] + [
        ((position ^ 1) - 2 * k) % count for k in range(half)
    ]
    slot = [
        jnp.where(
            (s - position) % 2 == 0,
            ((position - s) % count) // 2,
            half + (((position ^ 1) - s) % count) // 2,
        )
        for s in range(count)
    ]
    return full, (source, slot, rows)


def reorder_columns(values, order, rows):
    return jnp.concatenate(
        [lax.dynamic_slice_in_dim(values, where * rows, rows, axis=1) for where in order], axis=1
    )


def shards(receptor, poses, pairs, block_complex, w_key, w_value, w_query, score_weight):
    rows = receptor.shape[0]
    width = receptor.shape[1]
    contract = (((1,), (1,)), ((), ()))
    (full_key, full_value), order = gather_rows((w_key, w_value))
    moved = receptor if order is None else reorder_columns(receptor, order[0], order[2])
    keys = jnp.dot(moved, full_key, preferred_element_type=jnp.float32)
    values = jnp.dot(moved, full_value, preferred_element_type=jnp.float32)
    key_feat = features(keys).astype(jnp.bfloat16)
    val_round = values.astype(jnp.bfloat16)
    state = complex_total(local_state(key_feat, val_round), block_complex)
    pair_loss, pose_grad, pose_state = pose_side(poses, pairs, state, w_query, score_weight)
    state_grad = complex_total(pose_state, block_complex).astype(jnp.bfloat16)
    key_heads = key_feat.reshape(rows, H, DH)
    val_heads = val_round.reshape(rows, H, DH)
    grad_heads = state_grad[:DH].reshape(DH, H, DH)
    norm_back = state_grad[DH].astype(jnp.float32).reshape(H, DH)
    feat_grad = (
        jnp.einsum("the,dhe->thd", val_heads, grad_heads, preferred_element_type=jnp.float32)
        + norm_back[None]
    )
    key_grad = (feat_grad.reshape(rows, width) * slope(keys)).astype(jnp.bfloat16)
    value_grad = (
        jnp.einsum("thd,dhe->the", key_heads, grad_heads, preferred_element_type=jnp.float32)
        .reshape(rows, width)
        .astype(jnp.bfloat16)
    )
    total = lax.dot_general(key_grad, full_key, contract, preferred_element_type=jnp.float32)
    total = total + lax.dot_general(
        value_grad, full_value, contract, preferred_element_type=jnp.float32
    )
    total = total.astype(jnp.bfloat16)
    if order is not None:
        total = reorder_columns(total, order[1], order[2])
    return (pair_loss, pose_grad, total)


def solution(mesh):
    placed = (
        P(("sec", "blk"), None),
        P(("sec", "blk"), None),
        P(("sec", "blk"), None),
        P(),
        P("blk", None),
        P("blk", None),
        P(),
        P(),
    )
    return jax.shard_map(
        shards,
        mesh=mesh,
        in_specs=placed,
        out_specs=(P(("sec", "blk")), P(("sec", "blk"), None), P(("sec", "blk"), None)),
        check_vma=False,
    )
```

```python
import jax
import jax.numpy as jnp
from jax import lax
from jax.sharding import PartitionSpec as P

H = 16
DH = 64
MOSTB = 4


highest = lax.Precision.HIGHEST


def from_behind(value, axis, steps):
    count = lax.axis_size(axis)
    initial, last = (max(0, -steps), min(count, count - steps))
    return lax.ppermute(value, axis, [(source, source + steps) for source in range(initial, last)])


def features(values):
    return jnp.where(values > 0, values + 1.0, jnp.exp(jnp.minimum(values, 0.0)))


def slope(values):
    return jnp.where(values > 0, jnp.ones_like(values), jnp.exp(jnp.minimum(values, 0.0)))


def local_state(key_feat, val_round):
    rows = key_feat.shape[0]
    key_heads = key_feat.reshape(rows, H, DH)
    val_heads = val_round.reshape(rows, H, DH)
    outer = jnp.einsum(
        "thd,the->dhe", key_heads, val_heads, preferred_element_type=jnp.float32
    ).reshape(DH, H * DH)
    norm_row = jnp.sum(key_feat, axis=0, dtype=jnp.float32)
    return jnp.concatenate([outer, norm_row[None, :]], axis=0)


def complex_total(own, block_complex):
    position = lax.axis_index(("sec", "blk"))
    blocks = block_complex.shape[0]
    mine = jnp.take(block_complex, position)
    total = own
    for reach in range(1, MOSTB):
        lower = from_behind(own.astype(jnp.bfloat16), ("sec", "blk"), reach).astype(own.dtype)
        upper = from_behind(own.astype(jnp.bfloat16), ("sec", "blk"), -reach).astype(own.dtype)
        below = jnp.take(block_complex, jnp.maximum(position - reach, 0))
        above = jnp.take(block_complex, jnp.minimum(position + reach, blocks - 1))
        take_lower = jnp.logical_and(position - reach >= 0, below == mine)
        take_upper = jnp.logical_and(position + reach < blocks, above == mine)
        total = total + jnp.where(take_lower, lower, 0.0) + jnp.where(take_upper, upper, 0.0)
    return total


def pose_side(pose_rows, pair_rows, state, w_query, score_weight):
    count = pose_rows.shape[0]
    queries = jnp.dot(pose_rows, w_query, preferred_element_type=jnp.float32)
    query_heads = features(queries).reshape(count, H, DH)
    state_heads = state[:DH].reshape(DH, H, DH)
    norm_heads = state[DH].reshape(H, DH)
    numer = jnp.einsum("phd,dhe->phe", query_heads, state_heads, precision=highest)
    denom = jnp.sum(query_heads * norm_heads[None], axis=2)
    attended = numer / denom[:, :, None]
    weight_heads = score_weight.reshape(H, DH)
    scores = jnp.sum(attended * weight_heads[None], axis=(1, 2))
    slots = lax.broadcasted_iota(jnp.int32, (pair_rows.shape[0], count), 1)
    is_better = slots == pair_rows[:, 0:1]
    is_worse = slots == pair_rows[:, 1:2]
    better = jnp.sum(jnp.where(is_better, scores[None, :], 0.0), axis=1)
    worse = jnp.sum(jnp.where(is_worse, scores[None, :], 0.0), axis=1)
    delta = worse - better
    pair_loss = jax.nn.softplus(delta)
    push = jax.nn.sigmoid(delta)
    score_grad = jnp.sum(
        jnp.where(is_worse, push[:, None], 0.0) - jnp.where(is_better, push[:, None], 0.0),
        axis=0,
    )
    attended_grad = score_grad[:, None, None] * weight_heads[None]
    numer_grad = attended_grad / denom[:, :, None]
    denom_grad = -jnp.sum(attended_grad * attended, axis=2) / denom
    outer_grad = jnp.einsum("phd,phe->dhe", query_heads, numer_grad, precision=highest).reshape(
        DH, H * DH
    )
    norm_grad = jnp.sum(query_heads * denom_grad[:, :, None], axis=0).reshape(H * DH)
    pose_state = jnp.concatenate([outer_grad, norm_grad[None, :]], axis=0)
    feat_grad = (
        jnp.einsum("phe,dhe->phd", numer_grad, state_heads, precision=highest)
        + denom_grad[:, :, None] * norm_heads[None]
    )
    query_grad = (feat_grad.reshape(count, H * DH) * slope(queries)).astype(jnp.bfloat16)
    pose_grad = lax.dot_general(
        query_grad, w_query, (((1,), (1,)), ((), ())), preferred_element_type=jnp.float32
    )
    return (pair_loss, pose_grad.astype(jnp.bfloat16), pose_state)


def gather_rows(shard):
    count = lax.axis_size("blk")
    if count > 16 or count % 2:
        return lax.all_gather(shard, "blk", axis=0, tiled=True)
    position = lax.axis_index("blk")
    rows = shard.shape[0]
    got = [shard] + [
        lax.ppermute(shard, "blk", [(s, (s + 2 * k) % count) for s in range(count)])
        for k in range(1, count // 2)
    ]
    mine = jnp.stack(got)
    sibling = lax.ppermute(mine, "blk", [(s, s ^ 1) for s in range(count)])
    full = jnp.zeros((count,) + shard.shape, shard.dtype)
    for k in range(count // 2):
        full = lax.dynamic_update_slice(full, mine[k][None], ((position - 2 * k) % count, 0, 0))
        full = lax.dynamic_update_slice(
            full, sibling[k][None], (((position ^ 1) - 2 * k) % count, 0, 0)
        )
    return full.reshape(count * rows, shard.shape[1])


def shards(receptor, poses, pairs, block_complex, w_key, w_value, w_query, score_weight):
    rows = receptor.shape[0]
    width = receptor.shape[1]
    contract = (((1,), (1,)), ((), ()))
    full_both = gather_rows(jnp.concatenate([w_key, w_value], axis=1))
    both = jnp.dot(receptor, full_both, preferred_element_type=jnp.float32)
    keys = both[:, :width]
    values = both[:, width:]
    key_feat = features(keys).astype(jnp.bfloat16)
    val_round = values.astype(jnp.bfloat16)
    state = complex_total(local_state(key_feat, val_round), block_complex)
    pair_loss, pose_grad, pose_state = pose_side(poses, pairs, state, w_query, score_weight)
    state_grad = complex_total(pose_state, block_complex).astype(jnp.bfloat16)
    key_heads = key_feat.reshape(rows, H, DH)
    val_heads = val_round.reshape(rows, H, DH)
    grad_heads = state_grad[:DH].reshape(DH, H, DH)
    norm_back = state_grad[DH].astype(jnp.float32).reshape(H, DH)
    feat_grad = (
        jnp.einsum("the,dhe->thd", val_heads, grad_heads, preferred_element_type=jnp.float32)
        + norm_back[None]
    )
    key_grad = (feat_grad.reshape(rows, width) * slope(keys)).astype(jnp.bfloat16)
    value_grad = (
        jnp.einsum("thd,dhe->the", key_heads, grad_heads, preferred_element_type=jnp.float32)
        .reshape(rows, width)
        .astype(jnp.bfloat16)
    )
    both_grad = jnp.concatenate([key_grad, value_grad], axis=1)
    total = lax.dot_general(both_grad, full_both, contract, preferred_element_type=jnp.float32)
    return (pair_loss, pose_grad, total.astype(jnp.bfloat16))


def solution(mesh):
    placed = (
        P(("sec", "blk"), None),
        P(("sec", "blk"), None),
        P(("sec", "blk"), None),
        P(),
        P("blk", None),
        P("blk", None),
        P(),
        P(),
    )
    return jax.shard_map(
        shards,
        mesh=mesh,
        in_specs=placed,
        out_specs=(P(("sec", "blk")), P(("sec", "blk"), None), P(("sec", "blk"), None)),
        check_vma=False,
    )
```

```python
import jax
import jax.numpy as jnp
from jax import lax
from jax.sharding import PartitionSpec as P

H = 16
DH = 64
MOSTB = 4


highest = lax.Precision.HIGHEST


def from_behind(value, axis, steps):
    count = lax.axis_size(axis)
    initial, last = (max(0, -steps), min(count, count - steps))
    return lax.ppermute(value, axis, [(source, source + steps) for source in range(initial, last)])


def features(values):
    return jnp.where(values > 0, values + 1.0, jnp.exp(jnp.minimum(values, 0.0)))


def slope(values):
    return jnp.where(values > 0, jnp.ones_like(values), jnp.exp(jnp.minimum(values, 0.0)))


def local_state(key_feat, val_round):
    rows = key_feat.shape[0]
    key_heads = key_feat.reshape(rows, H, DH)
    val_heads = val_round.reshape(rows, H, DH)
    outer = jnp.einsum(
        "thd,the->dhe", key_heads, val_heads, preferred_element_type=jnp.float32
    ).reshape(DH, H * DH)
    norm_row = jnp.sum(key_feat, axis=0, dtype=jnp.float32)
    return jnp.concatenate([outer, norm_row[None, :]], axis=0)


def complex_total(own, block_complex):
    position = lax.axis_index(("sec", "blk"))
    blocks = block_complex.shape[0]
    mine = jnp.take(block_complex, position)
    total = own
    for reach in range(1, MOSTB):
        lower = from_behind(own.astype(jnp.bfloat16), ("sec", "blk"), reach).astype(own.dtype)
        upper = from_behind(own.astype(jnp.bfloat16), ("sec", "blk"), -reach).astype(own.dtype)
        below = jnp.take(block_complex, jnp.maximum(position - reach, 0))
        above = jnp.take(block_complex, jnp.minimum(position + reach, blocks - 1))
        take_lower = jnp.logical_and(position - reach >= 0, below == mine)
        take_upper = jnp.logical_and(position + reach < blocks, above == mine)
        total = total + jnp.where(take_lower, lower, 0.0) + jnp.where(take_upper, upper, 0.0)
    return total


def pose_side(pose_rows, pair_rows, state, w_query, score_weight):
    count = pose_rows.shape[0]
    queries = jnp.dot(pose_rows, w_query, preferred_element_type=jnp.float32)
    query_heads = features(queries).reshape(count, H, DH)
    state_heads = state[:DH].reshape(DH, H, DH)
    norm_heads = state[DH].reshape(H, DH)
    numer = jnp.einsum("phd,dhe->phe", query_heads, state_heads, precision=highest)
    denom = jnp.sum(query_heads * norm_heads[None], axis=2)
    attended = numer / denom[:, :, None]
    weight_heads = score_weight.reshape(H, DH)
    scores = jnp.sum(attended * weight_heads[None], axis=(1, 2))
    slots = lax.broadcasted_iota(jnp.int32, (pair_rows.shape[0], count), 1)
    is_better = slots == pair_rows[:, 0:1]
    is_worse = slots == pair_rows[:, 1:2]
    better = jnp.sum(jnp.where(is_better, scores[None, :], 0.0), axis=1)
    worse = jnp.sum(jnp.where(is_worse, scores[None, :], 0.0), axis=1)
    delta = worse - better
    pair_loss = jax.nn.softplus(delta)
    push = jax.nn.sigmoid(delta)
    score_grad = jnp.sum(
        jnp.where(is_worse, push[:, None], 0.0) - jnp.where(is_better, push[:, None], 0.0),
        axis=0,
    )
    attended_grad = score_grad[:, None, None] * weight_heads[None]
    numer_grad = attended_grad / denom[:, :, None]
    denom_grad = -jnp.sum(attended_grad * attended, axis=2) / denom
    outer_grad = jnp.einsum("phd,phe->dhe", query_heads, numer_grad, precision=highest).reshape(
        DH, H * DH
    )
    norm_grad = jnp.sum(query_heads * denom_grad[:, :, None], axis=0).reshape(H * DH)
    pose_state = jnp.concatenate([outer_grad, norm_grad[None, :]], axis=0)
    feat_grad = (
        jnp.einsum("phe,dhe->phd", numer_grad, state_heads, precision=highest)
        + denom_grad[:, :, None] * norm_heads[None]
    )
    query_grad = (feat_grad.reshape(count, H * DH) * slope(queries)).astype(jnp.bfloat16)
    pose_grad = lax.dot_general(
        query_grad, w_query, (((1,), (1,)), ((), ())), preferred_element_type=jnp.float32
    )
    return (pair_loss, pose_grad.astype(jnp.bfloat16), pose_state)


def gather_rows(shard):
    count = lax.axis_size("blk")
    if count != 8:
        return lax.all_gather(shard, "blk", axis=0, tiled=True)
    position = lax.axis_index("blk")
    rows = shard.shape[0]
    odd = position % 2
    first = jnp.where(odd == 1, 4, 2)
    second = 6 - first
    early = lax.ppermute(shard, "blk", [(s, s ^ (4 if s % 2 else 2)) for s in range(count)])
    late = lax.ppermute(
        jnp.stack([shard, early]), "blk", [(s, s ^ (2 if s % 2 else 4)) for s in range(count)]
    )
    mine = jnp.concatenate([jnp.stack([shard, early]), late], axis=0)
    sibling = lax.ppermute(mine, "blk", [(s, s ^ 1) for s in range(count)])
    twin = position ^ 1
    sources = [
        (mine, [position, position ^ first, position ^ second, position ^ 6]),
        (sibling, [twin, twin ^ second, twin ^ first, twin ^ 6]),
    ]
    full = jnp.zeros((count,) + shard.shape, shard.dtype)
    for pieces, where in sources:
        for k, at in enumerate(where):
            full = lax.dynamic_update_slice(full, pieces[k][None], (at, 0, 0))
    return full.reshape(count * rows, shard.shape[1])


def shards(receptor, poses, pairs, block_complex, w_key, w_value, w_query, score_weight):
    rows = receptor.shape[0]
    width = receptor.shape[1]
    contract = (((1,), (1,)), ((), ()))
    full_both = gather_rows(jnp.concatenate([w_key, w_value], axis=1))
    both = jnp.dot(receptor, full_both, preferred_element_type=jnp.float32)
    keys = both[:, :width]
    values = both[:, width:]
    key_feat = features(keys).astype(jnp.bfloat16)
    val_round = values.astype(jnp.bfloat16)
    state = complex_total(local_state(key_feat, val_round), block_complex)
    pair_loss, pose_grad, pose_state = pose_side(poses, pairs, state, w_query, score_weight)
    state_grad = complex_total(pose_state, block_complex).astype(jnp.bfloat16)
    key_heads = key_feat.reshape(rows, H, DH)
    val_heads = val_round.reshape(rows, H, DH)
    grad_heads = state_grad[:DH].reshape(DH, H, DH)
    norm_back = state_grad[DH].astype(jnp.float32).reshape(H, DH)
    feat_grad = (
        jnp.einsum("the,dhe->thd", val_heads, grad_heads, preferred_element_type=jnp.float32)
        + norm_back[None]
    )
    key_grad = (feat_grad.reshape(rows, width) * slope(keys)).astype(jnp.bfloat16)
    value_grad = (
        jnp.einsum("thd,dhe->the", key_heads, grad_heads, preferred_element_type=jnp.float32)
        .reshape(rows, width)
        .astype(jnp.bfloat16)
    )
    both_grad = jnp.concatenate([key_grad, value_grad], axis=1)
    total = lax.dot_general(both_grad, full_both, contract, preferred_element_type=jnp.float32)
    return (pair_loss, pose_grad, total.astype(jnp.bfloat16))


def solution(mesh):
    placed = (
        P(("sec", "blk"), None),
        P(("sec", "blk"), None),
        P(("sec", "blk"), None),
        P(),
        P("blk", None),
        P("blk", None),
        P(),
        P(),
    )
    return jax.shard_map(
        shards,
        mesh=mesh,
        in_specs=placed,
        out_specs=(P(("sec", "blk")), P(("sec", "blk"), None), P(("sec", "blk"), None)),
        check_vma=False,
    )
```

```python
import jax
import jax.numpy as jnp
from jax import lax
from jax.sharding import PartitionSpec as P

H = 16
DH = 64
MOSTB = 4


highest = lax.Precision.HIGHEST


def from_behind(value, axis, steps):
    count = lax.axis_size(axis)
    initial, last = (max(0, -steps), min(count, count - steps))
    return lax.ppermute(value, axis, [(source, source + steps) for source in range(initial, last)])


def features(values):
    return jnp.where(values > 0, values + 1.0, jnp.exp(jnp.minimum(values, 0.0)))


def slope(values):
    return jnp.where(values > 0, jnp.ones_like(values), jnp.exp(jnp.minimum(values, 0.0)))


def local_state(key_feat, val_round):
    rows = key_feat.shape[0]
    key_heads = key_feat.reshape(rows, H, DH)
    val_heads = val_round.reshape(rows, H, DH)
    outer = jnp.einsum(
        "thd,the->dhe", key_heads, val_heads, preferred_element_type=jnp.float32
    ).reshape(DH, H * DH)
    norm_row = jnp.sum(key_feat, axis=0, dtype=jnp.float32)
    return jnp.concatenate([outer, norm_row[None, :]], axis=0)


def complex_total(own, block_complex):
    position = lax.axis_index(("sec", "blk"))
    blocks = block_complex.shape[0]
    mine = jnp.take(block_complex, position)
    total = own
    for reach in range(1, MOSTB):
        lower = from_behind(own.astype(jnp.bfloat16), ("sec", "blk"), reach).astype(own.dtype)
        upper = from_behind(own.astype(jnp.bfloat16), ("sec", "blk"), -reach).astype(own.dtype)
        below = jnp.take(block_complex, jnp.maximum(position - reach, 0))
        above = jnp.take(block_complex, jnp.minimum(position + reach, blocks - 1))
        take_lower = jnp.logical_and(position - reach >= 0, below == mine)
        take_upper = jnp.logical_and(position + reach < blocks, above == mine)
        total = total + jnp.where(take_lower, lower, 0.0) + jnp.where(take_upper, upper, 0.0)
    return total


def pose_side(pose_rows, pair_rows, state, w_query, score_weight):
    count = pose_rows.shape[0]
    queries = jnp.dot(pose_rows, w_query, preferred_element_type=jnp.float32)
    query_heads = features(queries).reshape(count, H, DH)
    state_heads = state[:DH].reshape(DH, H, DH)
    norm_heads = state[DH].reshape(H, DH)
    numer = jnp.einsum("phd,dhe->phe", query_heads, state_heads, precision=highest)
    denom = jnp.sum(query_heads * norm_heads[None], axis=2)
    attended = numer / denom[:, :, None]
    weight_heads = score_weight.reshape(H, DH)
    scores = jnp.sum(attended * weight_heads[None], axis=(1, 2))
    slots = lax.broadcasted_iota(jnp.int32, (pair_rows.shape[0], count), 1)
    is_better = slots == pair_rows[:, 0:1]
    is_worse = slots == pair_rows[:, 1:2]
    better = jnp.sum(jnp.where(is_better, scores[None, :], 0.0), axis=1)
    worse = jnp.sum(jnp.where(is_worse, scores[None, :], 0.0), axis=1)
    delta = worse - better
    pair_loss = jax.nn.softplus(delta)
    push = jax.nn.sigmoid(delta)
    score_grad = jnp.sum(
        jnp.where(is_worse, push[:, None], 0.0) - jnp.where(is_better, push[:, None], 0.0),
        axis=0,
    )
    attended_grad = score_grad[:, None, None] * weight_heads[None]
    numer_grad = attended_grad / denom[:, :, None]
    denom_grad = -jnp.sum(attended_grad * attended, axis=2) / denom
    outer_grad = jnp.einsum("phd,phe->dhe", query_heads, numer_grad, precision=highest).reshape(
        DH, H * DH
    )
    norm_grad = jnp.sum(query_heads * denom_grad[:, :, None], axis=0).reshape(H * DH)
    pose_state = jnp.concatenate([outer_grad, norm_grad[None, :]], axis=0)
    feat_grad = (
        jnp.einsum("phe,dhe->phd", numer_grad, state_heads, precision=highest)
        + denom_grad[:, :, None] * norm_heads[None]
    )
    query_grad = (feat_grad.reshape(count, H * DH) * slope(queries)).astype(jnp.bfloat16)
    pose_grad = lax.dot_general(
        query_grad, w_query, (((1,), (1,)), ((), ())), preferred_element_type=jnp.float32
    )
    return (pair_loss, pose_grad.astype(jnp.bfloat16), pose_state)


def gather_rows(shard):
    count = lax.axis_size("blk")
    if count != 8:
        return lax.all_gather(shard, "blk", axis=0, tiled=True)
    position = lax.axis_index("blk")
    rows = shard.shape[0]
    odd = position % 2
    first = jnp.where(odd == 1, 4, 2)
    second = 6 - first
    along_first = [(s, s ^ (4 if s % 2 else 2)) for s in range(count)]
    along_second = [(s, s ^ (2 if s % 2 else 4)) for s in range(count)]
    near = lax.ppermute(shard, "blk", along_first)
    across = lax.ppermute(shard, "blk", along_second)
    corner = lax.ppermute(near, "blk", along_second)
    swap = [(s, s ^ 1) for s in range(count)]
    sibling = lax.ppermute(jnp.stack([shard, near, across]), "blk", swap)
    sibling_corner = lax.ppermute(corner, "blk", swap)
    twin = position ^ 1
    sources = [
        (
            [shard, near, across, corner],
            [position, position ^ first, position ^ second, position ^ 6],
        ),
        (
            [sibling[0], sibling[1], sibling[2], sibling_corner],
            [twin, twin ^ second, twin ^ first, twin ^ 6],
        ),
    ]
    full = jnp.zeros((count,) + shard.shape, shard.dtype)
    for pieces, where in sources:
        for k, at in enumerate(where):
            full = lax.dynamic_update_slice(full, pieces[k][None], (at, 0, 0))
    return full.reshape(count * rows, shard.shape[1])


def shards(receptor, poses, pairs, block_complex, w_key, w_value, w_query, score_weight):
    rows = receptor.shape[0]
    width = receptor.shape[1]
    contract = (((1,), (1,)), ((), ()))
    full_both = gather_rows(jnp.concatenate([w_key, w_value], axis=1))
    both = jnp.dot(receptor, full_both, preferred_element_type=jnp.float32)
    keys = both[:, :width]
    values = both[:, width:]
    key_feat = features(keys).astype(jnp.bfloat16)
    val_round = values.astype(jnp.bfloat16)
    state = complex_total(local_state(key_feat, val_round), block_complex)
    pair_loss, pose_grad, pose_state = pose_side(poses, pairs, state, w_query, score_weight)
    state_grad = complex_total(pose_state, block_complex).astype(jnp.bfloat16)
    key_heads = key_feat.reshape(rows, H, DH)
    val_heads = val_round.reshape(rows, H, DH)
    grad_heads = state_grad[:DH].reshape(DH, H, DH)
    norm_back = state_grad[DH].astype(jnp.float32).reshape(H, DH)
    feat_grad = (
        jnp.einsum("the,dhe->thd", val_heads, grad_heads, preferred_element_type=jnp.float32)
        + norm_back[None]
    )
    key_grad = (feat_grad.reshape(rows, width) * slope(keys)).astype(jnp.bfloat16)
    value_grad = (
        jnp.einsum("thd,dhe->the", key_heads, grad_heads, preferred_element_type=jnp.float32)
        .reshape(rows, width)
        .astype(jnp.bfloat16)
    )
    both_grad = jnp.concatenate([key_grad, value_grad], axis=1)
    total = lax.dot_general(both_grad, full_both, contract, preferred_element_type=jnp.float32)
    return (pair_loss, pose_grad, total.astype(jnp.bfloat16))


def solution(mesh):
    placed = (
        P(("sec", "blk"), None),
        P(("sec", "blk"), None),
        P(("sec", "blk"), None),
        P(),
        P("blk", None),
        P("blk", None),
        P(),
        P(),
    )
    return jax.shard_map(
        shards,
        mesh=mesh,
        in_specs=placed,
        out_specs=(P(("sec", "blk")), P(("sec", "blk"), None), P(("sec", "blk"), None)),
        check_vma=False,
    )
```

```python
import jax
import jax.numpy as jnp
from jax import lax
from jax.sharding import PartitionSpec as P
from jax.experimental import pallas as pl
from jax.experimental.pallas import tpu as pltpu

H = 16
DH = 64
MOSTB = 4


highest = lax.Precision.HIGHEST


def from_behind(value, axis, steps):
    count = lax.axis_size(axis)
    initial, last = (max(0, -steps), min(count, count - steps))
    return lax.ppermute(value, axis, [(source, source + steps) for source in range(initial, last)])


def features(values):
    return jnp.where(values > 0, values + 1.0, jnp.exp(jnp.minimum(values, 0.0)))


def slope(values):
    return jnp.where(values > 0, jnp.ones_like(values), jnp.exp(jnp.minimum(values, 0.0)))


def local_state(key_feat, val_round):
    rows = key_feat.shape[0]
    key_heads = key_feat.reshape(rows, H, DH)
    val_heads = val_round.reshape(rows, H, DH)
    outer = jnp.einsum(
        "thd,the->dhe", key_heads, val_heads, preferred_element_type=jnp.float32
    ).reshape(DH, H * DH)
    norm_row = jnp.sum(key_feat, axis=0, dtype=jnp.float32)
    return jnp.concatenate([outer, norm_row[None, :]], axis=0)


def complex_total(own, block_complex):
    position = lax.axis_index(("sec", "blk"))
    blocks = block_complex.shape[0]
    mine = jnp.take(block_complex, position)
    total = own
    for reach in range(1, MOSTB):
        lower = from_behind(own.astype(jnp.bfloat16), ("sec", "blk"), reach).astype(own.dtype)
        upper = from_behind(own.astype(jnp.bfloat16), ("sec", "blk"), -reach).astype(own.dtype)
        below = jnp.take(block_complex, jnp.maximum(position - reach, 0))
        above = jnp.take(block_complex, jnp.minimum(position + reach, blocks - 1))
        take_lower = jnp.logical_and(position - reach >= 0, below == mine)
        take_upper = jnp.logical_and(position + reach < blocks, above == mine)
        total = total + jnp.where(take_lower, lower, 0.0) + jnp.where(take_upper, upper, 0.0)
    return total


def pose_side(pose_rows, pair_rows, state, w_query, score_weight):
    count = pose_rows.shape[0]
    queries = jnp.dot(pose_rows, w_query, preferred_element_type=jnp.float32)
    query_heads = features(queries).reshape(count, H, DH)
    state_heads = state[:DH].reshape(DH, H, DH)
    norm_heads = state[DH].reshape(H, DH)
    numer = jnp.einsum("phd,dhe->phe", query_heads, state_heads, precision=highest)
    denom = jnp.sum(query_heads * norm_heads[None], axis=2)
    attended = numer / denom[:, :, None]
    weight_heads = score_weight.reshape(H, DH)
    scores = jnp.sum(attended * weight_heads[None], axis=(1, 2))
    slots = lax.broadcasted_iota(jnp.int32, (pair_rows.shape[0], count), 1)
    is_better = slots == pair_rows[:, 0:1]
    is_worse = slots == pair_rows[:, 1:2]
    better = jnp.sum(jnp.where(is_better, scores[None, :], 0.0), axis=1)
    worse = jnp.sum(jnp.where(is_worse, scores[None, :], 0.0), axis=1)
    delta = worse - better
    pair_loss = jax.nn.softplus(delta)
    push = jax.nn.sigmoid(delta)
    score_grad = jnp.sum(
        jnp.where(is_worse, push[:, None], 0.0) - jnp.where(is_better, push[:, None], 0.0),
        axis=0,
    )
    attended_grad = score_grad[:, None, None] * weight_heads[None]
    numer_grad = attended_grad / denom[:, :, None]
    denom_grad = -jnp.sum(attended_grad * attended, axis=2) / denom
    outer_grad = jnp.einsum("phd,phe->dhe", query_heads, numer_grad, precision=highest).reshape(
        DH, H * DH
    )
    norm_grad = jnp.sum(query_heads * denom_grad[:, :, None], axis=0).reshape(H * DH)
    pose_state = jnp.concatenate([outer_grad, norm_grad[None, :]], axis=0)
    feat_grad = (
        jnp.einsum("phe,dhe->phd", numer_grad, state_heads, precision=highest)
        + denom_grad[:, :, None] * norm_heads[None]
    )
    query_grad = (feat_grad.reshape(count, H * DH) * slope(queries)).astype(jnp.bfloat16)
    pose_grad = lax.dot_general(
        query_grad, w_query, (((1,), (1,)), ((), ())), preferred_element_type=jnp.float32
    )
    return (pair_loss, pose_grad.astype(jnp.bfloat16), pose_state)


def pose_kernel(pose_ref, pair_ref, state_ref, query_ref, weight_ref, loss_ref, grad_ref, back_ref, feat_ref):
    count, width = pose_ref.shape
    lanes = 2 * DH
    queries = jnp.dot(pose_ref[...], query_ref[...], preferred_element_type=jnp.float32)
    query_feat = features(queries)
    norm = state_ref[DH : DH + 1, :]
    weight = weight_ref[...]
    head_row = lax.broadcasted_iota(jnp.int32, (lanes, lanes), 0) // DH
    head_col = lax.broadcasted_iota(jnp.int32, (lanes, lanes), 1) // DH
    same = head_row == head_col
    ones = same.astype(jnp.float32)
    blocks, numers, denoms = [], [], []
    scores = jnp.zeros((count, 1), jnp.float32)
    for g in range(width // lanes):
        cols = slice(g * lanes, (g + 1) * lanes)
        part = state_ref[0:DH, cols]
        block = jnp.where(same, jnp.concatenate([part, part], axis=0), 0.0)
        feat = query_feat[:, cols]
        numer = jnp.dot(feat, block, precision=highest, preferred_element_type=jnp.float32)
        denom = jnp.dot(
            feat * norm[:, cols], ones, precision=highest, preferred_element_type=jnp.float32
        )
        attended = numer / denom
        scores = scores + jnp.sum(attended * weight[:, cols], axis=1, keepdims=True)
        blocks.append(block)
        numers.append(attended)
        denoms.append(denom)
    slots = lax.broadcasted_iota(jnp.int32, (count, pair_ref.shape[1]), 0)
    is_better = slots == pair_ref[0:1, :]
    is_worse = slots == pair_ref[1:2, :]
    better = jnp.sum(jnp.where(is_better, scores, 0.0), axis=0, keepdims=True)
    worse = jnp.sum(jnp.where(is_worse, scores, 0.0), axis=0, keepdims=True)
    delta = worse - better
    loss_ref[...] = jnp.maximum(delta, 0.0) + jnp.log1p(jnp.exp(-jnp.abs(delta)))
    push = 1.0 / (1.0 + jnp.exp(-delta))
    score_grad = jnp.sum(
        jnp.where(is_worse, push, 0.0) - jnp.where(is_better, push, 0.0), axis=1, keepdims=True
    )
    low = lax.broadcasted_iota(jnp.int32, (DH, lanes), 1) < DH
    for g in range(width // lanes):
        cols = slice(g * lanes, (g + 1) * lanes)
        feat = query_feat[:, cols]
        attended_grad = score_grad * weight[:, cols]
        numer_grad = attended_grad / denoms[g]
        denom_grad = -jnp.dot(
            attended_grad * numers[g], ones, precision=highest, preferred_element_type=jnp.float32
        ) / denoms[g]
        outer = jnp.dot(feat.T, numer_grad, precision=highest, preferred_element_type=jnp.float32)
        back_ref[0:DH, cols] = jnp.where(low, outer[:DH], outer[DH:])
        back_ref[DH : DH + 1, cols] = jnp.sum(feat * denom_grad, axis=0, keepdims=True)
        feat_grad = lax.dot_general(
            numer_grad,
            blocks[g],
            (((1,), (1,)), ((), ())),
            precision=highest,
            preferred_element_type=jnp.float32,
        ) + denom_grad * norm[:, cols]
        feat_ref[:, cols] = (feat_grad * slope(queries[:, cols])).astype(feat_ref.dtype)
    grad = lax.dot_general(
        feat_ref[...], query_ref[...], (((1,), (1,)), ((), ())), preferred_element_type=jnp.float32
    )
    grad_ref[...] = grad.astype(grad_ref.dtype)


def pose_fused(pose_rows, pair_rows, state, w_query, score_weight, interpret=False):
    count, width = pose_rows.shape
    pairs_t = pair_rows.T
    loss, grad, back = pl.pallas_call(
        pose_kernel,
        out_shape=(
            jax.ShapeDtypeStruct((1, pair_rows.shape[0]), jnp.float32),
            jax.ShapeDtypeStruct((count, width), jnp.bfloat16),
            jax.ShapeDtypeStruct(state.shape, jnp.float32),
        ),
        scratch_shapes=[pltpu.VMEM((count, width), jnp.bfloat16)],
        interpret=interpret,
    )(pose_rows, pairs_t, state, w_query, score_weight.reshape(1, width))
    return (loss.reshape(pair_rows.shape[0]), grad, back)


def gather_rows(shard):
    count = lax.axis_size("blk")
    if count != 8:
        return lax.all_gather(shard, "blk", axis=0, tiled=True)
    position = lax.axis_index("blk")
    rows = shard.shape[0]
    odd = position % 2
    first = jnp.where(odd == 1, 4, 2)
    second = 6 - first
    early = lax.ppermute(shard, "blk", [(s, s ^ (4 if s % 2 else 2)) for s in range(count)])
    late = lax.ppermute(
        jnp.stack([shard, early]), "blk", [(s, s ^ (2 if s % 2 else 4)) for s in range(count)]
    )
    mine = jnp.concatenate([jnp.stack([shard, early]), late], axis=0)
    sibling = lax.ppermute(mine, "blk", [(s, s ^ 1) for s in range(count)])
    twin = position ^ 1
    sources = [
        (mine, [position, position ^ first, position ^ second, position ^ 6]),
        (sibling, [twin, twin ^ second, twin ^ first, twin ^ 6]),
    ]
    full = jnp.zeros((count,) + shard.shape, shard.dtype)
    for pieces, where in sources:
        for k, at in enumerate(where):
            full = lax.dynamic_update_slice(full, pieces[k][None], (at, 0, 0))
    return full.reshape(count * rows, shard.shape[1])


def shards(receptor, poses, pairs, block_complex, w_key, w_value, w_query, score_weight):
    rows = receptor.shape[0]
    width = receptor.shape[1]
    contract = (((1,), (1,)), ((), ()))
    full_both = gather_rows(jnp.concatenate([w_key, w_value], axis=1))
    both = jnp.dot(receptor, full_both, preferred_element_type=jnp.float32)
    keys = both[:, :width]
    values = both[:, width:]
    key_feat = features(keys).astype(jnp.bfloat16)
    val_round = values.astype(jnp.bfloat16)
    state = complex_total(local_state(key_feat, val_round), block_complex)
    pair_loss, pose_grad, pose_state = pose_fused(poses, pairs, state, w_query, score_weight)
    state_grad = complex_total(pose_state, block_complex).astype(jnp.bfloat16)
    key_heads = key_feat.reshape(rows, H, DH)
    val_heads = val_round.reshape(rows, H, DH)
    grad_heads = state_grad[:DH].reshape(DH, H, DH)
    norm_back = state_grad[DH].astype(jnp.float32).reshape(H, DH)
    feat_grad = (
        jnp.einsum("the,dhe->thd", val_heads, grad_heads, preferred_element_type=jnp.float32)
        + norm_back[None]
    )
    key_grad = (feat_grad.reshape(rows, width) * slope(keys)).astype(jnp.bfloat16)
    value_grad = (
        jnp.einsum("thd,dhe->the", key_heads, grad_heads, preferred_element_type=jnp.float32)
        .reshape(rows, width)
        .astype(jnp.bfloat16)
    )
    both_grad = jnp.concatenate([key_grad, value_grad], axis=1)
    total = lax.dot_general(both_grad, full_both, contract, preferred_element_type=jnp.float32)
    return (pair_loss, pose_grad, total.astype(jnp.bfloat16))


def solution(mesh):
    placed = (
        P(("sec", "blk"), None),
        P(("sec", "blk"), None),
        P(("sec", "blk"), None),
        P(),
        P("blk", None),
        P("blk", None),
        P(),
        P(),
    )
    return jax.shard_map(
        shards,
        mesh=mesh,
        in_specs=placed,
        out_specs=(P(("sec", "blk")), P(("sec", "blk"), None), P(("sec", "blk"), None)),
        check_vma=False,
    )
```

```python
import jax
import jax.numpy as jnp
from jax import lax
from jax.sharding import PartitionSpec as P
from jax.experimental import pallas as pl
from jax.experimental.pallas import tpu as pltpu

H = 16
DH = 64
MOSTB = 4


highest = lax.Precision.HIGHEST


def from_behind(value, axis, steps):
    count = lax.axis_size(axis)
    initial, last = (max(0, -steps), min(count, count - steps))
    return lax.ppermute(value, axis, [(source, source + steps) for source in range(initial, last)])


def features(values):
    return jnp.where(values > 0, values + 1.0, jnp.exp(jnp.minimum(values, 0.0)))


def slope(values):
    return jnp.where(values > 0, jnp.ones_like(values), jnp.exp(jnp.minimum(values, 0.0)))


def local_state(key_feat, val_round):
    rows = key_feat.shape[0]
    key_heads = key_feat.reshape(rows, H, DH)
    val_heads = val_round.reshape(rows, H, DH)
    outer = jnp.einsum(
        "thd,the->dhe", key_heads, val_heads, preferred_element_type=jnp.float32
    ).reshape(DH, H * DH)
    norm_row = jnp.sum(key_feat, axis=0, dtype=jnp.float32)
    return jnp.concatenate([outer, norm_row[None, :]], axis=0)


def complex_total(own, block_complex):
    position = lax.axis_index(("sec", "blk"))
    blocks = block_complex.shape[0]
    mine = jnp.take(block_complex, position)
    total = own
    for reach in range(1, MOSTB):
        lower = from_behind(own.astype(jnp.bfloat16), ("sec", "blk"), reach).astype(own.dtype)
        upper = from_behind(own.astype(jnp.bfloat16), ("sec", "blk"), -reach).astype(own.dtype)
        below = jnp.take(block_complex, jnp.maximum(position - reach, 0))
        above = jnp.take(block_complex, jnp.minimum(position + reach, blocks - 1))
        take_lower = jnp.logical_and(position - reach >= 0, below == mine)
        take_upper = jnp.logical_and(position + reach < blocks, above == mine)
        total = total + jnp.where(take_lower, lower, 0.0) + jnp.where(take_upper, upper, 0.0)
    return total


def send(value, axis, pairs):
    return lax.ppermute(value, axis, pairs)


def complex_sum(own, block_complex):
    axis = ("sec", "blk")
    count = lax.axis_size(axis)
    position = lax.axis_index(axis)
    last = block_complex.shape[0] - 1

    def complex_of(block):
        return jnp.take(block_complex, jnp.clip(block, 0, last))

    def kept(value, block, target):
        inside = jnp.logical_and(target >= 0, target <= last)
        return jnp.where(jnp.logical_and(inside, complex_of(block) == complex_of(target)), value, 0.0)

    narrow = own.astype(jnp.bfloat16)
    twin = position ^ 1
    sibling = send(narrow, axis, [(s, s ^ 1) for s in range(count)]).astype(own.dtype)
    odd = position % 2 == 1
    far_target = jnp.where(odd, position + 3, position - 3)
    far = send(
        kept(own, position, far_target).astype(jnp.bfloat16),
        axis,
        [(s, s + 3) for s in range(1, count - 3, 2)] + [(s, s - 3) for s in range(4, count, 2)],
    )
    low = jnp.where(odd, sibling, own)
    high = jnp.where(odd, own, sibling)
    first = position - position % 2

    def chip_part(target):
        return (kept(low, first, target) + kept(high, first + 1, target)).astype(jnp.bfloat16)

    up = send(chip_part(position + 2), axis, [(s, s + 2) for s in range(count - 2)])
    down = send(chip_part(position - 2), axis, [(s, s - 2) for s in range(2, count)])
    total = own + kept(sibling, twin, position)
    return total + up.astype(own.dtype) + down.astype(own.dtype) + far.astype(own.dtype)


def pose_side(pose_rows, pair_rows, state, w_query, score_weight):
    count = pose_rows.shape[0]
    queries = jnp.dot(pose_rows, w_query, preferred_element_type=jnp.float32)
    query_heads = features(queries).reshape(count, H, DH)
    state_heads = state[:DH].reshape(DH, H, DH)
    norm_heads = state[DH].reshape(H, DH)
    numer = jnp.einsum("phd,dhe->phe", query_heads, state_heads, precision=highest)
    denom = jnp.sum(query_heads * norm_heads[None], axis=2)
    attended = numer / denom[:, :, None]
    weight_heads = score_weight.reshape(H, DH)
    scores = jnp.sum(attended * weight_heads[None], axis=(1, 2))
    slots = lax.broadcasted_iota(jnp.int32, (pair_rows.shape[0], count), 1)
    is_better = slots == pair_rows[:, 0:1]
    is_worse = slots == pair_rows[:, 1:2]
    better = jnp.sum(jnp.where(is_better, scores[None, :], 0.0), axis=1)
    worse = jnp.sum(jnp.where(is_worse, scores[None, :], 0.0), axis=1)
    delta = worse - better
    pair_loss = jax.nn.softplus(delta)
    push = jax.nn.sigmoid(delta)
    score_grad = jnp.sum(
        jnp.where(is_worse, push[:, None], 0.0) - jnp.where(is_better, push[:, None], 0.0),
        axis=0,
    )
    attended_grad = score_grad[:, None, None] * weight_heads[None]
    numer_grad = attended_grad / denom[:, :, None]
    denom_grad = -jnp.sum(attended_grad * attended, axis=2) / denom
    outer_grad = jnp.einsum("phd,phe->dhe", query_heads, numer_grad, precision=highest).reshape(
        DH, H * DH
    )
    norm_grad = jnp.sum(query_heads * denom_grad[:, :, None], axis=0).reshape(H * DH)
    pose_state = jnp.concatenate([outer_grad, norm_grad[None, :]], axis=0)
    feat_grad = (
        jnp.einsum("phe,dhe->phd", numer_grad, state_heads, precision=highest)
        + denom_grad[:, :, None] * norm_heads[None]
    )
    query_grad = (feat_grad.reshape(count, H * DH) * slope(queries)).astype(jnp.bfloat16)
    pose_grad = lax.dot_general(
        query_grad, w_query, (((1,), (1,)), ((), ())), preferred_element_type=jnp.float32
    )
    return (pair_loss, pose_grad.astype(jnp.bfloat16), pose_state)


def pose_kernel(pose_ref, pair_ref, state_ref, query_ref, weight_ref, loss_ref, grad_ref, back_ref, feat_ref):
    count, width = pose_ref.shape
    lanes = 2 * DH
    queries = jnp.dot(pose_ref[...], query_ref[...], preferred_element_type=jnp.float32)
    query_feat = features(queries)
    norm = state_ref[DH : DH + 1, :]
    weight = weight_ref[...]
    head_row = lax.broadcasted_iota(jnp.int32, (lanes, lanes), 0) // DH
    head_col = lax.broadcasted_iota(jnp.int32, (lanes, lanes), 1) // DH
    same = head_row == head_col
    ones = same.astype(jnp.float32)
    blocks, numers, denoms = [], [], []
    scores = jnp.zeros((count, 1), jnp.float32)
    for g in range(width // lanes):
        cols = slice(g * lanes, (g + 1) * lanes)
        part = state_ref[0:DH, cols]
        block = jnp.where(same, jnp.concatenate([part, part], axis=0), 0.0)
        feat = query_feat[:, cols]
        numer = jnp.dot(feat, block, precision=highest, preferred_element_type=jnp.float32)
        denom = jnp.dot(
            feat * norm[:, cols], ones, precision=highest, preferred_element_type=jnp.float32
        )
        attended = numer / denom
        scores = scores + jnp.sum(attended * weight[:, cols], axis=1, keepdims=True)
        blocks.append(block)
        numers.append(attended)
        denoms.append(denom)
    slots = lax.broadcasted_iota(jnp.int32, (count, pair_ref.shape[1]), 0)
    is_better = slots == pair_ref[0:1, :]
    is_worse = slots == pair_ref[1:2, :]
    better = jnp.sum(jnp.where(is_better, scores, 0.0), axis=0, keepdims=True)
    worse = jnp.sum(jnp.where(is_worse, scores, 0.0), axis=0, keepdims=True)
    delta = worse - better
    loss_ref[...] = jnp.maximum(delta, 0.0) + jnp.log1p(jnp.exp(-jnp.abs(delta)))
    push = 1.0 / (1.0 + jnp.exp(-delta))
    score_grad = jnp.sum(
        jnp.where(is_worse, push, 0.0) - jnp.where(is_better, push, 0.0), axis=1, keepdims=True
    )
    low = lax.broadcasted_iota(jnp.int32, (DH, lanes), 1) < DH
    for g in range(width // lanes):
        cols = slice(g * lanes, (g + 1) * lanes)
        feat = query_feat[:, cols]
        attended_grad = score_grad * weight[:, cols]
        numer_grad = attended_grad / denoms[g]
        denom_grad = -jnp.dot(
            attended_grad * numers[g], ones, precision=highest, preferred_element_type=jnp.float32
        ) / denoms[g]
        outer = jnp.dot(feat.T, numer_grad, precision=highest, preferred_element_type=jnp.float32)
        back_ref[0:DH, cols] = jnp.where(low, outer[:DH], outer[DH:])
        back_ref[DH : DH + 1, cols] = jnp.sum(feat * denom_grad, axis=0, keepdims=True)
        feat_grad = lax.dot_general(
            numer_grad,
            blocks[g],
            (((1,), (1,)), ((), ())),
            precision=highest,
            preferred_element_type=jnp.float32,
        ) + denom_grad * norm[:, cols]
        feat_ref[:, cols] = (feat_grad * slope(queries[:, cols])).astype(feat_ref.dtype)
    grad = lax.dot_general(
        feat_ref[...], query_ref[...], (((1,), (1,)), ((), ())), preferred_element_type=jnp.float32
    )
    grad_ref[...] = grad.astype(grad_ref.dtype)


def pose_fused(pose_rows, pair_rows, state, w_query, score_weight, interpret=False):
    count, width = pose_rows.shape
    pairs_t = pair_rows.T
    loss, grad, back = pl.pallas_call(
        pose_kernel,
        out_shape=(
            jax.ShapeDtypeStruct((1, pair_rows.shape[0]), jnp.float32),
            jax.ShapeDtypeStruct((count, width), jnp.bfloat16),
            jax.ShapeDtypeStruct(state.shape, jnp.float32),
        ),
        scratch_shapes=[pltpu.VMEM((count, width), jnp.bfloat16)],
        interpret=interpret,
    )(pose_rows, pairs_t, state, w_query, score_weight.reshape(1, width))
    return (loss.reshape(pair_rows.shape[0]), grad, back)


def gather_rows(shard):
    count = lax.axis_size("blk")
    if count != 8:
        return lax.all_gather(shard, "blk", axis=0, tiled=True)
    position = lax.axis_index("blk")
    rows = shard.shape[0]
    odd = position % 2
    first = jnp.where(odd == 1, 4, 2)
    second = 6 - first
    early = lax.ppermute(shard, "blk", [(s, s ^ (4 if s % 2 else 2)) for s in range(count)])
    late = lax.ppermute(
        jnp.stack([shard, early]), "blk", [(s, s ^ (2 if s % 2 else 4)) for s in range(count)]
    )
    mine = jnp.concatenate([jnp.stack([shard, early]), late], axis=0)
    sibling = lax.ppermute(mine, "blk", [(s, s ^ 1) for s in range(count)])
    twin = position ^ 1
    sources = [
        (mine, [position, position ^ first, position ^ second, position ^ 6]),
        (sibling, [twin, twin ^ second, twin ^ first, twin ^ 6]),
    ]
    full = jnp.zeros((count,) + shard.shape, shard.dtype)
    for pieces, where in sources:
        for k, at in enumerate(where):
            full = lax.dynamic_update_slice(full, pieces[k][None], (at, 0, 0))
    return full.reshape(count * rows, shard.shape[1])


def shards(receptor, poses, pairs, block_complex, w_key, w_value, w_query, score_weight):
    rows = receptor.shape[0]
    width = receptor.shape[1]
    contract = (((1,), (1,)), ((), ()))
    full_both = gather_rows(jnp.concatenate([w_key, w_value], axis=1))
    both = jnp.dot(receptor, full_both, preferred_element_type=jnp.float32)
    keys = both[:, :width]
    values = both[:, width:]
    key_feat = features(keys).astype(jnp.bfloat16)
    val_round = values.astype(jnp.bfloat16)
    state = complex_sum(local_state(key_feat, val_round), block_complex)
    pair_loss, pose_grad, pose_state = pose_fused(poses, pairs, state, w_query, score_weight)
    state_grad = complex_sum(pose_state, block_complex).astype(jnp.bfloat16)
    key_heads = key_feat.reshape(rows, H, DH)
    val_heads = val_round.reshape(rows, H, DH)
    grad_heads = state_grad[:DH].reshape(DH, H, DH)
    norm_back = state_grad[DH].astype(jnp.float32).reshape(H, DH)
    feat_grad = (
        jnp.einsum("the,dhe->thd", val_heads, grad_heads, preferred_element_type=jnp.float32)
        + norm_back[None]
    )
    key_grad = (feat_grad.reshape(rows, width) * slope(keys)).astype(jnp.bfloat16)
    value_grad = (
        jnp.einsum("thd,dhe->the", key_heads, grad_heads, preferred_element_type=jnp.float32)
        .reshape(rows, width)
        .astype(jnp.bfloat16)
    )
    both_grad = jnp.concatenate([key_grad, value_grad], axis=1)
    total = lax.dot_general(both_grad, full_both, contract, preferred_element_type=jnp.float32)
    return (pair_loss, pose_grad, total.astype(jnp.bfloat16))


def solution(mesh):
    placed = (
        P(("sec", "blk"), None),
        P(("sec", "blk"), None),
        P(("sec", "blk"), None),
        P(),
        P("blk", None),
        P("blk", None),
        P(),
        P(),
    )
    return jax.shard_map(
        shards,
        mesh=mesh,
        in_specs=placed,
        out_specs=(P(("sec", "blk")), P(("sec", "blk"), None), P(("sec", "blk"), None)),
        check_vma=False,
    )
```

```python
import jax
import jax.numpy as jnp
from jax import lax
from jax.sharding import PartitionSpec as P
from jax.experimental import pallas as pl
from jax.experimental.pallas import tpu as pltpu

H = 16
DH = 64
MOSTB = 4


highest = lax.Precision.HIGHEST


def from_behind(value, axis, steps):
    count = lax.axis_size(axis)
    initial, last = (max(0, -steps), min(count, count - steps))
    return lax.ppermute(value, axis, [(source, source + steps) for source in range(initial, last)])


def features(values):
    return jnp.where(values > 0, values + 1.0, jnp.exp(jnp.minimum(values, 0.0)))


def slope(values):
    return jnp.where(values > 0, jnp.ones_like(values), jnp.exp(jnp.minimum(values, 0.0)))


def local_state(key_feat, val_round):
    rows = key_feat.shape[0]
    key_heads = key_feat.reshape(rows, H, DH)
    val_heads = val_round.reshape(rows, H, DH)
    outer = jnp.einsum(
        "thd,the->dhe", key_heads, val_heads, preferred_element_type=jnp.float32
    ).reshape(DH, H * DH)
    norm_row = jnp.sum(key_feat, axis=0, dtype=jnp.float32)
    return jnp.concatenate([outer, norm_row[None, :]], axis=0)


def complex_total(own, block_complex):
    position = lax.axis_index(("sec", "blk"))
    blocks = block_complex.shape[0]
    mine = jnp.take(block_complex, position)
    total = own
    for reach in range(1, MOSTB):
        lower = from_behind(own.astype(jnp.bfloat16), ("sec", "blk"), reach).astype(own.dtype)
        upper = from_behind(own.astype(jnp.bfloat16), ("sec", "blk"), -reach).astype(own.dtype)
        below = jnp.take(block_complex, jnp.maximum(position - reach, 0))
        above = jnp.take(block_complex, jnp.minimum(position + reach, blocks - 1))
        take_lower = jnp.logical_and(position - reach >= 0, below == mine)
        take_upper = jnp.logical_and(position + reach < blocks, above == mine)
        total = total + jnp.where(take_lower, lower, 0.0) + jnp.where(take_upper, upper, 0.0)
    return total


def send(value, axis, pairs):
    return lax.ppermute(value, axis, pairs)


def complex_sum(own, block_complex):
    axis = ("sec", "blk")
    count = lax.axis_size(axis)
    position = lax.axis_index(axis)
    last = block_complex.shape[0] - 1

    def complex_of(block):
        return jnp.take(block_complex, jnp.clip(block, 0, last))

    def kept(value, block, target):
        inside = jnp.logical_and(target >= 0, target <= last)
        return jnp.where(jnp.logical_and(inside, complex_of(block) == complex_of(target)), value, 0.0)

    narrow = own.astype(jnp.bfloat16)
    twin = position ^ 1
    sibling = send(narrow, axis, [(s, s ^ 1) for s in range(count)]).astype(own.dtype)
    odd = position % 2 == 1
    far_target = jnp.where(odd, position + 3, position - 3)
    far = send(
        kept(own, position, far_target).astype(jnp.bfloat16),
        axis,
        [(s, s + 3) for s in range(1, count - 3, 2)] + [(s, s - 3) for s in range(4, count, 2)],
    )
    low = jnp.where(odd, sibling, own)
    high = jnp.where(odd, own, sibling)
    first = position - position % 2

    def chip_part(target):
        return (kept(low, first, target) + kept(high, first + 1, target)).astype(jnp.bfloat16)

    up = send(chip_part(position + 2), axis, [(s, s + 2) for s in range(count - 2)])
    down = send(chip_part(position - 2), axis, [(s, s - 2) for s in range(2, count)])
    total = own + kept(sibling, twin, position)
    return total + up.astype(own.dtype) + down.astype(own.dtype) + far.astype(own.dtype)


def pose_side(pose_rows, pair_rows, state, w_query, score_weight):
    count = pose_rows.shape[0]
    queries = jnp.dot(pose_rows, w_query, preferred_element_type=jnp.float32)
    query_heads = features(queries).reshape(count, H, DH)
    state_heads = state[:DH].reshape(DH, H, DH)
    norm_heads = state[DH].reshape(H, DH)
    numer = jnp.einsum("phd,dhe->phe", query_heads, state_heads, precision=highest)
    denom = jnp.sum(query_heads * norm_heads[None], axis=2)
    attended = numer / denom[:, :, None]
    weight_heads = score_weight.reshape(H, DH)
    scores = jnp.sum(attended * weight_heads[None], axis=(1, 2))
    slots = lax.broadcasted_iota(jnp.int32, (pair_rows.shape[0], count), 1)
    is_better = slots == pair_rows[:, 0:1]
    is_worse = slots == pair_rows[:, 1:2]
    better = jnp.sum(jnp.where(is_better, scores[None, :], 0.0), axis=1)
    worse = jnp.sum(jnp.where(is_worse, scores[None, :], 0.0), axis=1)
    delta = worse - better
    pair_loss = jax.nn.softplus(delta)
    push = jax.nn.sigmoid(delta)
    score_grad = jnp.sum(
        jnp.where(is_worse, push[:, None], 0.0) - jnp.where(is_better, push[:, None], 0.0),
        axis=0,
    )
    attended_grad = score_grad[:, None, None] * weight_heads[None]
    numer_grad = attended_grad / denom[:, :, None]
    denom_grad = -jnp.sum(attended_grad * attended, axis=2) / denom
    outer_grad = jnp.einsum("phd,phe->dhe", query_heads, numer_grad, precision=highest).reshape(
        DH, H * DH
    )
    norm_grad = jnp.sum(query_heads * denom_grad[:, :, None], axis=0).reshape(H * DH)
    pose_state = jnp.concatenate([outer_grad, norm_grad[None, :]], axis=0)
    feat_grad = (
        jnp.einsum("phe,dhe->phd", numer_grad, state_heads, precision=highest)
        + denom_grad[:, :, None] * norm_heads[None]
    )
    query_grad = (feat_grad.reshape(count, H * DH) * slope(queries)).astype(jnp.bfloat16)
    pose_grad = lax.dot_general(
        query_grad, w_query, (((1,), (1,)), ((), ())), preferred_element_type=jnp.float32
    )
    return (pair_loss, pose_grad.astype(jnp.bfloat16), pose_state)


def pose_kernel(pose_ref, pair_ref, state_ref, query_ref, weight_ref, loss_ref, grad_ref, back_ref, feat_ref):
    count, width = pose_ref.shape
    lanes = 2 * DH
    queries = jnp.dot(pose_ref[...], query_ref[...], preferred_element_type=jnp.float32)
    query_feat = features(queries)
    norm = state_ref[DH : DH + 1, :]
    weight = weight_ref[...]
    head_row = lax.broadcasted_iota(jnp.int32, (lanes, lanes), 0) // DH
    head_col = lax.broadcasted_iota(jnp.int32, (lanes, lanes), 1) // DH
    same = head_row == head_col
    ones = same.astype(jnp.float32)
    blocks, numers, denoms = [], [], []
    scores = jnp.zeros((count, 1), jnp.float32)
    for g in range(width // lanes):
        cols = slice(g * lanes, (g + 1) * lanes)
        part = state_ref[0:DH, cols]
        block = jnp.where(same, jnp.concatenate([part, part], axis=0), 0.0)
        feat = query_feat[:, cols]
        numer = jnp.dot(feat, block, precision=highest, preferred_element_type=jnp.float32)
        denom = jnp.dot(
            feat * norm[:, cols], ones, precision=highest, preferred_element_type=jnp.float32
        )
        attended = numer / denom
        scores = scores + jnp.sum(attended * weight[:, cols], axis=1, keepdims=True)
        blocks.append(block)
        numers.append(attended)
        denoms.append(denom)
    slots = lax.broadcasted_iota(jnp.int32, (count, pair_ref.shape[1]), 0)
    is_better = slots == pair_ref[0:1, :]
    is_worse = slots == pair_ref[1:2, :]
    better = jnp.sum(jnp.where(is_better, scores, 0.0), axis=0, keepdims=True)
    worse = jnp.sum(jnp.where(is_worse, scores, 0.0), axis=0, keepdims=True)
    delta = worse - better
    loss_ref[...] = jnp.maximum(delta, 0.0) + jnp.log1p(jnp.exp(-jnp.abs(delta)))
    push = 1.0 / (1.0 + jnp.exp(-delta))
    score_grad = jnp.sum(
        jnp.where(is_worse, push, 0.0) - jnp.where(is_better, push, 0.0), axis=1, keepdims=True
    )
    low = lax.broadcasted_iota(jnp.int32, (DH, lanes), 1) < DH
    for g in range(width // lanes):
        cols = slice(g * lanes, (g + 1) * lanes)
        feat = query_feat[:, cols]
        attended_grad = score_grad * weight[:, cols]
        numer_grad = attended_grad / denoms[g]
        denom_grad = -jnp.dot(
            attended_grad * numers[g], ones, precision=highest, preferred_element_type=jnp.float32
        ) / denoms[g]
        outer = jnp.dot(feat.T, numer_grad, precision=highest, preferred_element_type=jnp.float32)
        back_ref[0:DH, cols] = jnp.where(low, outer[:DH], outer[DH:])
        back_ref[DH : DH + 1, cols] = jnp.sum(feat * denom_grad, axis=0, keepdims=True)
        feat_grad = lax.dot_general(
            numer_grad,
            blocks[g],
            (((1,), (1,)), ((), ())),
            precision=highest,
            preferred_element_type=jnp.float32,
        ) + denom_grad * norm[:, cols]
        feat_ref[:, cols] = (feat_grad * slope(queries[:, cols])).astype(feat_ref.dtype)
    grad = lax.dot_general(
        feat_ref[...], query_ref[...], (((1,), (1,)), ((), ())), preferred_element_type=jnp.float32
    )
    grad_ref[...] = grad.astype(grad_ref.dtype)


def pose_fused(pose_rows, pair_rows, state, w_query, score_weight, interpret=False):
    count, width = pose_rows.shape
    pairs_t = pair_rows.T
    loss, grad, back = pl.pallas_call(
        pose_kernel,
        out_shape=(
            jax.ShapeDtypeStruct((1, pair_rows.shape[0]), jnp.float32),
            jax.ShapeDtypeStruct((count, width), jnp.bfloat16),
            jax.ShapeDtypeStruct(state.shape, jnp.float32),
        ),
        scratch_shapes=[pltpu.VMEM((count, width), jnp.bfloat16)],
        interpret=interpret,
    )(pose_rows, pairs_t, state, w_query, score_weight.reshape(1, width))
    return (loss.reshape(pair_rows.shape[0]), grad, back)


def project_kernel(
    order_ref, rec_ref, own_ref, early_ref, late_ref, twin_ref, feat_ref, val_ref, keys_ref, state_ref
):
    width = feat_ref.shape[1]
    lanes = 2 * DH
    pieces = [own_ref[...], early_ref[...], late_ref[0], late_ref[1]] + [
        twin_ref[k] for k in range(twin_ref.shape[0])
    ]
    both = jnp.dot(rec_ref[order_ref[0]], pieces[0], preferred_element_type=jnp.float32)
    for m in range(1, len(pieces)):
        both = both + jnp.dot(rec_ref[order_ref[m]], pieces[m], preferred_element_type=jnp.float32)
    keys = both[:, :width]
    keys_ref[...] = keys
    key_feat = features(keys).astype(jnp.bfloat16)
    val_round = both[:, width:].astype(jnp.bfloat16)
    feat_ref[...] = key_feat
    val_ref[...] = val_round
    wide_feat = key_feat.astype(jnp.float32)
    wide_val = val_round.astype(jnp.float32)
    low = lax.broadcasted_iota(jnp.int32, (DH, lanes), 1) < DH
    for g in range(width // lanes):
        cols = slice(g * lanes, (g + 1) * lanes)
        outer = jnp.dot(
            wide_feat[:, cols].T, wide_val[:, cols], precision=highest,
            preferred_element_type=jnp.float32,
        )
        state_ref[0:DH, cols] = jnp.where(low, outer[:DH], outer[DH:])
    state_ref[DH : DH + 1, :] = jnp.sum(wide_feat, axis=0, keepdims=True)


def project_fused(receptor, parts, interpret=False):
    own, early, late, twin, order = parts
    rows, width = receptor.shape
    count = order.shape[0]
    split = receptor.reshape(rows, count, width // count).transpose(1, 0, 2)
    whole = lambda shape: pl.BlockSpec(shape, lambda i, order: (0,) * len(shape))
    return pl.pallas_call(
        project_kernel,
        grid_spec=pltpu.PrefetchScalarGridSpec(
            num_scalar_prefetch=1,
            grid=(1,),
            in_specs=[whole(split.shape), whole(own.shape), whole(early.shape),
                      whole(late.shape), whole(twin.shape)],
            out_specs=[whole((rows, width)), whole((rows, width)), whole((rows, width)),
                       whole((DH + 1, width))],
        ),
        out_shape=(
            jax.ShapeDtypeStruct((rows, width), jnp.bfloat16),
            jax.ShapeDtypeStruct((rows, width), jnp.bfloat16),
            jax.ShapeDtypeStruct((rows, width), jnp.float32),
            jax.ShapeDtypeStruct((DH + 1, width), jnp.float32),
        ),
        interpret=interpret,
    )(order, split, own, early, late, twin)


def gather_rows(shard):
    count = lax.axis_size("blk")
    if count != 8:
        return lax.all_gather(shard, "blk", axis=0, tiled=True), None
    position = lax.axis_index("blk")
    rows = shard.shape[0]
    odd = position % 2
    first = jnp.where(odd == 1, 4, 2)
    second = 6 - first
    early = lax.ppermute(shard, "blk", [(s, s ^ (4 if s % 2 else 2)) for s in range(count)])
    late = lax.ppermute(
        jnp.stack([shard, early]), "blk", [(s, s ^ (2 if s % 2 else 4)) for s in range(count)]
    )
    mine = jnp.concatenate([jnp.stack([shard, early]), late], axis=0)
    sibling = lax.ppermute(mine, "blk", [(s, s ^ 1) for s in range(count)])
    twin = position ^ 1
    sources = [
        (mine, [position, position ^ first, position ^ second, position ^ 6]),
        (sibling, [twin, twin ^ second, twin ^ first, twin ^ 6]),
    ]
    full = jnp.zeros((count,) + shard.shape, shard.dtype)
    for pieces, where in sources:
        for k, at in enumerate(where):
            full = lax.dynamic_update_slice(full, pieces[k][None], (at, 0, 0))
    order = jnp.stack(sources[0][1] + sources[1][1]).astype(jnp.int32)
    return full.reshape(count * rows, shard.shape[1]), (shard, early, late, sibling, order)


def shards(receptor, poses, pairs, block_complex, w_key, w_value, w_query, score_weight):
    rows = receptor.shape[0]
    width = receptor.shape[1]
    contract = (((1,), (1,)), ((), ()))
    full_both, parts = gather_rows(jnp.concatenate([w_key, w_value], axis=1))
    if parts is None:
        both = jnp.dot(receptor, full_both, preferred_element_type=jnp.float32)
        keys = both[:, :width]
        key_feat = features(keys).astype(jnp.bfloat16)
        val_round = both[:, width:].astype(jnp.bfloat16)
        own_state = local_state(key_feat, val_round)
    else:
        key_feat, val_round, keys, own_state = project_fused(receptor, parts)
    state = complex_sum(own_state, block_complex)
    pair_loss, pose_grad, pose_state = pose_fused(poses, pairs, state, w_query, score_weight)
    state_grad = complex_sum(pose_state, block_complex).astype(jnp.bfloat16)
    key_heads = key_feat.reshape(rows, H, DH)
    val_heads = val_round.reshape(rows, H, DH)
    grad_heads = state_grad[:DH].reshape(DH, H, DH)
    norm_back = state_grad[DH].astype(jnp.float32).reshape(H, DH)
    feat_grad = (
        jnp.einsum("the,dhe->thd", val_heads, grad_heads, preferred_element_type=jnp.float32)
        + norm_back[None]
    )
    key_grad = (feat_grad.reshape(rows, width) * slope(keys)).astype(jnp.bfloat16)
    value_grad = (
        jnp.einsum("thd,dhe->the", key_heads, grad_heads, preferred_element_type=jnp.float32)
        .reshape(rows, width)
        .astype(jnp.bfloat16)
    )
    both_grad = jnp.concatenate([key_grad, value_grad], axis=1)
    total = lax.dot_general(both_grad, full_both, contract, preferred_element_type=jnp.float32)
    return (pair_loss, pose_grad, total.astype(jnp.bfloat16))


def solution(mesh):
    placed = (
        P(("sec", "blk"), None),
        P(("sec", "blk"), None),
        P(("sec", "blk"), None),
        P(),
        P("blk", None),
        P("blk", None),
        P(),
        P(),
    )
    return jax.shard_map(
        shards,
        mesh=mesh,
        in_specs=placed,
        out_specs=(P(("sec", "blk")), P(("sec", "blk"), None), P(("sec", "blk"), None)),
        check_vma=False,
    )
```

```python
import jax
import jax.numpy as jnp
from jax import lax
from jax.sharding import PartitionSpec as P
from jax.experimental import pallas as pl
from jax.experimental.pallas import tpu as pltpu

H = 16
DH = 64
MOSTB = 4


highest = lax.Precision.HIGHEST


def from_behind(value, axis, steps):
    count = lax.axis_size(axis)
    initial, last = (max(0, -steps), min(count, count - steps))
    return lax.ppermute(value, axis, [(source, source + steps) for source in range(initial, last)])


def features(values):
    return jnp.where(values > 0, values + 1.0, jnp.exp(jnp.minimum(values, 0.0)))


def slope(values):
    return jnp.where(values > 0, jnp.ones_like(values), jnp.exp(jnp.minimum(values, 0.0)))


def local_state(key_feat, val_round):
    rows = key_feat.shape[0]
    key_heads = key_feat.reshape(rows, H, DH)
    val_heads = val_round.reshape(rows, H, DH)
    outer = jnp.einsum(
        "thd,the->dhe", key_heads, val_heads, preferred_element_type=jnp.float32
    ).reshape(DH, H * DH)
    norm_row = jnp.sum(key_feat, axis=0, dtype=jnp.float32)
    return jnp.concatenate([outer, norm_row[None, :]], axis=0)


def complex_total(own, block_complex):
    position = lax.axis_index(("sec", "blk"))
    blocks = block_complex.shape[0]
    mine = jnp.take(block_complex, position)
    total = own
    for reach in range(1, MOSTB):
        lower = from_behind(own.astype(jnp.bfloat16), ("sec", "blk"), reach).astype(own.dtype)
        upper = from_behind(own.astype(jnp.bfloat16), ("sec", "blk"), -reach).astype(own.dtype)
        below = jnp.take(block_complex, jnp.maximum(position - reach, 0))
        above = jnp.take(block_complex, jnp.minimum(position + reach, blocks - 1))
        take_lower = jnp.logical_and(position - reach >= 0, below == mine)
        take_upper = jnp.logical_and(position + reach < blocks, above == mine)
        total = total + jnp.where(take_lower, lower, 0.0) + jnp.where(take_upper, upper, 0.0)
    return total


def send(value, axis, pairs):
    return lax.ppermute(value, axis, pairs)


def complex_sum(own, block_complex):
    axis = ("sec", "blk")
    count = lax.axis_size(axis)
    position = lax.axis_index(axis)
    last = block_complex.shape[0] - 1

    def complex_of(block):
        return jnp.take(block_complex, jnp.clip(block, 0, last))

    def kept(value, block, target):
        inside = jnp.logical_and(target >= 0, target <= last)
        return jnp.where(jnp.logical_and(inside, complex_of(block) == complex_of(target)), value, 0.0)

    narrow = own.astype(jnp.bfloat16)
    twin = position ^ 1
    sibling = send(narrow, axis, [(s, s ^ 1) for s in range(count)]).astype(own.dtype)
    odd = position % 2 == 1
    far_target = jnp.where(odd, position + 3, position - 3)
    far = send(
        kept(own, position, far_target).astype(jnp.bfloat16),
        axis,
        [(s, s + 3) for s in range(1, count - 3, 2)] + [(s, s - 3) for s in range(4, count, 2)],
    )
    low = jnp.where(odd, sibling, own)
    high = jnp.where(odd, own, sibling)
    first = position - position % 2

    def chip_part(target):
        return (kept(low, first, target) + kept(high, first + 1, target)).astype(jnp.bfloat16)

    up = send(chip_part(position + 2), axis, [(s, s + 2) for s in range(count - 2)])
    down = send(chip_part(position - 2), axis, [(s, s - 2) for s in range(2, count)])
    total = own + kept(sibling, twin, position)
    return total + up.astype(own.dtype) + down.astype(own.dtype) + far.astype(own.dtype)


def pose_side(pose_rows, pair_rows, state, w_query, score_weight):
    count = pose_rows.shape[0]
    queries = jnp.dot(pose_rows, w_query, preferred_element_type=jnp.float32)
    query_heads = features(queries).reshape(count, H, DH)
    state_heads = state[:DH].reshape(DH, H, DH)
    norm_heads = state[DH].reshape(H, DH)
    numer = jnp.einsum("phd,dhe->phe", query_heads, state_heads, precision=highest)
    denom = jnp.sum(query_heads * norm_heads[None], axis=2)
    attended = numer / denom[:, :, None]
    weight_heads = score_weight.reshape(H, DH)
    scores = jnp.sum(attended * weight_heads[None], axis=(1, 2))
    slots = lax.broadcasted_iota(jnp.int32, (pair_rows.shape[0], count), 1)
    is_better = slots == pair_rows[:, 0:1]
    is_worse = slots == pair_rows[:, 1:2]
    better = jnp.sum(jnp.where(is_better, scores[None, :], 0.0), axis=1)
    worse = jnp.sum(jnp.where(is_worse, scores[None, :], 0.0), axis=1)
    delta = worse - better
    pair_loss = jax.nn.softplus(delta)
    push = jax.nn.sigmoid(delta)
    score_grad = jnp.sum(
        jnp.where(is_worse, push[:, None], 0.0) - jnp.where(is_better, push[:, None], 0.0),
        axis=0,
    )
    attended_grad = score_grad[:, None, None] * weight_heads[None]
    numer_grad = attended_grad / denom[:, :, None]
    denom_grad = -jnp.sum(attended_grad * attended, axis=2) / denom
    outer_grad = jnp.einsum("phd,phe->dhe", query_heads, numer_grad, precision=highest).reshape(
        DH, H * DH
    )
    norm_grad = jnp.sum(query_heads * denom_grad[:, :, None], axis=0).reshape(H * DH)
    pose_state = jnp.concatenate([outer_grad, norm_grad[None, :]], axis=0)
    feat_grad = (
        jnp.einsum("phe,dhe->phd", numer_grad, state_heads, precision=highest)
        + denom_grad[:, :, None] * norm_heads[None]
    )
    query_grad = (feat_grad.reshape(count, H * DH) * slope(queries)).astype(jnp.bfloat16)
    pose_grad = lax.dot_general(
        query_grad, w_query, (((1,), (1,)), ((), ())), preferred_element_type=jnp.float32
    )
    return (pair_loss, pose_grad.astype(jnp.bfloat16), pose_state)


def pose_kernel(pose_ref, pair_ref, state_ref, query_ref, weight_ref, loss_ref, grad_ref, back_ref, feat_ref):
    count, width = pose_ref.shape
    lanes = 2 * DH
    queries = jnp.dot(pose_ref[...], query_ref[...], preferred_element_type=jnp.float32)
    query_feat = features(queries)
    norm = state_ref[DH : DH + 1, :]
    weight = weight_ref[...]
    head_row = lax.broadcasted_iota(jnp.int32, (lanes, lanes), 0) // DH
    head_col = lax.broadcasted_iota(jnp.int32, (lanes, lanes), 1) // DH
    same = head_row == head_col
    ones = same.astype(jnp.float32)
    blocks, numers, denoms = [], [], []
    scores = jnp.zeros((count, 1), jnp.float32)
    for g in range(width // lanes):
        cols = slice(g * lanes, (g + 1) * lanes)
        part = state_ref[0:DH, cols]
        block = jnp.where(same, jnp.concatenate([part, part], axis=0), 0.0)
        feat = query_feat[:, cols]
        numer = jnp.dot(feat, block, precision=highest, preferred_element_type=jnp.float32)
        denom = jnp.dot(
            feat * norm[:, cols], ones, precision=highest, preferred_element_type=jnp.float32
        )
        attended = numer / denom
        scores = scores + jnp.sum(attended * weight[:, cols], axis=1, keepdims=True)
        blocks.append(block)
        numers.append(attended)
        denoms.append(denom)
    slots = lax.broadcasted_iota(jnp.int32, (count, pair_ref.shape[1]), 0)
    is_better = slots == pair_ref[0:1, :]
    is_worse = slots == pair_ref[1:2, :]
    better = jnp.sum(jnp.where(is_better, scores, 0.0), axis=0, keepdims=True)
    worse = jnp.sum(jnp.where(is_worse, scores, 0.0), axis=0, keepdims=True)
    delta = worse - better
    loss_ref[...] = jnp.maximum(delta, 0.0) + jnp.log1p(jnp.exp(-jnp.abs(delta)))
    push = 1.0 / (1.0 + jnp.exp(-delta))
    score_grad = jnp.sum(
        jnp.where(is_worse, push, 0.0) - jnp.where(is_better, push, 0.0), axis=1, keepdims=True
    )
    low = lax.broadcasted_iota(jnp.int32, (DH, lanes), 1) < DH
    for g in range(width // lanes):
        cols = slice(g * lanes, (g + 1) * lanes)
        feat = query_feat[:, cols]
        attended_grad = score_grad * weight[:, cols]
        numer_grad = attended_grad / denoms[g]
        denom_grad = -jnp.dot(
            attended_grad * numers[g], ones, precision=highest, preferred_element_type=jnp.float32
        ) / denoms[g]
        outer = jnp.dot(feat.T, numer_grad, precision=highest, preferred_element_type=jnp.float32)
        back_ref[0:DH, cols] = jnp.where(low, outer[:DH], outer[DH:])
        back_ref[DH : DH + 1, cols] = jnp.sum(feat * denom_grad, axis=0, keepdims=True)
        feat_grad = lax.dot_general(
            numer_grad,
            blocks[g],
            (((1,), (1,)), ((), ())),
            precision=highest,
            preferred_element_type=jnp.float32,
        ) + denom_grad * norm[:, cols]
        feat_ref[:, cols] = (feat_grad * slope(queries[:, cols])).astype(feat_ref.dtype)
    grad = lax.dot_general(
        feat_ref[...], query_ref[...], (((1,), (1,)), ((), ())), preferred_element_type=jnp.float32
    )
    grad_ref[...] = grad.astype(grad_ref.dtype)


def pose_fused(pose_rows, pair_rows, state, w_query, score_weight, interpret=False):
    count, width = pose_rows.shape
    pairs_t = pair_rows.T
    loss, grad, back = pl.pallas_call(
        pose_kernel,
        out_shape=(
            jax.ShapeDtypeStruct((1, pair_rows.shape[0]), jnp.float32),
            jax.ShapeDtypeStruct((count, width), jnp.bfloat16),
            jax.ShapeDtypeStruct(state.shape, jnp.float32),
        ),
        scratch_shapes=[pltpu.VMEM((count, width), jnp.bfloat16)],
        interpret=interpret,
    )(pose_rows, pairs_t, state, w_query, score_weight.reshape(1, width))
    return (loss.reshape(pair_rows.shape[0]), grad, back)


def back_kernel(feat_ref, val_ref, keys_ref, grad_ref, full_ref, out_ref, both_ref):
    width = feat_ref.shape[1]
    lanes = 2 * DH
    head_row = lax.broadcasted_iota(jnp.int32, (lanes, lanes), 0) // DH
    head_col = lax.broadcasted_iota(jnp.int32, (lanes, lanes), 1) // DH
    same = head_row == head_col
    for g in range(width // lanes):
        cols = slice(g * lanes, (g + 1) * lanes)
        part = grad_ref[0:DH, cols].astype(jnp.float32)
        block = jnp.where(same, jnp.concatenate([part, part], axis=0), 0.0).astype(jnp.bfloat16)
        feat_grad = lax.dot_general(
            val_ref[:, cols], block, (((1,), (1,)), ((), ())), preferred_element_type=jnp.float32
        ) + grad_ref[DH : DH + 1, cols].astype(jnp.float32)
        both_ref[:, cols] = (feat_grad * slope(keys_ref[:, cols])).astype(both_ref.dtype)
        value_grad = jnp.dot(feat_ref[:, cols], block, preferred_element_type=jnp.float32)
        both_ref[:, width + g * lanes : width + (g + 1) * lanes] = value_grad.astype(both_ref.dtype)
    total = lax.dot_general(
        both_ref[...], full_ref[...], (((1,), (1,)), ((), ())), preferred_element_type=jnp.float32
    )
    out_ref[...] = total.astype(out_ref.dtype)


def back_fused(key_feat, val_round, keys, state_grad, full_both, interpret=False):
    rows, width = key_feat.shape
    return pl.pallas_call(
        back_kernel,
        out_shape=jax.ShapeDtypeStruct((rows, width), jnp.bfloat16),
        scratch_shapes=[pltpu.VMEM((rows, 2 * width), jnp.bfloat16)],
        interpret=interpret,
    )(key_feat, val_round, keys, state_grad, full_both)


def gather_rows(shard):
    count = lax.axis_size("blk")
    if count != 8:
        return lax.all_gather(shard, "blk", axis=0, tiled=True)
    position = lax.axis_index("blk")
    rows = shard.shape[0]
    odd = position % 2
    first = jnp.where(odd == 1, 4, 2)
    second = 6 - first
    early = lax.ppermute(shard, "blk", [(s, s ^ (4 if s % 2 else 2)) for s in range(count)])
    late = lax.ppermute(
        jnp.stack([shard, early]), "blk", [(s, s ^ (2 if s % 2 else 4)) for s in range(count)]
    )
    mine = jnp.concatenate([jnp.stack([shard, early]), late], axis=0)
    sibling = lax.ppermute(mine, "blk", [(s, s ^ 1) for s in range(count)])
    twin = position ^ 1
    sources = [
        (mine, [position, position ^ first, position ^ second, position ^ 6]),
        (sibling, [twin, twin ^ second, twin ^ first, twin ^ 6]),
    ]
    full = jnp.zeros((count,) + shard.shape, shard.dtype)
    for pieces, where in sources:
        for k, at in enumerate(where):
            full = lax.dynamic_update_slice(full, pieces[k][None], (at, 0, 0))
    return full.reshape(count * rows, shard.shape[1])


def shards(receptor, poses, pairs, block_complex, w_key, w_value, w_query, score_weight):
    rows = receptor.shape[0]
    width = receptor.shape[1]
    contract = (((1,), (1,)), ((), ()))
    full_both = gather_rows(jnp.concatenate([w_key, w_value], axis=1))
    both = jnp.dot(receptor, full_both, preferred_element_type=jnp.float32)
    keys = both[:, :width]
    values = both[:, width:]
    key_feat = features(keys).astype(jnp.bfloat16)
    val_round = values.astype(jnp.bfloat16)
    state = complex_sum(local_state(key_feat, val_round), block_complex)
    pair_loss, pose_grad, pose_state = pose_fused(poses, pairs, state, w_query, score_weight)
    state_grad = complex_sum(pose_state, block_complex).astype(jnp.bfloat16)
    total = back_fused(key_feat, val_round, keys, state_grad, full_both)
    return (pair_loss, pose_grad, total)


def solution(mesh):
    placed = (
        P(("sec", "blk"), None),
        P(("sec", "blk"), None),
        P(("sec", "blk"), None),
        P(),
        P("blk", None),
        P("blk", None),
        P(),
        P(),
    )
    return jax.shard_map(
        shards,
        mesh=mesh,
        in_specs=placed,
        out_specs=(P(("sec", "blk")), P(("sec", "blk"), None), P(("sec", "blk"), None)),
        check_vma=False,
    )
```

```python
import jax
import jax.numpy as jnp
from jax import lax
from jax.sharding import PartitionSpec as P
from jax.experimental import pallas as pl
from jax.experimental.pallas import tpu as pltpu

H = 16
DH = 64
MOSTB = 4


highest = lax.Precision.HIGHEST


def from_behind(value, axis, steps):
    count = lax.axis_size(axis)
    initial, last = (max(0, -steps), min(count, count - steps))
    return lax.ppermute(value, axis, [(source, source + steps) for source in range(initial, last)])


def features(values):
    return jnp.where(values > 0, values + 1.0, jnp.exp(jnp.minimum(values, 0.0)))


def slope(values):
    return jnp.where(values > 0, jnp.ones_like(values), jnp.exp(jnp.minimum(values, 0.0)))


def local_state(key_feat, val_round):
    rows = key_feat.shape[0]
    key_heads = key_feat.reshape(rows, H, DH)
    val_heads = val_round.reshape(rows, H, DH)
    outer = jnp.einsum(
        "thd,the->dhe", key_heads, val_heads, preferred_element_type=jnp.float32
    ).reshape(DH, H * DH)
    norm_row = jnp.sum(key_feat, axis=0, dtype=jnp.float32)
    return jnp.concatenate([outer, norm_row[None, :]], axis=0)


def complex_total(own, block_complex):
    position = lax.axis_index(("sec", "blk"))
    blocks = block_complex.shape[0]
    mine = jnp.take(block_complex, position)
    total = own
    for reach in range(1, MOSTB):
        lower = from_behind(own.astype(jnp.bfloat16), ("sec", "blk"), reach).astype(own.dtype)
        upper = from_behind(own.astype(jnp.bfloat16), ("sec", "blk"), -reach).astype(own.dtype)
        below = jnp.take(block_complex, jnp.maximum(position - reach, 0))
        above = jnp.take(block_complex, jnp.minimum(position + reach, blocks - 1))
        take_lower = jnp.logical_and(position - reach >= 0, below == mine)
        take_upper = jnp.logical_and(position + reach < blocks, above == mine)
        total = total + jnp.where(take_lower, lower, 0.0) + jnp.where(take_upper, upper, 0.0)
    return total


def send(value, axis, pairs):
    return lax.ppermute(value, axis, pairs)


def complex_sum(own, block_complex):
    axis = ("sec", "blk")
    count = lax.axis_size(axis)
    position = lax.axis_index(axis)
    last = block_complex.shape[0] - 1

    def complex_of(block):
        return jnp.take(block_complex, jnp.clip(block, 0, last))

    def kept(value, block, target):
        inside = jnp.logical_and(target >= 0, target <= last)
        return jnp.where(jnp.logical_and(inside, complex_of(block) == complex_of(target)), value, 0.0)

    narrow = own.astype(jnp.bfloat16)
    twin = position ^ 1
    sibling = send(narrow, axis, [(s, s ^ 1) for s in range(count)]).astype(own.dtype)
    odd = position % 2 == 1
    far_target = jnp.where(odd, position + 3, position - 3)
    far = send(
        kept(own, position, far_target).astype(jnp.bfloat16),
        axis,
        [(s, s + 3) for s in range(1, count - 3, 2)] + [(s, s - 3) for s in range(4, count, 2)],
    )
    low = jnp.where(odd, sibling, own)
    high = jnp.where(odd, own, sibling)
    first = position - position % 2

    def chip_part(target):
        return (kept(low, first, target) + kept(high, first + 1, target)).astype(jnp.bfloat16)

    up = send(chip_part(position + 2), axis, [(s, s + 2) for s in range(count - 2)])
    down = send(chip_part(position - 2), axis, [(s, s - 2) for s in range(2, count)])
    total = own + kept(sibling, twin, position)
    return total + up.astype(own.dtype) + down.astype(own.dtype) + far.astype(own.dtype)


def pose_side(pose_rows, pair_rows, state, w_query, score_weight):
    count = pose_rows.shape[0]
    queries = jnp.dot(pose_rows, w_query, preferred_element_type=jnp.float32)
    query_heads = features(queries).reshape(count, H, DH)
    state_heads = state[:DH].reshape(DH, H, DH)
    norm_heads = state[DH].reshape(H, DH)
    numer = jnp.einsum("phd,dhe->phe", query_heads, state_heads, precision=highest)
    denom = jnp.sum(query_heads * norm_heads[None], axis=2)
    attended = numer / denom[:, :, None]
    weight_heads = score_weight.reshape(H, DH)
    scores = jnp.sum(attended * weight_heads[None], axis=(1, 2))
    slots = lax.broadcasted_iota(jnp.int32, (pair_rows.shape[0], count), 1)
    is_better = slots == pair_rows[:, 0:1]
    is_worse = slots == pair_rows[:, 1:2]
    better = jnp.sum(jnp.where(is_better, scores[None, :], 0.0), axis=1)
    worse = jnp.sum(jnp.where(is_worse, scores[None, :], 0.0), axis=1)
    delta = worse - better
    pair_loss = jax.nn.softplus(delta)
    push = jax.nn.sigmoid(delta)
    score_grad = jnp.sum(
        jnp.where(is_worse, push[:, None], 0.0) - jnp.where(is_better, push[:, None], 0.0),
        axis=0,
    )
    attended_grad = score_grad[:, None, None] * weight_heads[None]
    numer_grad = attended_grad / denom[:, :, None]
    denom_grad = -jnp.sum(attended_grad * attended, axis=2) / denom
    outer_grad = jnp.einsum("phd,phe->dhe", query_heads, numer_grad, precision=highest).reshape(
        DH, H * DH
    )
    norm_grad = jnp.sum(query_heads * denom_grad[:, :, None], axis=0).reshape(H * DH)
    pose_state = jnp.concatenate([outer_grad, norm_grad[None, :]], axis=0)
    feat_grad = (
        jnp.einsum("phe,dhe->phd", numer_grad, state_heads, precision=highest)
        + denom_grad[:, :, None] * norm_heads[None]
    )
    query_grad = (feat_grad.reshape(count, H * DH) * slope(queries)).astype(jnp.bfloat16)
    pose_grad = lax.dot_general(
        query_grad, w_query, (((1,), (1,)), ((), ())), preferred_element_type=jnp.float32
    )
    return (pair_loss, pose_grad.astype(jnp.bfloat16), pose_state)


def pose_kernel(pose_ref, pair_ref, state_ref, query_ref, weight_ref, loss_ref, grad_ref, back_ref, feat_ref):
    count, width = pose_ref.shape
    lanes = 2 * DH
    queries = jnp.dot(pose_ref[...], query_ref[...], preferred_element_type=jnp.float32)
    query_feat = features(queries)
    norm = state_ref[DH : DH + 1, :]
    weight = weight_ref[...]
    head_row = lax.broadcasted_iota(jnp.int32, (lanes, lanes), 0) // DH
    head_col = lax.broadcasted_iota(jnp.int32, (lanes, lanes), 1) // DH
    same = head_row == head_col
    ones = same.astype(jnp.float32)
    blocks, numers, denoms = [], [], []
    scores = jnp.zeros((count, 1), jnp.float32)
    for g in range(width // lanes):
        cols = slice(g * lanes, (g + 1) * lanes)
        part = state_ref[0:DH, cols]
        block = jnp.where(same, jnp.concatenate([part, part], axis=0), 0.0)
        feat = query_feat[:, cols]
        numer = jnp.dot(feat, block, precision=highest, preferred_element_type=jnp.float32)
        denom = jnp.dot(
            feat * norm[:, cols], ones, precision=highest, preferred_element_type=jnp.float32
        )
        attended = numer / denom
        scores = scores + jnp.sum(attended * weight[:, cols], axis=1, keepdims=True)
        blocks.append(block)
        numers.append(attended)
        denoms.append(denom)
    slots = lax.broadcasted_iota(jnp.int32, (count, pair_ref.shape[1]), 0)
    is_better = slots == pair_ref[0:1, :]
    is_worse = slots == pair_ref[1:2, :]
    better = jnp.sum(jnp.where(is_better, scores, 0.0), axis=0, keepdims=True)
    worse = jnp.sum(jnp.where(is_worse, scores, 0.0), axis=0, keepdims=True)
    delta = worse - better
    loss_ref[...] = jnp.maximum(delta, 0.0) + jnp.log1p(jnp.exp(-jnp.abs(delta)))
    push = 1.0 / (1.0 + jnp.exp(-delta))
    score_grad = jnp.sum(
        jnp.where(is_worse, push, 0.0) - jnp.where(is_better, push, 0.0), axis=1, keepdims=True
    )
    low = lax.broadcasted_iota(jnp.int32, (DH, lanes), 1) < DH
    for g in range(width // lanes):
        cols = slice(g * lanes, (g + 1) * lanes)
        feat = query_feat[:, cols]
        attended_grad = score_grad * weight[:, cols]
        numer_grad = attended_grad / denoms[g]
        denom_grad = -jnp.dot(
            attended_grad * numers[g], ones, precision=highest, preferred_element_type=jnp.float32
        ) / denoms[g]
        outer = jnp.dot(feat.T, numer_grad, precision=highest, preferred_element_type=jnp.float32)
        back_ref[0:DH, cols] = jnp.where(low, outer[:DH], outer[DH:])
        back_ref[DH : DH + 1, cols] = jnp.sum(feat * denom_grad, axis=0, keepdims=True)
        feat_grad = lax.dot_general(
            numer_grad,
            blocks[g],
            (((1,), (1,)), ((), ())),
            precision=highest,
            preferred_element_type=jnp.float32,
        ) + denom_grad * norm[:, cols]
        feat_ref[:, cols] = (feat_grad * slope(queries[:, cols])).astype(feat_ref.dtype)
    grad = lax.dot_general(
        feat_ref[...], query_ref[...], (((1,), (1,)), ((), ())), preferred_element_type=jnp.float32
    )
    grad_ref[...] = grad.astype(grad_ref.dtype)


def pose_fused(pose_rows, pair_rows, state, w_query, score_weight, interpret=False):
    count, width = pose_rows.shape
    pairs_t = pair_rows.T
    loss, grad, back = pl.pallas_call(
        pose_kernel,
        out_shape=(
            jax.ShapeDtypeStruct((1, pair_rows.shape[0]), jnp.float32),
            jax.ShapeDtypeStruct((count, width), jnp.bfloat16),
            jax.ShapeDtypeStruct(state.shape, jnp.float32),
        ),
        scratch_shapes=[pltpu.VMEM((count, width), jnp.bfloat16)],
        interpret=interpret,
    )(pose_rows, pairs_t, state, w_query, score_weight.reshape(1, width))
    return (loss.reshape(pair_rows.shape[0]), grad, back)


def back_kernel(feat_ref, val_ref, keys_ref, grad_ref, full_ref, out_ref, both_ref):
    width = feat_ref.shape[1]
    lanes = 2 * DH
    head_row = lax.broadcasted_iota(jnp.int32, (lanes, lanes), 0) // DH
    head_col = lax.broadcasted_iota(jnp.int32, (lanes, lanes), 1) // DH
    same = head_row == head_col
    for g in range(width // lanes):
        cols = slice(g * lanes, (g + 1) * lanes)
        part = grad_ref[0:DH, cols].astype(jnp.float32)
        block = jnp.where(same, jnp.concatenate([part, part], axis=0), 0.0).astype(jnp.bfloat16)
        feat_grad = lax.dot_general(
            val_ref[:, cols], block, (((1,), (1,)), ((), ())), preferred_element_type=jnp.float32
        ) + grad_ref[DH : DH + 1, cols].astype(jnp.float32)
        both_ref[:, cols] = (feat_grad * slope(keys_ref[:, cols])).astype(both_ref.dtype)
        value_grad = jnp.dot(feat_ref[:, cols], block, preferred_element_type=jnp.float32)
        both_ref[:, width + g * lanes : width + (g + 1) * lanes] = value_grad.astype(both_ref.dtype)
    total = lax.dot_general(
        both_ref[...], full_ref[...], (((1,), (1,)), ((), ())), preferred_element_type=jnp.float32
    )
    out_ref[...] = total.astype(out_ref.dtype)


def back_fused(key_feat, val_round, keys, state_grad, full_both, interpret=False):
    rows, width = key_feat.shape
    return pl.pallas_call(
        back_kernel,
        out_shape=jax.ShapeDtypeStruct((rows, width), jnp.bfloat16),
        scratch_shapes=[pltpu.VMEM((rows, 2 * width), jnp.bfloat16)],
        interpret=interpret,
    )(key_feat, val_round, keys, state_grad, full_both)


def gather_rows(shard):
    count = lax.axis_size("blk")
    if count != 8:
        return lax.all_gather(shard, "blk", axis=0, tiled=True)
    position = lax.axis_index("blk")
    rows = shard.shape[0]
    odd = position % 2
    first = jnp.where(odd == 1, 4, 2)
    second = 6 - first
    swap = [(s, s ^ 1) for s in range(count)]
    twin_own = lax.ppermute(shard, "blk", swap)
    early = lax.ppermute(shard, "blk", [(s, s ^ (4 if s % 2 else 2)) for s in range(count)])
    twin_early = lax.ppermute(early, "blk", swap)
    late = lax.ppermute(
        jnp.stack([shard, early]), "blk", [(s, s ^ (2 if s % 2 else 4)) for s in range(count)]
    )
    twin_late = lax.ppermute(late, "blk", swap)
    twin = position ^ 1
    sources = [
        ([shard, twin_own, early, twin_early], [position, twin, position ^ first, twin ^ second]),
        (
            [late[0], late[1], twin_late[0], twin_late[1]],
            [position ^ second, position ^ 6, twin ^ first, twin ^ 6],
        ),
    ]
    full = jnp.zeros((count,) + shard.shape, shard.dtype)
    for pieces, where in sources:
        for k, at in enumerate(where):
            full = lax.dynamic_update_slice(full, pieces[k][None], (at, 0, 0))
    return full.reshape(count * rows, shard.shape[1])


def shards(receptor, poses, pairs, block_complex, w_key, w_value, w_query, score_weight):
    rows = receptor.shape[0]
    width = receptor.shape[1]
    contract = (((1,), (1,)), ((), ()))
    full_both = gather_rows(jnp.concatenate([w_key, w_value], axis=1))
    both = jnp.dot(receptor, full_both, preferred_element_type=jnp.float32)
    keys = both[:, :width]
    values = both[:, width:]
    key_feat = features(keys).astype(jnp.bfloat16)
    val_round = values.astype(jnp.bfloat16)
    state = complex_sum(local_state(key_feat, val_round), block_complex)
    pair_loss, pose_grad, pose_state = pose_fused(poses, pairs, state, w_query, score_weight)
    state_grad = complex_sum(pose_state, block_complex).astype(jnp.bfloat16)
    total = back_fused(key_feat, val_round, keys, state_grad, full_both)
    return (pair_loss, pose_grad, total)


def solution(mesh):
    placed = (
        P(("sec", "blk"), None),
        P(("sec", "blk"), None),
        P(("sec", "blk"), None),
        P(),
        P("blk", None),
        P("blk", None),
        P(),
        P(),
    )
    return jax.shard_map(
        shards,
        mesh=mesh,
        in_specs=placed,
        out_specs=(P(("sec", "blk")), P(("sec", "blk"), None), P(("sec", "blk"), None)),
        check_vma=False,
    )
```

```python
import jax
import jax.numpy as jnp
from jax import lax
from jax.sharding import PartitionSpec as P
from jax.experimental import pallas as pl
from jax.experimental.pallas import tpu as pltpu

H = 16
DH = 64
MOSTB = 4


highest = lax.Precision.HIGHEST


def from_behind(value, axis, steps):
    count = lax.axis_size(axis)
    initial, last = (max(0, -steps), min(count, count - steps))
    return lax.ppermute(value, axis, [(source, source + steps) for source in range(initial, last)])


def features(values):
    return jnp.where(values > 0, values + 1.0, jnp.exp(jnp.minimum(values, 0.0)))


def slope(values):
    return jnp.where(values > 0, jnp.ones_like(values), jnp.exp(jnp.minimum(values, 0.0)))


def local_state(key_feat, val_round):
    rows = key_feat.shape[0]
    key_heads = key_feat.reshape(rows, H, DH)
    val_heads = val_round.reshape(rows, H, DH)
    outer = jnp.einsum(
        "thd,the->dhe", key_heads, val_heads, preferred_element_type=jnp.float32
    ).reshape(DH, H * DH)
    norm_row = jnp.sum(key_feat, axis=0, dtype=jnp.float32)
    return jnp.concatenate([outer, norm_row[None, :]], axis=0)


def complex_total(own, block_complex):
    position = lax.axis_index(("sec", "blk"))
    blocks = block_complex.shape[0]
    mine = jnp.take(block_complex, position)
    total = own
    for reach in range(1, MOSTB):
        lower = from_behind(own.astype(jnp.bfloat16), ("sec", "blk"), reach).astype(own.dtype)
        upper = from_behind(own.astype(jnp.bfloat16), ("sec", "blk"), -reach).astype(own.dtype)
        below = jnp.take(block_complex, jnp.maximum(position - reach, 0))
        above = jnp.take(block_complex, jnp.minimum(position + reach, blocks - 1))
        take_lower = jnp.logical_and(position - reach >= 0, below == mine)
        take_upper = jnp.logical_and(position + reach < blocks, above == mine)
        total = total + jnp.where(take_lower, lower, 0.0) + jnp.where(take_upper, upper, 0.0)
    return total


def send(value, axis, pairs):
    return lax.ppermute(value, axis, pairs)


def complex_sum(own, block_complex):
    axis = ("sec", "blk")
    count = lax.axis_size(axis)
    position = lax.axis_index(axis)
    last = block_complex.shape[0] - 1

    def complex_of(block):
        return jnp.take(block_complex, jnp.clip(block, 0, last))

    def kept(value, block, target):
        inside = jnp.logical_and(target >= 0, target <= last)
        return jnp.where(jnp.logical_and(inside, complex_of(block) == complex_of(target)), value, 0.0)

    narrow = own.astype(jnp.bfloat16)
    twin = position ^ 1
    sibling = send(narrow, axis, [(s, s ^ 1) for s in range(count)]).astype(own.dtype)
    odd = position % 2 == 1
    far_target = jnp.where(odd, position + 3, position - 3)
    far = send(
        kept(own, position, far_target).astype(jnp.bfloat16),
        axis,
        [(s, s + 3) for s in range(1, count - 3, 2)] + [(s, s - 3) for s in range(4, count, 2)],
    )
    low = jnp.where(odd, sibling, own)
    high = jnp.where(odd, own, sibling)
    first = position - position % 2

    def chip_part(target):
        return (kept(low, first, target) + kept(high, first + 1, target)).astype(jnp.bfloat16)

    up = send(chip_part(position + 2), axis, [(s, s + 2) for s in range(count - 2)])
    down = send(chip_part(position - 2), axis, [(s, s - 2) for s in range(2, count)])
    total = own + kept(sibling, twin, position)
    return total + up.astype(own.dtype) + down.astype(own.dtype) + far.astype(own.dtype)


def pose_side(pose_rows, pair_rows, state, w_query, score_weight):
    count = pose_rows.shape[0]
    queries = jnp.dot(pose_rows, w_query, preferred_element_type=jnp.float32)
    query_heads = features(queries).reshape(count, H, DH)
    state_heads = state[:DH].reshape(DH, H, DH)
    norm_heads = state[DH].reshape(H, DH)
    numer = jnp.einsum("phd,dhe->phe", query_heads, state_heads, precision=highest)
    denom = jnp.sum(query_heads * norm_heads[None], axis=2)
    attended = numer / denom[:, :, None]
    weight_heads = score_weight.reshape(H, DH)
    scores = jnp.sum(attended * weight_heads[None], axis=(1, 2))
    slots = lax.broadcasted_iota(jnp.int32, (pair_rows.shape[0], count), 1)
    is_better = slots == pair_rows[:, 0:1]
    is_worse = slots == pair_rows[:, 1:2]
    better = jnp.sum(jnp.where(is_better, scores[None, :], 0.0), axis=1)
    worse = jnp.sum(jnp.where(is_worse, scores[None, :], 0.0), axis=1)
    delta = worse - better
    pair_loss = jax.nn.softplus(delta)
    push = jax.nn.sigmoid(delta)
    score_grad = jnp.sum(
        jnp.where(is_worse, push[:, None], 0.0) - jnp.where(is_better, push[:, None], 0.0),
        axis=0,
    )
    attended_grad = score_grad[:, None, None] * weight_heads[None]
    numer_grad = attended_grad / denom[:, :, None]
    denom_grad = -jnp.sum(attended_grad * attended, axis=2) / denom
    outer_grad = jnp.einsum("phd,phe->dhe", query_heads, numer_grad, precision=highest).reshape(
        DH, H * DH
    )
    norm_grad = jnp.sum(query_heads * denom_grad[:, :, None], axis=0).reshape(H * DH)
    pose_state = jnp.concatenate([outer_grad, norm_grad[None, :]], axis=0)
    feat_grad = (
        jnp.einsum("phe,dhe->phd", numer_grad, state_heads, precision=highest)
        + denom_grad[:, :, None] * norm_heads[None]
    )
    query_grad = (feat_grad.reshape(count, H * DH) * slope(queries)).astype(jnp.bfloat16)
    pose_grad = lax.dot_general(
        query_grad, w_query, (((1,), (1,)), ((), ())), preferred_element_type=jnp.float32
    )
    return (pair_loss, pose_grad.astype(jnp.bfloat16), pose_state)


def pose_kernel(pose_ref, pair_ref, state_ref, query_ref, weight_ref, loss_ref, grad_ref, back_ref, feat_ref):
    count, width = pose_ref.shape
    lanes = 2 * DH
    queries = jnp.dot(pose_ref[...], query_ref[...], preferred_element_type=jnp.float32)
    query_feat = features(queries)
    norm = state_ref[DH : DH + 1, :]
    weight = weight_ref[...]
    head_row = lax.broadcasted_iota(jnp.int32, (lanes, lanes), 0) // DH
    head_col = lax.broadcasted_iota(jnp.int32, (lanes, lanes), 1) // DH
    same = head_row == head_col
    ones = same.astype(jnp.float32)
    blocks, numers, denoms = [], [], []
    scores = jnp.zeros((count, 1), jnp.float32)
    for g in range(width // lanes):
        cols = slice(g * lanes, (g + 1) * lanes)
        part = state_ref[0:DH, cols]
        block = jnp.where(same, jnp.concatenate([part, part], axis=0), 0.0)
        feat = query_feat[:, cols]
        numer = jnp.dot(feat, block, precision=highest, preferred_element_type=jnp.float32)
        denom = jnp.dot(
            feat * norm[:, cols], ones, precision=highest, preferred_element_type=jnp.float32
        )
        attended = numer / denom
        scores = scores + jnp.sum(attended * weight[:, cols], axis=1, keepdims=True)
        blocks.append(block)
        numers.append(attended)
        denoms.append(denom)
    slots = lax.broadcasted_iota(jnp.int32, (count, pair_ref.shape[1]), 0)
    is_better = slots == pair_ref[0:1, :]
    is_worse = slots == pair_ref[1:2, :]
    better = jnp.sum(jnp.where(is_better, scores, 0.0), axis=0, keepdims=True)
    worse = jnp.sum(jnp.where(is_worse, scores, 0.0), axis=0, keepdims=True)
    delta = worse - better
    loss_ref[...] = jnp.maximum(delta, 0.0) + jnp.log1p(jnp.exp(-jnp.abs(delta)))
    push = 1.0 / (1.0 + jnp.exp(-delta))
    score_grad = jnp.sum(
        jnp.where(is_worse, push, 0.0) - jnp.where(is_better, push, 0.0), axis=1, keepdims=True
    )
    low = lax.broadcasted_iota(jnp.int32, (DH, lanes), 1) < DH
    for g in range(width // lanes):
        cols = slice(g * lanes, (g + 1) * lanes)
        feat = query_feat[:, cols]
        attended_grad = score_grad * weight[:, cols]
        numer_grad = attended_grad / denoms[g]
        denom_grad = -jnp.dot(
            attended_grad * numers[g], ones, precision=highest, preferred_element_type=jnp.float32
        ) / denoms[g]
        outer = jnp.dot(feat.T, numer_grad, precision=highest, preferred_element_type=jnp.float32)
        back_ref[0:DH, cols] = jnp.where(low, outer[:DH], outer[DH:])
        back_ref[DH : DH + 1, cols] = jnp.sum(feat * denom_grad, axis=0, keepdims=True)
        feat_grad = lax.dot_general(
            numer_grad,
            blocks[g],
            (((1,), (1,)), ((), ())),
            precision=highest,
            preferred_element_type=jnp.float32,
        ) + denom_grad * norm[:, cols]
        feat_ref[:, cols] = (feat_grad * slope(queries[:, cols])).astype(feat_ref.dtype)
    grad = lax.dot_general(
        feat_ref[...], query_ref[...], (((1,), (1,)), ((), ())), preferred_element_type=jnp.float32
    )
    grad_ref[...] = grad.astype(grad_ref.dtype)


def pose_fused(pose_rows, pair_rows, state, w_query, score_weight, interpret=False):
    count, width = pose_rows.shape
    pairs_t = pair_rows.T
    loss, grad, back = pl.pallas_call(
        pose_kernel,
        out_shape=(
            jax.ShapeDtypeStruct((1, pair_rows.shape[0]), jnp.float32),
            jax.ShapeDtypeStruct((count, width), jnp.bfloat16),
            jax.ShapeDtypeStruct(state.shape, jnp.float32),
        ),
        scratch_shapes=[pltpu.VMEM((count, width), jnp.bfloat16)],
        interpret=interpret,
    )(pose_rows, pairs_t, state, w_query, score_weight.reshape(1, width))
    return (loss.reshape(pair_rows.shape[0]), grad, back)


def back_kernel(feat_ref, val_ref, keys_ref, grad_ref, full_ref, out_ref, both_ref):
    width = feat_ref.shape[1]
    lanes = 2 * DH
    head_row = lax.broadcasted_iota(jnp.int32, (lanes, lanes), 0) // DH
    head_col = lax.broadcasted_iota(jnp.int32, (lanes, lanes), 1) // DH
    same = head_row == head_col
    for g in range(width // lanes):
        cols = slice(g * lanes, (g + 1) * lanes)
        part = grad_ref[0:DH, cols].astype(jnp.float32)
        block = jnp.where(same, jnp.concatenate([part, part], axis=0), 0.0).astype(jnp.bfloat16)
        feat_grad = lax.dot_general(
            val_ref[:, cols], block, (((1,), (1,)), ((), ())), preferred_element_type=jnp.float32
        ) + grad_ref[DH : DH + 1, cols].astype(jnp.float32)
        both_ref[:, cols] = (feat_grad * slope(keys_ref[:, cols])).astype(both_ref.dtype)
        value_grad = jnp.dot(feat_ref[:, cols], block, preferred_element_type=jnp.float32)
        both_ref[:, width + g * lanes : width + (g + 1) * lanes] = value_grad.astype(both_ref.dtype)
    total = lax.dot_general(
        both_ref[...], full_ref[...], (((1,), (1,)), ((), ())), preferred_element_type=jnp.float32
    )
    out_ref[...] = total.astype(out_ref.dtype)


def back_fused(key_feat, val_round, keys, state_grad, full_both, interpret=False):
    rows, width = key_feat.shape
    return pl.pallas_call(
        back_kernel,
        out_shape=jax.ShapeDtypeStruct((rows, width), jnp.bfloat16),
        scratch_shapes=[pltpu.VMEM((rows, 2 * width), jnp.bfloat16)],
        interpret=interpret,
    )(key_feat, val_round, keys, state_grad, full_both)


def gather_rows(shard):
    count = lax.axis_size("blk")
    if count != 8:
        return lax.all_gather(shard, "blk", axis=0, tiled=True), None
    position = lax.axis_index("blk")
    rows = shard.shape[0]
    odd = position % 2
    first = jnp.where(odd == 1, 4, 2)
    second = 6 - first
    swap = [(s, s ^ 1) for s in range(count)]
    twin_own = lax.ppermute(shard, "blk", swap)
    early = lax.ppermute(shard, "blk", [(s, s ^ (4 if s % 2 else 2)) for s in range(count)])
    twin_early = lax.ppermute(early, "blk", swap)
    late = lax.ppermute(
        jnp.stack([shard, early]), "blk", [(s, s ^ (2 if s % 2 else 4)) for s in range(count)]
    )
    twin_late = lax.ppermute(late, "blk", swap)
    twin = position ^ 1
    sources = [
        ([shard, twin_own, early, twin_early], [position, twin, position ^ first, twin ^ second]),
        ([late[0], late[1]], [position ^ second, position ^ 6]),
    ]
    full = jnp.zeros((count,) + shard.shape, shard.dtype)
    for pieces, where in sources:
        for k, at in enumerate(where):
            full = lax.dynamic_update_slice(full, pieces[k][None], (at, 0, 0))
    return full, (twin_late, [twin ^ first, twin ^ 6])


def shards(receptor, poses, pairs, block_complex, w_key, w_value, w_query, score_weight):
    rows = receptor.shape[0]
    width = receptor.shape[1]
    full_both, rest = gather_rows(jnp.concatenate([w_key, w_value], axis=1))
    if rest is None:
        both = jnp.dot(receptor, full_both, preferred_element_type=jnp.float32)
    else:
        pieces, where = rest
        part = full_both.shape[1]
        both = jnp.dot(
            receptor, full_both.reshape(-1, full_both.shape[2]), preferred_element_type=jnp.float32
        )
        picked = jnp.concatenate(
            [lax.dynamic_slice_in_dim(receptor, at * part, part, axis=1) for at in where], axis=1
        )
        both = both + jnp.dot(
            picked, pieces.reshape(-1, pieces.shape[2]), preferred_element_type=jnp.float32
        )
        for k, at in enumerate(where):
            full_both = lax.dynamic_update_slice(full_both, pieces[k][None], (at, 0, 0))
        full_both = full_both.reshape(-1, full_both.shape[2])
    keys = both[:, :width]
    values = both[:, width:]
    key_feat = features(keys).astype(jnp.bfloat16)
    val_round = values.astype(jnp.bfloat16)
    state = complex_sum(local_state(key_feat, val_round), block_complex)
    pair_loss, pose_grad, pose_state = pose_fused(poses, pairs, state, w_query, score_weight)
    state_grad = complex_sum(pose_state, block_complex).astype(jnp.bfloat16)
    total = back_fused(key_feat, val_round, keys, state_grad, full_both)
    return (pair_loss, pose_grad, total)


def solution(mesh):
    placed = (
        P(("sec", "blk"), None),
        P(("sec", "blk"), None),
        P(("sec", "blk"), None),
        P(),
        P("blk", None),
        P("blk", None),
        P(),
        P(),
    )
    return jax.shard_map(
        shards,
        mesh=mesh,
        in_specs=placed,
        out_specs=(P(("sec", "blk")), P(("sec", "blk"), None), P(("sec", "blk"), None)),
        check_vma=False,
    )
```

```python
import jax
import jax.numpy as jnp
from jax import lax
from jax.sharding import PartitionSpec as P
from jax.experimental import pallas as pl
from jax.experimental.pallas import tpu as pltpu

H = 16
DH = 64
MOSTB = 4


highest = lax.Precision.HIGHEST


def from_behind(value, axis, steps):
    count = lax.axis_size(axis)
    initial, last = (max(0, -steps), min(count, count - steps))
    return lax.ppermute(value, axis, [(source, source + steps) for source in range(initial, last)])


def features(values):
    return jnp.where(values > 0, values + 1.0, jnp.exp(jnp.minimum(values, 0.0)))


def slope(values):
    return jnp.where(values > 0, jnp.ones_like(values), jnp.exp(jnp.minimum(values, 0.0)))


def local_state(key_feat, val_round):
    rows = key_feat.shape[0]
    key_heads = key_feat.reshape(rows, H, DH)
    val_heads = val_round.reshape(rows, H, DH)
    outer = jnp.einsum(
        "thd,the->dhe", key_heads, val_heads, preferred_element_type=jnp.float32
    ).reshape(DH, H * DH)
    norm_row = jnp.sum(key_feat, axis=0, dtype=jnp.float32)
    return jnp.concatenate([outer, norm_row[None, :]], axis=0)


def complex_total(own, block_complex):
    position = lax.axis_index(("sec", "blk"))
    blocks = block_complex.shape[0]
    mine = jnp.take(block_complex, position)
    total = own
    for reach in range(1, MOSTB):
        lower = from_behind(own.astype(jnp.bfloat16), ("sec", "blk"), reach).astype(own.dtype)
        upper = from_behind(own.astype(jnp.bfloat16), ("sec", "blk"), -reach).astype(own.dtype)
        below = jnp.take(block_complex, jnp.maximum(position - reach, 0))
        above = jnp.take(block_complex, jnp.minimum(position + reach, blocks - 1))
        take_lower = jnp.logical_and(position - reach >= 0, below == mine)
        take_upper = jnp.logical_and(position + reach < blocks, above == mine)
        total = total + jnp.where(take_lower, lower, 0.0) + jnp.where(take_upper, upper, 0.0)
    return total


def send(value, axis, pairs):
    return lax.ppermute(value, axis, pairs)


def complex_sum(own, block_complex):
    axis = ("sec", "blk")
    count = lax.axis_size(axis)
    position = lax.axis_index(axis)
    last = block_complex.shape[0] - 1

    def complex_of(block):
        return jnp.take(block_complex, jnp.clip(block, 0, last))

    def kept(value, block, target):
        inside = jnp.logical_and(target >= 0, target <= last)
        return jnp.where(jnp.logical_and(inside, complex_of(block) == complex_of(target)), value, 0.0)

    narrow = own.astype(jnp.bfloat16)
    twin = position ^ 1
    sibling = send(narrow, axis, [(s, s ^ 1) for s in range(count)]).astype(own.dtype)
    odd = position % 2 == 1
    far_target = jnp.where(odd, position + 3, position - 3)
    far = send(
        kept(own, position, far_target).astype(jnp.bfloat16),
        axis,
        [(s, s + 3) for s in range(1, count - 3, 2)] + [(s, s - 3) for s in range(4, count, 2)],
    )
    low = jnp.where(odd, sibling, own)
    high = jnp.where(odd, own, sibling)
    first = position - position % 2

    def chip_part(target):
        return (kept(low, first, target) + kept(high, first + 1, target)).astype(jnp.bfloat16)

    up = send(chip_part(position + 2), axis, [(s, s + 2) for s in range(count - 2)])
    down = send(chip_part(position - 2), axis, [(s, s - 2) for s in range(2, count)])
    total = own + kept(sibling, twin, position)
    return total + up.astype(own.dtype) + down.astype(own.dtype) + far.astype(own.dtype)


def pose_side(pose_rows, pair_rows, state, w_query, score_weight):
    count = pose_rows.shape[0]
    queries = jnp.dot(pose_rows, w_query, preferred_element_type=jnp.float32)
    query_heads = features(queries).reshape(count, H, DH)
    state_heads = state[:DH].reshape(DH, H, DH)
    norm_heads = state[DH].reshape(H, DH)
    numer = jnp.einsum("phd,dhe->phe", query_heads, state_heads, precision=highest)
    denom = jnp.sum(query_heads * norm_heads[None], axis=2)
    attended = numer / denom[:, :, None]
    weight_heads = score_weight.reshape(H, DH)
    scores = jnp.sum(attended * weight_heads[None], axis=(1, 2))
    slots = lax.broadcasted_iota(jnp.int32, (pair_rows.shape[0], count), 1)
    is_better = slots == pair_rows[:, 0:1]
    is_worse = slots == pair_rows[:, 1:2]
    better = jnp.sum(jnp.where(is_better, scores[None, :], 0.0), axis=1)
    worse = jnp.sum(jnp.where(is_worse, scores[None, :], 0.0), axis=1)
    delta = worse - better
    pair_loss = jax.nn.softplus(delta)
    push = jax.nn.sigmoid(delta)
    score_grad = jnp.sum(
        jnp.where(is_worse, push[:, None], 0.0) - jnp.where(is_better, push[:, None], 0.0),
        axis=0,
    )
    attended_grad = score_grad[:, None, None] * weight_heads[None]
    numer_grad = attended_grad / denom[:, :, None]
    denom_grad = -jnp.sum(attended_grad * attended, axis=2) / denom
    outer_grad = jnp.einsum("phd,phe->dhe", query_heads, numer_grad, precision=highest).reshape(
        DH, H * DH
    )
    norm_grad = jnp.sum(query_heads * denom_grad[:, :, None], axis=0).reshape(H * DH)
    pose_state = jnp.concatenate([outer_grad, norm_grad[None, :]], axis=0)
    feat_grad = (
        jnp.einsum("phe,dhe->phd", numer_grad, state_heads, precision=highest)
        + denom_grad[:, :, None] * norm_heads[None]
    )
    query_grad = (feat_grad.reshape(count, H * DH) * slope(queries)).astype(jnp.bfloat16)
    pose_grad = lax.dot_general(
        query_grad, w_query, (((1,), (1,)), ((), ())), preferred_element_type=jnp.float32
    )
    return (pair_loss, pose_grad.astype(jnp.bfloat16), pose_state)


def pose_kernel(pose_ref, pair_ref, state_ref, query_ref, weight_ref, loss_ref, grad_ref, back_ref, feat_ref):
    count, width = pose_ref.shape
    lanes = 2 * DH
    queries = jnp.dot(pose_ref[...], query_ref[...], preferred_element_type=jnp.float32)
    query_feat = features(queries)
    norm = state_ref[DH : DH + 1, :]
    weight = weight_ref[...]
    head_row = lax.broadcasted_iota(jnp.int32, (lanes, lanes), 0) // DH
    head_col = lax.broadcasted_iota(jnp.int32, (lanes, lanes), 1) // DH
    same = head_row == head_col
    ones = same.astype(jnp.float32)
    blocks, numers, denoms = [], [], []
    scores = jnp.zeros((count, 1), jnp.float32)
    for g in range(width // lanes):
        cols = slice(g * lanes, (g + 1) * lanes)
        part = state_ref[0:DH, cols]
        block = jnp.where(same, jnp.concatenate([part, part], axis=0), 0.0)
        feat = query_feat[:, cols]
        numer = jnp.dot(feat, block, precision=highest, preferred_element_type=jnp.float32)
        denom = jnp.dot(
            feat * norm[:, cols], ones, precision=highest, preferred_element_type=jnp.float32
        )
        attended = numer / denom
        scores = scores + jnp.sum(attended * weight[:, cols], axis=1, keepdims=True)
        blocks.append(block)
        numers.append(attended)
        denoms.append(denom)
    slots = lax.broadcasted_iota(jnp.int32, (count, pair_ref.shape[1]), 0)
    is_better = slots == pair_ref[0:1, :]
    is_worse = slots == pair_ref[1:2, :]
    better = jnp.sum(jnp.where(is_better, scores, 0.0), axis=0, keepdims=True)
    worse = jnp.sum(jnp.where(is_worse, scores, 0.0), axis=0, keepdims=True)
    delta = worse - better
    loss_ref[...] = jnp.maximum(delta, 0.0) + jnp.log1p(jnp.exp(-jnp.abs(delta)))
    push = 1.0 / (1.0 + jnp.exp(-delta))
    score_grad = jnp.sum(
        jnp.where(is_worse, push, 0.0) - jnp.where(is_better, push, 0.0), axis=1, keepdims=True
    )
    low = lax.broadcasted_iota(jnp.int32, (DH, lanes), 1) < DH
    for g in range(width // lanes):
        cols = slice(g * lanes, (g + 1) * lanes)
        feat = query_feat[:, cols]
        attended_grad = score_grad * weight[:, cols]
        numer_grad = attended_grad / denoms[g]
        denom_grad = -jnp.dot(
            attended_grad * numers[g], ones, precision=highest, preferred_element_type=jnp.float32
        ) / denoms[g]
        outer = jnp.dot(feat.T, numer_grad, precision=highest, preferred_element_type=jnp.float32)
        back_ref[0:DH, cols] = jnp.where(low, outer[:DH], outer[DH:])
        back_ref[DH : DH + 1, cols] = jnp.sum(feat * denom_grad, axis=0, keepdims=True)
        feat_grad = lax.dot_general(
            numer_grad,
            blocks[g],
            (((1,), (1,)), ((), ())),
            precision=highest,
            preferred_element_type=jnp.float32,
        ) + denom_grad * norm[:, cols]
        feat_ref[:, cols] = (feat_grad * slope(queries[:, cols])).astype(feat_ref.dtype)
    grad = lax.dot_general(
        feat_ref[...], query_ref[...], (((1,), (1,)), ((), ())), preferred_element_type=jnp.float32
    )
    grad_ref[...] = grad.astype(grad_ref.dtype)


def pose_fused(pose_rows, pair_rows, state, w_query, score_weight, interpret=False):
    count, width = pose_rows.shape
    pairs_t = pair_rows.T
    loss, grad, back = pl.pallas_call(
        pose_kernel,
        out_shape=(
            jax.ShapeDtypeStruct((1, pair_rows.shape[0]), jnp.float32),
            jax.ShapeDtypeStruct((count, width), jnp.bfloat16),
            jax.ShapeDtypeStruct(state.shape, jnp.float32),
        ),
        scratch_shapes=[pltpu.VMEM((count, width), jnp.bfloat16)],
        interpret=interpret,
    )(pose_rows, pairs_t, state, w_query, score_weight.reshape(1, width))
    return (loss.reshape(pair_rows.shape[0]), grad, back)


def back_kernel(feat_ref, val_ref, keys_ref, grad_ref, full_ref, out_ref, both_ref):
    width = feat_ref.shape[1]
    lanes = 2 * DH
    head_row = lax.broadcasted_iota(jnp.int32, (lanes, lanes), 0) // DH
    head_col = lax.broadcasted_iota(jnp.int32, (lanes, lanes), 1) // DH
    same = head_row == head_col
    for g in range(width // lanes):
        cols = slice(g * lanes, (g + 1) * lanes)
        part = grad_ref[0:DH, cols].astype(jnp.float32)
        block = jnp.where(same, jnp.concatenate([part, part], axis=0), 0.0).astype(jnp.bfloat16)
        feat_grad = lax.dot_general(
            val_ref[:, cols], block, (((1,), (1,)), ((), ())), preferred_element_type=jnp.float32
        ) + grad_ref[DH : DH + 1, cols].astype(jnp.float32)
        both_ref[:, cols] = (feat_grad * slope(keys_ref[:, cols])).astype(both_ref.dtype)
        value_grad = jnp.dot(feat_ref[:, cols], block, preferred_element_type=jnp.float32)
        both_ref[:, width + g * lanes : width + (g + 1) * lanes] = value_grad.astype(both_ref.dtype)
    total = lax.dot_general(
        both_ref[...], full_ref[...], (((1,), (1,)), ((), ())), preferred_element_type=jnp.float32
    )
    out_ref[...] = total.astype(out_ref.dtype)


def back_fused(key_feat, val_round, keys, state_grad, full_both, interpret=False):
    rows, width = key_feat.shape
    return pl.pallas_call(
        back_kernel,
        out_shape=jax.ShapeDtypeStruct((rows, width), jnp.bfloat16),
        scratch_shapes=[pltpu.VMEM((rows, 2 * width), jnp.bfloat16)],
        interpret=interpret,
    )(key_feat, val_round, keys, state_grad, full_both)


def gather_rows(shard):
    count = lax.axis_size("blk")
    if count != 8:
        return lax.all_gather(shard, "blk", axis=0, tiled=True), None
    position = lax.axis_index("blk")
    rows = shard.shape[0]
    odd = position % 2
    first = jnp.where(odd == 1, 4, 2)
    second = 6 - first
    swap = [(s, s ^ 1) for s in range(count)]
    twin_own = lax.ppermute(shard, "blk", swap)
    early = lax.ppermute(shard, "blk", [(s, s ^ (4 if s % 2 else 2)) for s in range(count)])
    twin_early = lax.ppermute(early, "blk", swap)
    late = lax.ppermute(
        jnp.stack([shard, early]), "blk", [(s, s ^ (2 if s % 2 else 4)) for s in range(count)]
    )
    twin_late = lax.ppermute(late, "blk", swap)
    twin = position ^ 1
    sources = [
        ([shard, twin_own, early, twin_early], [position, twin, position ^ first, twin ^ second]),
    ]
    full = jnp.zeros((count,) + shard.shape, shard.dtype)
    for pieces, where in sources:
        for k, at in enumerate(where):
            full = lax.dynamic_update_slice(full, pieces[k][None], (at, 0, 0))
    return full, [(late, [position ^ second, position ^ 6]), (twin_late, [twin ^ first, twin ^ 6])]


def shards(receptor, poses, pairs, block_complex, w_key, w_value, w_query, score_weight):
    rows = receptor.shape[0]
    width = receptor.shape[1]
    full_both, rest = gather_rows(jnp.concatenate([w_key, w_value], axis=1))
    if rest is None:
        both = jnp.dot(receptor, full_both, preferred_element_type=jnp.float32)
    else:
        part = full_both.shape[1]
        both = jnp.dot(
            receptor, full_both.reshape(-1, full_both.shape[2]), preferred_element_type=jnp.float32
        )
        for pieces, where in rest:
            picked = jnp.concatenate(
                [lax.dynamic_slice_in_dim(receptor, at * part, part, axis=1) for at in where], axis=1
            )
            both = both + jnp.dot(
                picked, pieces.reshape(-1, pieces.shape[2]), preferred_element_type=jnp.float32
            )
        for pieces, where in rest:
            for k, at in enumerate(where):
                full_both = lax.dynamic_update_slice(full_both, pieces[k][None], (at, 0, 0))
        full_both = full_both.reshape(-1, full_both.shape[2])
    keys = both[:, :width]
    values = both[:, width:]
    key_feat = features(keys).astype(jnp.bfloat16)
    val_round = values.astype(jnp.bfloat16)
    state = complex_sum(local_state(key_feat, val_round), block_complex)
    pair_loss, pose_grad, pose_state = pose_fused(poses, pairs, state, w_query, score_weight)
    state_grad = complex_sum(pose_state, block_complex).astype(jnp.bfloat16)
    total = back_fused(key_feat, val_round, keys, state_grad, full_both)
    return (pair_loss, pose_grad, total)


def solution(mesh):
    placed = (
        P(("sec", "blk"), None),
        P(("sec", "blk"), None),
        P(("sec", "blk"), None),
        P(),
        P("blk", None),
        P("blk", None),
        P(),
        P(),
    )
    return jax.shard_map(
        shards,
        mesh=mesh,
        in_specs=placed,
        out_specs=(P(("sec", "blk")), P(("sec", "blk"), None), P(("sec", "blk"), None)),
        check_vma=False,
    )
```

```python
import jax
import jax.numpy as jnp
from jax import lax
from jax.sharding import PartitionSpec as P
from jax.experimental import pallas as pl
from jax.experimental.pallas import tpu as pltpu

H = 16
DH = 64
MOSTB = 4


highest = lax.Precision.HIGHEST


def from_behind(value, axis, steps):
    count = lax.axis_size(axis)
    initial, last = (max(0, -steps), min(count, count - steps))
    return lax.ppermute(value, axis, [(source, source + steps) for source in range(initial, last)])


def features(values):
    return jnp.where(values > 0, values + 1.0, jnp.exp(jnp.minimum(values, 0.0)))


def slope(values):
    return jnp.where(values > 0, jnp.ones_like(values), jnp.exp(jnp.minimum(values, 0.0)))


def local_state(key_feat, val_round):
    rows = key_feat.shape[0]
    key_heads = key_feat.reshape(rows, H, DH)
    val_heads = val_round.reshape(rows, H, DH)
    outer = jnp.einsum(
        "thd,the->dhe", key_heads, val_heads, preferred_element_type=jnp.float32
    ).reshape(DH, H * DH)
    norm_row = jnp.sum(key_feat, axis=0, dtype=jnp.float32)
    return jnp.concatenate([outer, norm_row[None, :]], axis=0)


def complex_total(own, block_complex):
    position = lax.axis_index(("sec", "blk"))
    blocks = block_complex.shape[0]
    mine = jnp.take(block_complex, position)
    total = own
    for reach in range(1, MOSTB):
        lower = from_behind(own.astype(jnp.bfloat16), ("sec", "blk"), reach).astype(own.dtype)
        upper = from_behind(own.astype(jnp.bfloat16), ("sec", "blk"), -reach).astype(own.dtype)
        below = jnp.take(block_complex, jnp.maximum(position - reach, 0))
        above = jnp.take(block_complex, jnp.minimum(position + reach, blocks - 1))
        take_lower = jnp.logical_and(position - reach >= 0, below == mine)
        take_upper = jnp.logical_and(position + reach < blocks, above == mine)
        total = total + jnp.where(take_lower, lower, 0.0) + jnp.where(take_upper, upper, 0.0)
    return total


def send(value, axis, pairs):
    return lax.ppermute(value, axis, pairs)


def complex_sum(own, block_complex):
    axis = ("sec", "blk")
    count = lax.axis_size(axis)
    position = lax.axis_index(axis)
    last = block_complex.shape[0] - 1

    def complex_of(block):
        return jnp.take(block_complex, jnp.clip(block, 0, last))

    def kept(value, block, target):
        inside = jnp.logical_and(target >= 0, target <= last)
        return jnp.where(jnp.logical_and(inside, complex_of(block) == complex_of(target)), value, 0.0)

    narrow = own.astype(jnp.bfloat16)
    twin = position ^ 1
    sibling = send(narrow, axis, [(s, s ^ 1) for s in range(count)]).astype(own.dtype)
    odd = position % 2 == 1
    far_target = jnp.where(odd, position + 3, position - 3)
    far = send(
        kept(own, position, far_target).astype(jnp.bfloat16),
        axis,
        [(s, s + 3) for s in range(1, count - 3, 2)] + [(s, s - 3) for s in range(4, count, 2)],
    )
    low = jnp.where(odd, sibling, own)
    high = jnp.where(odd, own, sibling)
    first = position - position % 2

    def chip_part(target):
        return (kept(low, first, target) + kept(high, first + 1, target)).astype(jnp.bfloat16)

    up = send(chip_part(position + 2), axis, [(s, s + 2) for s in range(count - 2)])
    down = send(chip_part(position - 2), axis, [(s, s - 2) for s in range(2, count)])
    total = own + kept(sibling, twin, position)
    return total + up.astype(own.dtype) + down.astype(own.dtype) + far.astype(own.dtype)


def pose_side(pose_rows, pair_rows, state, w_query, score_weight):
    count = pose_rows.shape[0]
    queries = jnp.dot(pose_rows, w_query, preferred_element_type=jnp.float32)
    query_heads = features(queries).reshape(count, H, DH)
    state_heads = state[:DH].reshape(DH, H, DH)
    norm_heads = state[DH].reshape(H, DH)
    numer = jnp.einsum("phd,dhe->phe", query_heads, state_heads, precision=highest)
    denom = jnp.sum(query_heads * norm_heads[None], axis=2)
    attended = numer / denom[:, :, None]
    weight_heads = score_weight.reshape(H, DH)
    scores = jnp.sum(attended * weight_heads[None], axis=(1, 2))
    slots = lax.broadcasted_iota(jnp.int32, (pair_rows.shape[0], count), 1)
    is_better = slots == pair_rows[:, 0:1]
    is_worse = slots == pair_rows[:, 1:2]
    better = jnp.sum(jnp.where(is_better, scores[None, :], 0.0), axis=1)
    worse = jnp.sum(jnp.where(is_worse, scores[None, :], 0.0), axis=1)
    delta = worse - better
    pair_loss = jax.nn.softplus(delta)
    push = jax.nn.sigmoid(delta)
    score_grad = jnp.sum(
        jnp.where(is_worse, push[:, None], 0.0) - jnp.where(is_better, push[:, None], 0.0),
        axis=0,
    )
    attended_grad = score_grad[:, None, None] * weight_heads[None]
    numer_grad = attended_grad / denom[:, :, None]
    denom_grad = -jnp.sum(attended_grad * attended, axis=2) / denom
    outer_grad = jnp.einsum("phd,phe->dhe", query_heads, numer_grad, precision=highest).reshape(
        DH, H * DH
    )
    norm_grad = jnp.sum(query_heads * denom_grad[:, :, None], axis=0).reshape(H * DH)
    pose_state = jnp.concatenate([outer_grad, norm_grad[None, :]], axis=0)
    feat_grad = (
        jnp.einsum("phe,dhe->phd", numer_grad, state_heads, precision=highest)
        + denom_grad[:, :, None] * norm_heads[None]
    )
    query_grad = (feat_grad.reshape(count, H * DH) * slope(queries)).astype(jnp.bfloat16)
    pose_grad = lax.dot_general(
        query_grad, w_query, (((1,), (1,)), ((), ())), preferred_element_type=jnp.float32
    )
    return (pair_loss, pose_grad.astype(jnp.bfloat16), pose_state)


def pose_kernel(pose_ref, pair_ref, state_ref, query_ref, weight_ref, loss_ref, grad_ref, back_ref, feat_ref):
    count, width = pose_ref.shape
    lanes = 2 * DH
    queries = jnp.dot(pose_ref[...], query_ref[...], preferred_element_type=jnp.float32)
    query_feat = features(queries)
    norm = state_ref[DH : DH + 1, :]
    weight = weight_ref[...]
    head_row = lax.broadcasted_iota(jnp.int32, (lanes, lanes), 0) // DH
    head_col = lax.broadcasted_iota(jnp.int32, (lanes, lanes), 1) // DH
    same = head_row == head_col
    ones = same.astype(jnp.float32)
    blocks, numers, denoms = [], [], []
    scores = jnp.zeros((count, 1), jnp.float32)
    for g in range(width // lanes):
        cols = slice(g * lanes, (g + 1) * lanes)
        part = state_ref[0:DH, cols]
        block = jnp.where(same, jnp.concatenate([part, part], axis=0), 0.0)
        feat = query_feat[:, cols]
        numer = jnp.dot(feat, block, precision=highest, preferred_element_type=jnp.float32)
        denom = jnp.dot(
            feat * norm[:, cols], ones, precision=highest, preferred_element_type=jnp.float32
        )
        attended = numer / denom
        scores = scores + jnp.sum(attended * weight[:, cols], axis=1, keepdims=True)
        blocks.append(block)
        numers.append(attended)
        denoms.append(denom)
    slots = lax.broadcasted_iota(jnp.int32, (count, pair_ref.shape[1]), 0)
    is_better = slots == pair_ref[0:1, :]
    is_worse = slots == pair_ref[1:2, :]
    better = jnp.sum(jnp.where(is_better, scores, 0.0), axis=0, keepdims=True)
    worse = jnp.sum(jnp.where(is_worse, scores, 0.0), axis=0, keepdims=True)
    delta = worse - better
    loss_ref[...] = jnp.maximum(delta, 0.0) + jnp.log1p(jnp.exp(-jnp.abs(delta)))
    push = 1.0 / (1.0 + jnp.exp(-delta))
    score_grad = jnp.sum(
        jnp.where(is_worse, push, 0.0) - jnp.where(is_better, push, 0.0), axis=1, keepdims=True
    )
    low = lax.broadcasted_iota(jnp.int32, (DH, lanes), 1) < DH
    for g in range(width // lanes):
        cols = slice(g * lanes, (g + 1) * lanes)
        feat = query_feat[:, cols]
        attended_grad = score_grad * weight[:, cols]
        numer_grad = attended_grad / denoms[g]
        denom_grad = -jnp.dot(
            attended_grad * numers[g], ones, precision=highest, preferred_element_type=jnp.float32
        ) / denoms[g]
        outer = jnp.dot(feat.T, numer_grad, precision=highest, preferred_element_type=jnp.float32)
        back_ref[0:DH, cols] = jnp.where(low, outer[:DH], outer[DH:])
        back_ref[DH : DH + 1, cols] = jnp.sum(feat * denom_grad, axis=0, keepdims=True)
        feat_grad = lax.dot_general(
            numer_grad,
            blocks[g],
            (((1,), (1,)), ((), ())),
            precision=highest,
            preferred_element_type=jnp.float32,
        ) + denom_grad * norm[:, cols]
        feat_ref[:, cols] = (feat_grad * slope(queries[:, cols])).astype(feat_ref.dtype)
    grad = lax.dot_general(
        feat_ref[...], query_ref[...], (((1,), (1,)), ((), ())), preferred_element_type=jnp.float32
    )
    grad_ref[...] = grad.astype(grad_ref.dtype)


def pose_fused(pose_rows, pair_rows, state, w_query, score_weight, interpret=False):
    count, width = pose_rows.shape
    pairs_t = pair_rows.T
    loss, grad, back = pl.pallas_call(
        pose_kernel,
        out_shape=(
            jax.ShapeDtypeStruct((1, pair_rows.shape[0]), jnp.float32),
            jax.ShapeDtypeStruct((count, width), jnp.bfloat16),
            jax.ShapeDtypeStruct(state.shape, jnp.float32),
        ),
        scratch_shapes=[pltpu.VMEM((count, width), jnp.bfloat16)],
        interpret=interpret,
    )(pose_rows, pairs_t, state, w_query, score_weight.reshape(1, width))
    return (loss.reshape(pair_rows.shape[0]), grad, back)


def back_kernel(feat_ref, val_ref, keys_ref, grad_ref, full_ref, out_ref, both_ref):
    width = feat_ref.shape[1]
    lanes = 2 * DH
    head_row = lax.broadcasted_iota(jnp.int32, (lanes, lanes), 0) // DH
    head_col = lax.broadcasted_iota(jnp.int32, (lanes, lanes), 1) // DH
    same = head_row == head_col
    for g in range(width // lanes):
        cols = slice(g * lanes, (g + 1) * lanes)
        part = grad_ref[0:DH, cols].astype(jnp.float32)
        block = jnp.where(same, jnp.concatenate([part, part], axis=0), 0.0).astype(jnp.bfloat16)
        feat_grad = lax.dot_general(
            val_ref[:, cols], block, (((1,), (1,)), ((), ())), preferred_element_type=jnp.float32
        ) + grad_ref[DH : DH + 1, cols].astype(jnp.float32)
        both_ref[:, cols] = (feat_grad * slope(keys_ref[:, cols])).astype(both_ref.dtype)
        value_grad = jnp.dot(feat_ref[:, cols], block, preferred_element_type=jnp.float32)
        both_ref[:, width + g * lanes : width + (g + 1) * lanes] = value_grad.astype(both_ref.dtype)
    total = lax.dot_general(
        both_ref[...], full_ref[...], (((1,), (1,)), ((), ())), preferred_element_type=jnp.float32
    )
    out_ref[...] = total.astype(out_ref.dtype)


def back_fused(key_feat, val_round, keys, state_grad, full_both, interpret=False):
    rows, width = key_feat.shape
    return pl.pallas_call(
        back_kernel,
        out_shape=jax.ShapeDtypeStruct((rows, width), jnp.bfloat16),
        scratch_shapes=[pltpu.VMEM((rows, 2 * width), jnp.bfloat16)],
        interpret=interpret,
    )(key_feat, val_round, keys, state_grad, full_both)


def gather_rows(shard):
    count = lax.axis_size("blk")
    if count != 8:
        return lax.all_gather(shard, "blk", axis=0, tiled=True), None
    position = lax.axis_index("blk")
    rows = shard.shape[0]
    odd = position % 2
    first = jnp.where(odd == 1, 4, 2)
    second = 6 - first
    swap = [(s, s ^ 1) for s in range(count)]
    twin_own = lax.ppermute(shard, "blk", swap)
    early = lax.ppermute(shard, "blk", [(s, s ^ (4 if s % 2 else 2)) for s in range(count)])
    twin_early = lax.ppermute(early, "blk", swap)
    late = lax.ppermute(
        jnp.stack([shard, early]), "blk", [(s, s ^ (2 if s % 2 else 4)) for s in range(count)]
    )
    twin = position ^ 1
    sources = [
        ([shard, twin_own, early, twin_early], [position, twin, position ^ first, twin ^ second]),
    ]
    full = jnp.zeros((count,) + shard.shape, shard.dtype)
    for pieces, where in sources:
        for k, at in enumerate(where):
            full = lax.dynamic_update_slice(full, pieces[k][None], (at, 0, 0))
    return full, (late, [position ^ second, position ^ 6], [twin ^ first, twin ^ 6])


def shards(receptor, poses, pairs, block_complex, w_key, w_value, w_query, score_weight):
    rows = receptor.shape[0]
    width = receptor.shape[1]
    full_both, rest = gather_rows(jnp.concatenate([w_key, w_value], axis=1))
    if rest is None:
        both = jnp.dot(receptor, full_both, preferred_element_type=jnp.float32)
    else:
        part = full_both.shape[1]
        both = jnp.dot(
            receptor, full_both.reshape(-1, full_both.shape[2]), preferred_element_type=jnp.float32
        )
        late, mine, theirs = rest
        both, late = lax.optimization_barrier((both, late))
        count = lax.axis_size("blk")
        twin_late = lax.ppermute(late, "blk", [(s, s ^ 1) for s in range(count)])
        rest = [(late, mine), (twin_late, theirs)]
        for pieces, where in rest:
            picked = jnp.concatenate(
                [lax.dynamic_slice_in_dim(receptor, at * part, part, axis=1) for at in where], axis=1
            )
            both = both + jnp.dot(
                picked, pieces.reshape(-1, pieces.shape[2]), preferred_element_type=jnp.float32
            )
        for pieces, where in rest:
            for k, at in enumerate(where):
                full_both = lax.dynamic_update_slice(full_both, pieces[k][None], (at, 0, 0))
        full_both = full_both.reshape(-1, full_both.shape[2])
    keys = both[:, :width]
    values = both[:, width:]
    key_feat = features(keys).astype(jnp.bfloat16)
    val_round = values.astype(jnp.bfloat16)
    state = complex_sum(local_state(key_feat, val_round), block_complex)
    pair_loss, pose_grad, pose_state = pose_fused(poses, pairs, state, w_query, score_weight)
    state_grad = complex_sum(pose_state, block_complex).astype(jnp.bfloat16)
    total = back_fused(key_feat, val_round, keys, state_grad, full_both)
    return (pair_loss, pose_grad, total)


def solution(mesh):
    placed = (
        P(("sec", "blk"), None),
        P(("sec", "blk"), None),
        P(("sec", "blk"), None),
        P(),
        P("blk", None),
        P("blk", None),
        P(),
        P(),
    )
    return jax.shard_map(
        shards,
        mesh=mesh,
        in_specs=placed,
        out_specs=(P(("sec", "blk")), P(("sec", "blk"), None), P(("sec", "blk"), None)),
        check_vma=False,
    )
```

```python
import jax
import jax.numpy as jnp
from jax import lax
from jax.sharding import PartitionSpec as P
from jax.experimental import pallas as pl
from jax.experimental.pallas import tpu as pltpu

H = 16
DH = 64
MOSTB = 4


highest = lax.Precision.HIGHEST


def from_behind(value, axis, steps):
    count = lax.axis_size(axis)
    initial, last = (max(0, -steps), min(count, count - steps))
    return lax.ppermute(value, axis, [(source, source + steps) for source in range(initial, last)])


def features(values):
    return jnp.where(values > 0, values + 1.0, jnp.exp(jnp.minimum(values, 0.0)))


def slope(values):
    return jnp.where(values > 0, jnp.ones_like(values), jnp.exp(jnp.minimum(values, 0.0)))


def local_state(key_feat, val_round):
    width = key_feat.shape[1]
    outer = lax.dot_general(
        key_feat, val_round, (((0,), (0,)), ((), ())), preferred_element_type=jnp.float32
    )
    head_row = lax.broadcasted_iota(jnp.int32, (width, width), 0) // DH
    head_col = lax.broadcasted_iota(jnp.int32, (width, width), 1) // DH
    diagonal = jnp.where(head_row == head_col, outer, 0.0).reshape(width // DH, DH, width)
    norm_row = jnp.sum(key_feat, axis=0, dtype=jnp.float32)
    return jnp.concatenate([jnp.sum(diagonal, axis=0), norm_row[None, :]], axis=0)


def complex_total(own, block_complex):
    position = lax.axis_index(("sec", "blk"))
    blocks = block_complex.shape[0]
    mine = jnp.take(block_complex, position)
    total = own
    for reach in range(1, MOSTB):
        lower = from_behind(own.astype(jnp.bfloat16), ("sec", "blk"), reach).astype(own.dtype)
        upper = from_behind(own.astype(jnp.bfloat16), ("sec", "blk"), -reach).astype(own.dtype)
        below = jnp.take(block_complex, jnp.maximum(position - reach, 0))
        above = jnp.take(block_complex, jnp.minimum(position + reach, blocks - 1))
        take_lower = jnp.logical_and(position - reach >= 0, below == mine)
        take_upper = jnp.logical_and(position + reach < blocks, above == mine)
        total = total + jnp.where(take_lower, lower, 0.0) + jnp.where(take_upper, upper, 0.0)
    return total


def send(value, axis, pairs):
    return lax.ppermute(value, axis, pairs)


def complex_sum(own, block_complex):
    axis = ("sec", "blk")
    count = lax.axis_size(axis)
    position = lax.axis_index(axis)
    last = block_complex.shape[0] - 1

    def complex_of(block):
        return jnp.take(block_complex, jnp.clip(block, 0, last))

    def kept(value, block, target):
        inside = jnp.logical_and(target >= 0, target <= last)
        return jnp.where(jnp.logical_and(inside, complex_of(block) == complex_of(target)), value, 0.0)

    narrow = own.astype(jnp.bfloat16)
    twin = position ^ 1
    sibling = send(narrow, axis, [(s, s ^ 1) for s in range(count)]).astype(own.dtype)
    odd = position % 2 == 1
    far_target = jnp.where(odd, position + 3, position - 3)
    far = send(
        kept(own, position, far_target).astype(jnp.bfloat16),
        axis,
        [(s, s + 3) for s in range(1, count - 3, 2)] + [(s, s - 3) for s in range(4, count, 2)],
    )
    low = jnp.where(odd, sibling, own)
    high = jnp.where(odd, own, sibling)
    first = position - position % 2

    def chip_part(target):
        return (kept(low, first, target) + kept(high, first + 1, target)).astype(jnp.bfloat16)

    up = send(chip_part(position + 2), axis, [(s, s + 2) for s in range(count - 2)])
    down = send(chip_part(position - 2), axis, [(s, s - 2) for s in range(2, count)])
    total = own + kept(sibling, twin, position)
    return total + up.astype(own.dtype) + down.astype(own.dtype) + far.astype(own.dtype)


def pose_side(pose_rows, pair_rows, state, w_query, score_weight):
    count = pose_rows.shape[0]
    queries = jnp.dot(pose_rows, w_query, preferred_element_type=jnp.float32)
    query_heads = features(queries).reshape(count, H, DH)
    state_heads = state[:DH].reshape(DH, H, DH)
    norm_heads = state[DH].reshape(H, DH)
    numer = jnp.einsum("phd,dhe->phe", query_heads, state_heads, precision=highest)
    denom = jnp.sum(query_heads * norm_heads[None], axis=2)
    attended = numer / denom[:, :, None]
    weight_heads = score_weight.reshape(H, DH)
    scores = jnp.sum(attended * weight_heads[None], axis=(1, 2))
    slots = lax.broadcasted_iota(jnp.int32, (pair_rows.shape[0], count), 1)
    is_better = slots == pair_rows[:, 0:1]
    is_worse = slots == pair_rows[:, 1:2]
    better = jnp.sum(jnp.where(is_better, scores[None, :], 0.0), axis=1)
    worse = jnp.sum(jnp.where(is_worse, scores[None, :], 0.0), axis=1)
    delta = worse - better
    pair_loss = jax.nn.softplus(delta)
    push = jax.nn.sigmoid(delta)
    score_grad = jnp.sum(
        jnp.where(is_worse, push[:, None], 0.0) - jnp.where(is_better, push[:, None], 0.0),
        axis=0,
    )
    attended_grad = score_grad[:, None, None] * weight_heads[None]
    numer_grad = attended_grad / denom[:, :, None]
    denom_grad = -jnp.sum(attended_grad * attended, axis=2) / denom
    outer_grad = jnp.einsum("phd,phe->dhe", query_heads, numer_grad, precision=highest).reshape(
        DH, H * DH
    )
    norm_grad = jnp.sum(query_heads * denom_grad[:, :, None], axis=0).reshape(H * DH)
    pose_state = jnp.concatenate([outer_grad, norm_grad[None, :]], axis=0)
    feat_grad = (
        jnp.einsum("phe,dhe->phd", numer_grad, state_heads, precision=highest)
        + denom_grad[:, :, None] * norm_heads[None]
    )
    query_grad = (feat_grad.reshape(count, H * DH) * slope(queries)).astype(jnp.bfloat16)
    pose_grad = lax.dot_general(
        query_grad, w_query, (((1,), (1,)), ((), ())), preferred_element_type=jnp.float32
    )
    return (pair_loss, pose_grad.astype(jnp.bfloat16), pose_state)


def pose_kernel(pose_ref, pair_ref, state_ref, query_ref, weight_ref, loss_ref, grad_ref, back_ref, feat_ref):
    count, width = pose_ref.shape
    lanes = 2 * DH
    queries = jnp.dot(pose_ref[...], query_ref[...], preferred_element_type=jnp.float32)
    query_feat = features(queries)
    norm = state_ref[DH : DH + 1, :]
    weight = weight_ref[...]
    head_row = lax.broadcasted_iota(jnp.int32, (lanes, lanes), 0) // DH
    head_col = lax.broadcasted_iota(jnp.int32, (lanes, lanes), 1) // DH
    same = head_row == head_col
    ones = same.astype(jnp.float32)
    blocks, numers, denoms = [], [], []
    scores = jnp.zeros((count, 1), jnp.float32)
    for g in range(width // lanes):
        cols = slice(g * lanes, (g + 1) * lanes)
        part = state_ref[0:DH, cols]
        block = jnp.where(same, jnp.concatenate([part, part], axis=0), 0.0)
        feat = query_feat[:, cols]
        numer = jnp.dot(feat, block, precision=highest, preferred_element_type=jnp.float32)
        denom = jnp.dot(
            feat * norm[:, cols], ones, precision=highest, preferred_element_type=jnp.float32
        )
        attended = numer / denom
        scores = scores + jnp.sum(attended * weight[:, cols], axis=1, keepdims=True)
        blocks.append(block)
        numers.append(attended)
        denoms.append(denom)
    slots = lax.broadcasted_iota(jnp.int32, (count, pair_ref.shape[1]), 0)
    is_better = slots == pair_ref[0:1, :]
    is_worse = slots == pair_ref[1:2, :]
    better = jnp.sum(jnp.where(is_better, scores, 0.0), axis=0, keepdims=True)
    worse = jnp.sum(jnp.where(is_worse, scores, 0.0), axis=0, keepdims=True)
    delta = worse - better
    loss_ref[...] = jnp.maximum(delta, 0.0) + jnp.log1p(jnp.exp(-jnp.abs(delta)))
    push = 1.0 / (1.0 + jnp.exp(-delta))
    score_grad = jnp.sum(
        jnp.where(is_worse, push, 0.0) - jnp.where(is_better, push, 0.0), axis=1, keepdims=True
    )
    low = lax.broadcasted_iota(jnp.int32, (DH, lanes), 1) < DH
    for g in range(width // lanes):
        cols = slice(g * lanes, (g + 1) * lanes)
        feat = query_feat[:, cols]
        attended_grad = score_grad * weight[:, cols]
        numer_grad = attended_grad / denoms[g]
        denom_grad = -jnp.dot(
            attended_grad * numers[g], ones, precision=highest, preferred_element_type=jnp.float32
        ) / denoms[g]
        outer = jnp.dot(feat.T, numer_grad, precision=highest, preferred_element_type=jnp.float32)
        back_ref[0:DH, cols] = jnp.where(low, outer[:DH], outer[DH:])
        back_ref[DH : DH + 1, cols] = jnp.sum(feat * denom_grad, axis=0, keepdims=True)
        feat_grad = lax.dot_general(
            numer_grad,
            blocks[g],
            (((1,), (1,)), ((), ())),
            precision=highest,
            preferred_element_type=jnp.float32,
        ) + denom_grad * norm[:, cols]
        feat_ref[:, cols] = (feat_grad * slope(queries[:, cols])).astype(feat_ref.dtype)
    grad = lax.dot_general(
        feat_ref[...], query_ref[...], (((1,), (1,)), ((), ())), preferred_element_type=jnp.float32
    )
    grad_ref[...] = grad.astype(grad_ref.dtype)


def pose_fused(pose_rows, pair_rows, state, w_query, score_weight, interpret=False):
    count, width = pose_rows.shape
    pairs_t = pair_rows.T
    loss, grad, back = pl.pallas_call(
        pose_kernel,
        out_shape=(
            jax.ShapeDtypeStruct((1, pair_rows.shape[0]), jnp.float32),
            jax.ShapeDtypeStruct((count, width), jnp.bfloat16),
            jax.ShapeDtypeStruct(state.shape, jnp.float32),
        ),
        scratch_shapes=[pltpu.VMEM((count, width), jnp.bfloat16)],
        interpret=interpret,
    )(pose_rows, pairs_t, state, w_query, score_weight.reshape(1, width))
    return (loss.reshape(pair_rows.shape[0]), grad, back)


def back_kernel(feat_ref, val_ref, keys_ref, grad_ref, full_ref, out_ref, both_ref):
    width = feat_ref.shape[1]
    lanes = 2 * DH
    head_row = lax.broadcasted_iota(jnp.int32, (lanes, lanes), 0) // DH
    head_col = lax.broadcasted_iota(jnp.int32, (lanes, lanes), 1) // DH
    same = head_row == head_col
    for g in range(width // lanes):
        cols = slice(g * lanes, (g + 1) * lanes)
        part = grad_ref[0:DH, cols].astype(jnp.float32)
        block = jnp.where(same, jnp.concatenate([part, part], axis=0), 0.0).astype(jnp.bfloat16)
        feat_grad = lax.dot_general(
            val_ref[:, cols], block, (((1,), (1,)), ((), ())), preferred_element_type=jnp.float32
        ) + grad_ref[DH : DH + 1, cols].astype(jnp.float32)
        both_ref[:, cols] = (feat_grad * slope(keys_ref[:, cols])).astype(both_ref.dtype)
        value_grad = jnp.dot(feat_ref[:, cols], block, preferred_element_type=jnp.float32)
        both_ref[:, width + g * lanes : width + (g + 1) * lanes] = value_grad.astype(both_ref.dtype)
    total = lax.dot_general(
        both_ref[...], full_ref[...], (((1,), (1,)), ((), ())), preferred_element_type=jnp.float32
    )
    out_ref[...] = total.astype(out_ref.dtype)


def back_fused(key_feat, val_round, keys, state_grad, full_both, interpret=False):
    rows, width = key_feat.shape
    return pl.pallas_call(
        back_kernel,
        out_shape=jax.ShapeDtypeStruct((rows, width), jnp.bfloat16),
        scratch_shapes=[pltpu.VMEM((rows, 2 * width), jnp.bfloat16)],
        interpret=interpret,
    )(key_feat, val_round, keys, state_grad, full_both)


def gather_rows(shard):
    count = lax.axis_size("blk")
    if count != 8:
        return lax.all_gather(shard, "blk", axis=0, tiled=True), None
    position = lax.axis_index("blk")
    rows = shard.shape[0]
    odd = position % 2
    first = jnp.where(odd == 1, 4, 2)
    second = 6 - first
    swap = [(s, s ^ 1) for s in range(count)]
    twin_own = lax.ppermute(shard, "blk", swap)
    early = lax.ppermute(shard, "blk", [(s, s ^ (4 if s % 2 else 2)) for s in range(count)])
    twin_early = lax.ppermute(early, "blk", swap)
    late = lax.ppermute(
        jnp.stack([shard, early]), "blk", [(s, s ^ (2 if s % 2 else 4)) for s in range(count)]
    )
    twin_late = lax.ppermute(late, "blk", swap)
    twin = position ^ 1
    sources = [
        ([shard, twin_own, early, twin_early], [position, twin, position ^ first, twin ^ second]),
        ([late[0], late[1]], [position ^ second, position ^ 6]),
    ]
    full = jnp.zeros((count,) + shard.shape, shard.dtype)
    for pieces, where in sources:
        for k, at in enumerate(where):
            full = lax.dynamic_update_slice(full, pieces[k][None], (at, 0, 0))
    return full, (twin_late, [twin ^ first, twin ^ 6])


def shards(receptor, poses, pairs, block_complex, w_key, w_value, w_query, score_weight):
    rows = receptor.shape[0]
    width = receptor.shape[1]
    full_both, rest = gather_rows(jnp.concatenate([w_key, w_value], axis=1))
    if rest is None:
        both = jnp.dot(receptor, full_both, preferred_element_type=jnp.float32)
    else:
        pieces, where = rest
        part = full_both.shape[1]
        both = jnp.dot(
            receptor, full_both.reshape(-1, full_both.shape[2]), preferred_element_type=jnp.float32
        )
        picked = jnp.concatenate(
            [lax.dynamic_slice_in_dim(receptor, at * part, part, axis=1) for at in where], axis=1
        )
        both = both + jnp.dot(
            picked, pieces.reshape(-1, pieces.shape[2]), preferred_element_type=jnp.float32
        )
        for k, at in enumerate(where):
            full_both = lax.dynamic_update_slice(full_both, pieces[k][None], (at, 0, 0))
        full_both = full_both.reshape(-1, full_both.shape[2])
    keys = both[:, :width]
    values = both[:, width:]
    key_feat = features(keys).astype(jnp.bfloat16)
    val_round = values.astype(jnp.bfloat16)
    state = complex_sum(local_state(key_feat, val_round), block_complex)
    pair_loss, pose_grad, pose_state = pose_fused(poses, pairs, state, w_query, score_weight)
    state_grad = complex_sum(pose_state, block_complex).astype(jnp.bfloat16)
    total = back_fused(key_feat, val_round, keys, state_grad, full_both)
    return (pair_loss, pose_grad, total)


def solution(mesh):
    placed = (
        P(("sec", "blk"), None),
        P(("sec", "blk"), None),
        P(("sec", "blk"), None),
        P(),
        P("blk", None),
        P("blk", None),
        P(),
        P(),
    )
    return jax.shard_map(
        shards,
        mesh=mesh,
        in_specs=placed,
        out_specs=(P(("sec", "blk")), P(("sec", "blk"), None), P(("sec", "blk"), None)),
        check_vma=False,
    )
```

```python
import jax
import jax.numpy as jnp
from jax import lax
from jax.sharding import PartitionSpec as P
from jax.experimental import pallas as pl
from jax.experimental.pallas import tpu as pltpu

H = 16
DH = 64
MOSTB = 4


highest = lax.Precision.HIGHEST


def from_behind(value, axis, steps):
    count = lax.axis_size(axis)
    initial, last = (max(0, -steps), min(count, count - steps))
    return lax.ppermute(value, axis, [(source, source + steps) for source in range(initial, last)])


def features(values):
    return jnp.where(values > 0, values + 1.0, jnp.exp(jnp.minimum(values, 0.0)))


def slope(values):
    return jnp.where(values > 0, jnp.ones_like(values), jnp.exp(jnp.minimum(values, 0.0)))


def local_state(key_feat, val_round):
    rows = key_feat.shape[0]
    key_heads = key_feat.reshape(rows, H, DH)
    val_heads = val_round.reshape(rows, H, DH)
    outer = jnp.einsum(
        "thd,the->dhe", key_heads, val_heads, preferred_element_type=jnp.float32
    ).reshape(DH, H * DH)
    norm_row = jnp.sum(key_feat, axis=0, dtype=jnp.float32)
    return jnp.concatenate([outer, norm_row[None, :]], axis=0)


def complex_total(own, block_complex):
    position = lax.axis_index(("sec", "blk"))
    blocks = block_complex.shape[0]
    mine = jnp.take(block_complex, position)
    total = own
    for reach in range(1, MOSTB):
        lower = from_behind(own.astype(jnp.bfloat16), ("sec", "blk"), reach).astype(own.dtype)
        upper = from_behind(own.astype(jnp.bfloat16), ("sec", "blk"), -reach).astype(own.dtype)
        below = jnp.take(block_complex, jnp.maximum(position - reach, 0))
        above = jnp.take(block_complex, jnp.minimum(position + reach, blocks - 1))
        take_lower = jnp.logical_and(position - reach >= 0, below == mine)
        take_upper = jnp.logical_and(position + reach < blocks, above == mine)
        total = total + jnp.where(take_lower, lower, 0.0) + jnp.where(take_upper, upper, 0.0)
    return total


def send(value, axis, pairs):
    return lax.ppermute(value, axis, pairs)


def complex_sum(own, block_complex):
    axis = ("sec", "blk")
    count = lax.axis_size(axis)
    position = lax.axis_index(axis)
    last = block_complex.shape[0] - 1

    def complex_of(block):
        return jnp.take(block_complex, jnp.clip(block, 0, last))

    def kept(value, block, target):
        inside = jnp.logical_and(target >= 0, target <= last)
        return jnp.where(jnp.logical_and(inside, complex_of(block) == complex_of(target)), value, 0.0)

    narrow = own.astype(jnp.bfloat16)
    twin = position ^ 1
    sibling = send(narrow, axis, [(s, s ^ 1) for s in range(count)]).astype(own.dtype)
    odd = position % 2 == 1
    far_target = jnp.where(odd, position + 3, position - 3)
    far = send(
        kept(own, position, far_target).astype(jnp.bfloat16),
        axis,
        [(s, s + 3) for s in range(1, count - 3, 2)] + [(s, s - 3) for s in range(4, count, 2)],
    )
    low = jnp.where(odd, sibling, own)
    high = jnp.where(odd, own, sibling)
    first = position - position % 2

    def chip_part(target):
        return (kept(low, first, target) + kept(high, first + 1, target)).astype(jnp.bfloat16)

    up = send(chip_part(position + 2), axis, [(s, s + 2) for s in range(count - 2)])
    down = send(chip_part(position - 2), axis, [(s, s - 2) for s in range(2, count)])
    total = own + kept(sibling, twin, position)
    return total + up.astype(own.dtype) + down.astype(own.dtype) + far.astype(own.dtype)


def pose_side(pose_rows, pair_rows, state, w_query, score_weight):
    count = pose_rows.shape[0]
    queries = jnp.dot(pose_rows, w_query, preferred_element_type=jnp.float32)
    query_heads = features(queries).reshape(count, H, DH)
    state_heads = state[:DH].reshape(DH, H, DH)
    norm_heads = state[DH].reshape(H, DH)
    numer = jnp.einsum("phd,dhe->phe", query_heads, state_heads, precision=highest)
    denom = jnp.sum(query_heads * norm_heads[None], axis=2)
    attended = numer / denom[:, :, None]
    weight_heads = score_weight.reshape(H, DH)
    scores = jnp.sum(attended * weight_heads[None], axis=(1, 2))
    slots = lax.broadcasted_iota(jnp.int32, (pair_rows.shape[0], count), 1)
    is_better = slots == pair_rows[:, 0:1]
    is_worse = slots == pair_rows[:, 1:2]
    better = jnp.sum(jnp.where(is_better, scores[None, :], 0.0), axis=1)
    worse = jnp.sum(jnp.where(is_worse, scores[None, :], 0.0), axis=1)
    delta = worse - better
    pair_loss = jax.nn.softplus(delta)
    push = jax.nn.sigmoid(delta)
    score_grad = jnp.sum(
        jnp.where(is_worse, push[:, None], 0.0) - jnp.where(is_better, push[:, None], 0.0),
        axis=0,
    )
    attended_grad = score_grad[:, None, None] * weight_heads[None]
    numer_grad = attended_grad / denom[:, :, None]
    denom_grad = -jnp.sum(attended_grad * attended, axis=2) / denom
    outer_grad = jnp.einsum("phd,phe->dhe", query_heads, numer_grad, precision=highest).reshape(
        DH, H * DH
    )
    norm_grad = jnp.sum(query_heads * denom_grad[:, :, None], axis=0).reshape(H * DH)
    pose_state = jnp.concatenate([outer_grad, norm_grad[None, :]], axis=0)
    feat_grad = (
        jnp.einsum("phe,dhe->phd", numer_grad, state_heads, precision=highest)
        + denom_grad[:, :, None] * norm_heads[None]
    )
    query_grad = (feat_grad.reshape(count, H * DH) * slope(queries)).astype(jnp.bfloat16)
    pose_grad = lax.dot_general(
        query_grad, w_query, (((1,), (1,)), ((), ())), preferred_element_type=jnp.float32
    )
    return (pair_loss, pose_grad.astype(jnp.bfloat16), pose_state)


def pose_kernel(pose_ref, pair_ref, state_ref, query_ref, weight_ref, loss_ref, grad_ref, back_ref, feat_ref):
    count, width = pose_ref.shape
    lanes = 2 * DH
    queries = jnp.dot(pose_ref[...], query_ref[...], preferred_element_type=jnp.float32)
    query_feat = features(queries)
    norm = state_ref[DH : DH + 1, :]
    weight = weight_ref[...]
    head_row = lax.broadcasted_iota(jnp.int32, (lanes, lanes), 0) // DH
    head_col = lax.broadcasted_iota(jnp.int32, (lanes, lanes), 1) // DH
    same = head_row == head_col
    ones = same.astype(jnp.float32)
    blocks, numers, denoms = [], [], []
    scores = jnp.zeros((count, 1), jnp.float32)
    for g in range(width // lanes):
        cols = slice(g * lanes, (g + 1) * lanes)
        part = state_ref[0:DH, cols]
        block = jnp.where(same, jnp.concatenate([part, part], axis=0), 0.0)
        feat = query_feat[:, cols]
        numer = jnp.dot(feat, block, precision=highest, preferred_element_type=jnp.float32)
        denom = jnp.dot(
            feat * norm[:, cols], ones, precision=highest, preferred_element_type=jnp.float32
        )
        attended = numer / denom
        scores = scores + jnp.sum(attended * weight[:, cols], axis=1, keepdims=True)
        blocks.append(block)
        numers.append(attended)
        denoms.append(denom)
    slots = lax.broadcasted_iota(jnp.int32, (count, pair_ref.shape[1]), 0)
    is_better = slots == pair_ref[0:1, :]
    is_worse = slots == pair_ref[1:2, :]
    better = jnp.sum(jnp.where(is_better, scores, 0.0), axis=0, keepdims=True)
    worse = jnp.sum(jnp.where(is_worse, scores, 0.0), axis=0, keepdims=True)
    delta = worse - better
    loss_ref[...] = jnp.maximum(delta, 0.0) + jnp.log1p(jnp.exp(-jnp.abs(delta)))
    push = 1.0 / (1.0 + jnp.exp(-delta))
    score_grad = jnp.sum(
        jnp.where(is_worse, push, 0.0) - jnp.where(is_better, push, 0.0), axis=1, keepdims=True
    )
    low = lax.broadcasted_iota(jnp.int32, (DH, lanes), 1) < DH
    for g in range(width // lanes):
        cols = slice(g * lanes, (g + 1) * lanes)
        feat = query_feat[:, cols]
        attended_grad = score_grad * weight[:, cols]
        numer_grad = attended_grad / denoms[g]
        denom_grad = -jnp.dot(
            attended_grad * numers[g], ones, precision=highest, preferred_element_type=jnp.float32
        ) / denoms[g]
        outer = jnp.dot(feat.T, numer_grad, precision=highest, preferred_element_type=jnp.float32)
        back_ref[0:DH, cols] = jnp.where(low, outer[:DH], outer[DH:])
        back_ref[DH : DH + 1, cols] = jnp.sum(feat * denom_grad, axis=0, keepdims=True)
        feat_grad = lax.dot_general(
            numer_grad,
            blocks[g],
            (((1,), (1,)), ((), ())),
            precision=highest,
            preferred_element_type=jnp.float32,
        ) + denom_grad * norm[:, cols]
        feat_ref[:, cols] = (feat_grad * slope(queries[:, cols])).astype(feat_ref.dtype)
    grad = lax.dot_general(
        feat_ref[...], query_ref[...], (((1,), (1,)), ((), ())), preferred_element_type=jnp.float32
    )
    grad_ref[...] = grad.astype(grad_ref.dtype)


def pose_fused(pose_rows, pair_rows, state, w_query, score_weight, interpret=False):
    count, width = pose_rows.shape
    pairs_t = pair_rows.T
    loss, grad, back = pl.pallas_call(
        pose_kernel,
        out_shape=(
            jax.ShapeDtypeStruct((1, pair_rows.shape[0]), jnp.float32),
            jax.ShapeDtypeStruct((count, width), jnp.bfloat16),
            jax.ShapeDtypeStruct(state.shape, jnp.float32),
        ),
        scratch_shapes=[pltpu.VMEM((count, width), jnp.bfloat16)],
        interpret=interpret,
    )(pose_rows, pairs_t, state, w_query, score_weight.reshape(1, width))
    return (loss.reshape(pair_rows.shape[0]), grad, back)


def back_kernel(feat_ref, val_ref, keys_ref, grad_ref, full_ref, out_ref, both_ref):
    width = feat_ref.shape[1]
    lanes = 2 * DH
    head_row = lax.broadcasted_iota(jnp.int32, (lanes, lanes), 0) // DH
    head_col = lax.broadcasted_iota(jnp.int32, (lanes, lanes), 1) // DH
    same = head_row == head_col
    for g in range(width // lanes):
        cols = slice(g * lanes, (g + 1) * lanes)
        part = grad_ref[0:DH, cols].astype(jnp.float32)
        block = jnp.where(same, jnp.concatenate([part, part], axis=0), 0.0).astype(jnp.bfloat16)
        feat_grad = lax.dot_general(
            val_ref[:, cols], block, (((1,), (1,)), ((), ())), preferred_element_type=jnp.float32
        ) + grad_ref[DH : DH + 1, cols].astype(jnp.float32)
        both_ref[:, cols] = (feat_grad * slope(keys_ref[:, cols])).astype(both_ref.dtype)
        value_grad = jnp.dot(feat_ref[:, cols], block, preferred_element_type=jnp.float32)
        both_ref[:, width + g * lanes : width + (g + 1) * lanes] = value_grad.astype(both_ref.dtype)
    total = jnp.dot(both_ref[...], full_ref[...], preferred_element_type=jnp.float32)
    out_ref[...] = total.astype(out_ref.dtype)


def back_fused(key_feat, val_round, keys, state_grad, full_both, interpret=False):
    rows, width = key_feat.shape
    return pl.pallas_call(
        back_kernel,
        out_shape=jax.ShapeDtypeStruct((rows, width), jnp.bfloat16),
        scratch_shapes=[pltpu.VMEM((rows, 2 * width), jnp.bfloat16)],
        interpret=interpret,
    )(key_feat, val_round, keys, state_grad, full_both.T)


def gather_rows(shard):
    count = lax.axis_size("blk")
    if count != 8:
        return lax.all_gather(shard, "blk", axis=0, tiled=True), None
    position = lax.axis_index("blk")
    rows = shard.shape[0]
    odd = position % 2
    first = jnp.where(odd == 1, 4, 2)
    second = 6 - first
    swap = [(s, s ^ 1) for s in range(count)]
    twin_own = lax.ppermute(shard, "blk", swap)
    early = lax.ppermute(shard, "blk", [(s, s ^ (4 if s % 2 else 2)) for s in range(count)])
    twin_early = lax.ppermute(early, "blk", swap)
    late = lax.ppermute(
        jnp.stack([shard, early]), "blk", [(s, s ^ (2 if s % 2 else 4)) for s in range(count)]
    )
    twin_late = lax.ppermute(late, "blk", swap)
    twin = position ^ 1
    sources = [
        ([shard, twin_own, early, twin_early], [position, twin, position ^ first, twin ^ second]),
        ([late[0], late[1]], [position ^ second, position ^ 6]),
    ]
    full = jnp.zeros((count,) + shard.shape, shard.dtype)
    for pieces, where in sources:
        for k, at in enumerate(where):
            full = lax.dynamic_update_slice(full, pieces[k][None], (at, 0, 0))
    return full, (twin_late, [twin ^ first, twin ^ 6])


def shards(receptor, poses, pairs, block_complex, w_key, w_value, w_query, score_weight):
    rows = receptor.shape[0]
    width = receptor.shape[1]
    full_both, rest = gather_rows(jnp.concatenate([w_key, w_value], axis=1))
    if rest is None:
        both = jnp.dot(receptor, full_both, preferred_element_type=jnp.float32)
    else:
        pieces, where = rest
        part = full_both.shape[1]
        both = jnp.dot(
            receptor, full_both.reshape(-1, full_both.shape[2]), preferred_element_type=jnp.float32
        )
        picked = jnp.concatenate(
            [lax.dynamic_slice_in_dim(receptor, at * part, part, axis=1) for at in where], axis=1
        )
        both = both + jnp.dot(
            picked, pieces.reshape(-1, pieces.shape[2]), preferred_element_type=jnp.float32
        )
        for k, at in enumerate(where):
            full_both = lax.dynamic_update_slice(full_both, pieces[k][None], (at, 0, 0))
        full_both = full_both.reshape(-1, full_both.shape[2])
    keys = both[:, :width]
    values = both[:, width:]
    key_feat = features(keys).astype(jnp.bfloat16)
    val_round = values.astype(jnp.bfloat16)
    state = complex_sum(local_state(key_feat, val_round), block_complex)
    pair_loss, pose_grad, pose_state = pose_fused(poses, pairs, state, w_query, score_weight)
    state_grad = complex_sum(pose_state, block_complex).astype(jnp.bfloat16)
    total = back_fused(key_feat, val_round, keys, state_grad, full_both)
    return (pair_loss, pose_grad, total)


def solution(mesh):
    placed = (
        P(("sec", "blk"), None),
        P(("sec", "blk"), None),
        P(("sec", "blk"), None),
        P(),
        P("blk", None),
        P("blk", None),
        P(),
        P(),
    )
    return jax.shard_map(
        shards,
        mesh=mesh,
        in_specs=placed,
        out_specs=(P(("sec", "blk")), P(("sec", "blk"), None), P(("sec", "blk"), None)),
        check_vma=False,
    )
```

```python
import jax
import jax.numpy as jnp
from jax import lax
from jax.sharding import PartitionSpec as P
from jax.experimental import pallas as pl
from jax.experimental.pallas import tpu as pltpu

H = 16
DH = 64
MOSTB = 4


highest = lax.Precision.HIGHEST


def from_behind(value, axis, steps):
    count = lax.axis_size(axis)
    initial, last = (max(0, -steps), min(count, count - steps))
    return lax.ppermute(value, axis, [(source, source + steps) for source in range(initial, last)])


def features(values):
    return jnp.where(values > 0, values + 1.0, jnp.exp(jnp.minimum(values, 0.0)))


def slope(values):
    return jnp.where(values > 0, jnp.ones_like(values), jnp.exp(jnp.minimum(values, 0.0)))


def local_state(key_feat, val_round):
    rows = key_feat.shape[0]
    key_heads = key_feat.reshape(rows, H, DH)
    val_heads = val_round.reshape(rows, H, DH)
    outer = jnp.einsum(
        "thd,the->dhe", key_heads, val_heads, preferred_element_type=jnp.float32
    ).reshape(DH, H * DH)
    norm_row = jnp.sum(key_feat, axis=0, dtype=jnp.float32)
    return jnp.concatenate([outer, norm_row[None, :]], axis=0)


def complex_total(own, block_complex):
    position = lax.axis_index(("sec", "blk"))
    blocks = block_complex.shape[0]
    mine = jnp.take(block_complex, position)
    total = own
    for reach in range(1, MOSTB):
        lower = from_behind(own.astype(jnp.bfloat16), ("sec", "blk"), reach).astype(own.dtype)
        upper = from_behind(own.astype(jnp.bfloat16), ("sec", "blk"), -reach).astype(own.dtype)
        below = jnp.take(block_complex, jnp.maximum(position - reach, 0))
        above = jnp.take(block_complex, jnp.minimum(position + reach, blocks - 1))
        take_lower = jnp.logical_and(position - reach >= 0, below == mine)
        take_upper = jnp.logical_and(position + reach < blocks, above == mine)
        total = total + jnp.where(take_lower, lower, 0.0) + jnp.where(take_upper, upper, 0.0)
    return total


def send(value, axis, pairs):
    return lax.ppermute(value, axis, pairs)


def complex_sum(own, block_complex):
    axis = ("sec", "blk")
    count = lax.axis_size(axis)
    position = lax.axis_index(axis)
    last = block_complex.shape[0] - 1

    def complex_of(block):
        return jnp.take(block_complex, jnp.clip(block, 0, last))

    def kept(value, block, target):
        inside = jnp.logical_and(target >= 0, target <= last)
        return jnp.where(jnp.logical_and(inside, complex_of(block) == complex_of(target)), value, 0.0)

    narrow = own.astype(jnp.bfloat16)
    twin = position ^ 1
    sibling = send(narrow, axis, [(s, s ^ 1) for s in range(count)]).astype(own.dtype)
    odd = position % 2 == 1
    far_target = jnp.where(odd, position + 3, position - 3)
    far = send(
        kept(own, position, far_target).astype(jnp.bfloat16),
        axis,
        [(s, s + 3) for s in range(1, count - 3, 2)] + [(s, s - 3) for s in range(4, count, 2)],
    )
    low = jnp.where(odd, sibling, own)
    high = jnp.where(odd, own, sibling)
    first = position - position % 2

    def chip_part(target):
        return (kept(low, first, target) + kept(high, first + 1, target)).astype(jnp.bfloat16)

    up = send(chip_part(position + 2), axis, [(s, s + 2) for s in range(count - 2)])
    down = send(chip_part(position - 2), axis, [(s, s - 2) for s in range(2, count)])
    alike = jnp.logical_and(twin <= last, complex_of(twin) == complex_of(position))
    return own, sibling, alike.astype(own.dtype).reshape(1, 1), up, down, far


def add_terms(own_ref, twin_ref, alike_ref, up_ref, down_ref, far_ref):
    total = own_ref[...] + twin_ref[...].astype(jnp.float32) * alike_ref[...]
    for ref in (up_ref, down_ref, far_ref):
        total = total + ref[...].astype(jnp.float32)
    return total


def pose_side(pose_rows, pair_rows, state, w_query, score_weight):
    count = pose_rows.shape[0]
    queries = jnp.dot(pose_rows, w_query, preferred_element_type=jnp.float32)
    query_heads = features(queries).reshape(count, H, DH)
    state_heads = state[:DH].reshape(DH, H, DH)
    norm_heads = state[DH].reshape(H, DH)
    numer = jnp.einsum("phd,dhe->phe", query_heads, state_heads, precision=highest)
    denom = jnp.sum(query_heads * norm_heads[None], axis=2)
    attended = numer / denom[:, :, None]
    weight_heads = score_weight.reshape(H, DH)
    scores = jnp.sum(attended * weight_heads[None], axis=(1, 2))
    slots = lax.broadcasted_iota(jnp.int32, (pair_rows.shape[0], count), 1)
    is_better = slots == pair_rows[:, 0:1]
    is_worse = slots == pair_rows[:, 1:2]
    better = jnp.sum(jnp.where(is_better, scores[None, :], 0.0), axis=1)
    worse = jnp.sum(jnp.where(is_worse, scores[None, :], 0.0), axis=1)
    delta = worse - better
    pair_loss = jax.nn.softplus(delta)
    push = jax.nn.sigmoid(delta)
    score_grad = jnp.sum(
        jnp.where(is_worse, push[:, None], 0.0) - jnp.where(is_better, push[:, None], 0.0),
        axis=0,
    )
    attended_grad = score_grad[:, None, None] * weight_heads[None]
    numer_grad = attended_grad / denom[:, :, None]
    denom_grad = -jnp.sum(attended_grad * attended, axis=2) / denom
    outer_grad = jnp.einsum("phd,phe->dhe", query_heads, numer_grad, precision=highest).reshape(
        DH, H * DH
    )
    norm_grad = jnp.sum(query_heads * denom_grad[:, :, None], axis=0).reshape(H * DH)
    pose_state = jnp.concatenate([outer_grad, norm_grad[None, :]], axis=0)
    feat_grad = (
        jnp.einsum("phe,dhe->phd", numer_grad, state_heads, precision=highest)
        + denom_grad[:, :, None] * norm_heads[None]
    )
    query_grad = (feat_grad.reshape(count, H * DH) * slope(queries)).astype(jnp.bfloat16)
    pose_grad = lax.dot_general(
        query_grad, w_query, (((1,), (1,)), ((), ())), preferred_element_type=jnp.float32
    )
    return (pair_loss, pose_grad.astype(jnp.bfloat16), pose_state)


def pose_kernel(
    pose_ref, pair_ref, *refs
):
    terms = refs[:6]
    query_ref, weight_ref, loss_ref, grad_ref, back_ref, feat_ref, state_ref = refs[6:]
    state_ref[...] = add_terms(*terms)
    count, width = pose_ref.shape
    lanes = 2 * DH
    queries = jnp.dot(pose_ref[...], query_ref[...], preferred_element_type=jnp.float32)
    query_feat = features(queries)
    norm = state_ref[DH : DH + 1, :]
    weight = weight_ref[...]
    head_row = lax.broadcasted_iota(jnp.int32, (lanes, lanes), 0) // DH
    head_col = lax.broadcasted_iota(jnp.int32, (lanes, lanes), 1) // DH
    same = head_row == head_col
    ones = same.astype(jnp.float32)
    blocks, numers, denoms = [], [], []
    scores = jnp.zeros((count, 1), jnp.float32)
    for g in range(width // lanes):
        cols = slice(g * lanes, (g + 1) * lanes)
        part = state_ref[0:DH, cols]
        block = jnp.where(same, jnp.concatenate([part, part], axis=0), 0.0)
        feat = query_feat[:, cols]
        numer = jnp.dot(feat, block, precision=highest, preferred_element_type=jnp.float32)
        denom = jnp.dot(
            feat * norm[:, cols], ones, precision=highest, preferred_element_type=jnp.float32
        )
        attended = numer / denom
        scores = scores + jnp.sum(attended * weight[:, cols], axis=1, keepdims=True)
        blocks.append(block)
        numers.append(attended)
        denoms.append(denom)
    slots = lax.broadcasted_iota(jnp.int32, (count, pair_ref.shape[1]), 0)
    is_better = slots == pair_ref[0:1, :]
    is_worse = slots == pair_ref[1:2, :]
    better = jnp.sum(jnp.where(is_better, scores, 0.0), axis=0, keepdims=True)
    worse = jnp.sum(jnp.where(is_worse, scores, 0.0), axis=0, keepdims=True)
    delta = worse - better
    loss_ref[...] = jnp.maximum(delta, 0.0) + jnp.log1p(jnp.exp(-jnp.abs(delta)))
    push = 1.0 / (1.0 + jnp.exp(-delta))
    score_grad = jnp.sum(
        jnp.where(is_worse, push, 0.0) - jnp.where(is_better, push, 0.0), axis=1, keepdims=True
    )
    low = lax.broadcasted_iota(jnp.int32, (DH, lanes), 1) < DH
    for g in range(width // lanes):
        cols = slice(g * lanes, (g + 1) * lanes)
        feat = query_feat[:, cols]
        attended_grad = score_grad * weight[:, cols]
        numer_grad = attended_grad / denoms[g]
        denom_grad = -jnp.dot(
            attended_grad * numers[g], ones, precision=highest, preferred_element_type=jnp.float32
        ) / denoms[g]
        outer = jnp.dot(feat.T, numer_grad, precision=highest, preferred_element_type=jnp.float32)
        back_ref[0:DH, cols] = jnp.where(low, outer[:DH], outer[DH:])
        back_ref[DH : DH + 1, cols] = jnp.sum(feat * denom_grad, axis=0, keepdims=True)
        feat_grad = lax.dot_general(
            numer_grad,
            blocks[g],
            (((1,), (1,)), ((), ())),
            precision=highest,
            preferred_element_type=jnp.float32,
        ) + denom_grad * norm[:, cols]
        feat_ref[:, cols] = (feat_grad * slope(queries[:, cols])).astype(feat_ref.dtype)
    grad = lax.dot_general(
        feat_ref[...], query_ref[...], (((1,), (1,)), ((), ())), preferred_element_type=jnp.float32
    )
    grad_ref[...] = grad.astype(grad_ref.dtype)


def pose_fused(pose_rows, pair_rows, state, w_query, score_weight, interpret=False):
    count, width = pose_rows.shape
    pairs_t = pair_rows.T
    loss, grad, back = pl.pallas_call(
        pose_kernel,
        out_shape=(
            jax.ShapeDtypeStruct((1, pair_rows.shape[0]), jnp.float32),
            jax.ShapeDtypeStruct((count, width), jnp.bfloat16),
            jax.ShapeDtypeStruct(state[0].shape, jnp.float32),
        ),
        scratch_shapes=[
            pltpu.VMEM((count, width), jnp.bfloat16),
            pltpu.VMEM(state[0].shape, jnp.float32),
        ],
        interpret=interpret,
    )(pose_rows, pairs_t, *state, w_query, score_weight.reshape(1, width))
    return (loss.reshape(pair_rows.shape[0]), grad, back)


def back_kernel(feat_ref, val_ref, keys_ref, *refs):
    terms = refs[:6]
    full_ref, out_ref, both_ref, grad_ref = refs[6:]
    grad_ref[...] = add_terms(*terms).astype(grad_ref.dtype)
    width = feat_ref.shape[1]
    lanes = 2 * DH
    head_row = lax.broadcasted_iota(jnp.int32, (lanes, lanes), 0) // DH
    head_col = lax.broadcasted_iota(jnp.int32, (lanes, lanes), 1) // DH
    same = head_row == head_col
    for g in range(width // lanes):
        cols = slice(g * lanes, (g + 1) * lanes)
        part = grad_ref[0:DH, cols].astype(jnp.float32)
        block = jnp.where(same, jnp.concatenate([part, part], axis=0), 0.0).astype(jnp.bfloat16)
        feat_grad = lax.dot_general(
            val_ref[:, cols], block, (((1,), (1,)), ((), ())), preferred_element_type=jnp.float32
        ) + grad_ref[DH : DH + 1, cols].astype(jnp.float32)
        both_ref[:, cols] = (feat_grad * slope(keys_ref[:, cols])).astype(both_ref.dtype)
        value_grad = jnp.dot(feat_ref[:, cols], block, preferred_element_type=jnp.float32)
        both_ref[:, width + g * lanes : width + (g + 1) * lanes] = value_grad.astype(both_ref.dtype)
    total = lax.dot_general(
        both_ref[...], full_ref[...], (((1,), (1,)), ((), ())), preferred_element_type=jnp.float32
    )
    out_ref[...] = total.astype(out_ref.dtype)


def back_fused(key_feat, val_round, keys, state_grad, full_both, interpret=False):
    rows, width = key_feat.shape
    return pl.pallas_call(
        back_kernel,
        out_shape=jax.ShapeDtypeStruct((rows, width), jnp.bfloat16),
        scratch_shapes=[
            pltpu.VMEM((rows, 2 * width), jnp.bfloat16),
            pltpu.VMEM(state_grad[0].shape, jnp.bfloat16),
        ],
        interpret=interpret,
    )(key_feat, val_round, keys, *state_grad, full_both)


def gather_rows(shard):
    count = lax.axis_size("blk")
    if count != 8:
        return lax.all_gather(shard, "blk", axis=0, tiled=True), None
    position = lax.axis_index("blk")
    rows = shard.shape[0]
    odd = position % 2
    first = jnp.where(odd == 1, 4, 2)
    second = 6 - first
    swap = [(s, s ^ 1) for s in range(count)]
    twin_own = lax.ppermute(shard, "blk", swap)
    early = lax.ppermute(shard, "blk", [(s, s ^ (4 if s % 2 else 2)) for s in range(count)])
    twin_early = lax.ppermute(early, "blk", swap)
    late = lax.ppermute(
        jnp.stack([shard, early]), "blk", [(s, s ^ (2 if s % 2 else 4)) for s in range(count)]
    )
    twin_late = lax.ppermute(late, "blk", swap)
    twin = position ^ 1
    sources = [
        ([shard, twin_own, early, twin_early], [position, twin, position ^ first, twin ^ second]),
        ([late[0], late[1]], [position ^ second, position ^ 6]),
    ]
    full = jnp.zeros((count,) + shard.shape, shard.dtype)
    for pieces, where in sources:
        for k, at in enumerate(where):
            full = lax.dynamic_update_slice(full, pieces[k][None], (at, 0, 0))
    return full, (twin_late, [twin ^ first, twin ^ 6])


def shards(receptor, poses, pairs, block_complex, w_key, w_value, w_query, score_weight):
    rows = receptor.shape[0]
    width = receptor.shape[1]
    full_both, rest = gather_rows(jnp.concatenate([w_key, w_value], axis=1))
    if rest is None:
        both = jnp.dot(receptor, full_both, preferred_element_type=jnp.float32)
    else:
        pieces, where = rest
        part = full_both.shape[1]
        both = jnp.dot(
            receptor, full_both.reshape(-1, full_both.shape[2]), preferred_element_type=jnp.float32
        )
        picked = jnp.concatenate(
            [lax.dynamic_slice_in_dim(receptor, at * part, part, axis=1) for at in where], axis=1
        )
        both = both + jnp.dot(
            picked, pieces.reshape(-1, pieces.shape[2]), preferred_element_type=jnp.float32
        )
        for k, at in enumerate(where):
            full_both = lax.dynamic_update_slice(full_both, pieces[k][None], (at, 0, 0))
        full_both = full_both.reshape(-1, full_both.shape[2])
    keys = both[:, :width]
    values = both[:, width:]
    key_feat = features(keys).astype(jnp.bfloat16)
    val_round = values.astype(jnp.bfloat16)
    state = complex_sum(local_state(key_feat, val_round), block_complex)
    pair_loss, pose_grad, pose_state = pose_fused(poses, pairs, state, w_query, score_weight)
    state_grad = complex_sum(pose_state, block_complex)
    total = back_fused(key_feat, val_round, keys, state_grad, full_both)
    return (pair_loss, pose_grad, total)


def solution(mesh):
    placed = (
        P(("sec", "blk"), None),
        P(("sec", "blk"), None),
        P(("sec", "blk"), None),
        P(),
        P("blk", None),
        P("blk", None),
        P(),
        P(),
    )
    return jax.shard_map(
        shards,
        mesh=mesh,
        in_specs=placed,
        out_specs=(P(("sec", "blk")), P(("sec", "blk"), None), P(("sec", "blk"), None)),
        check_vma=False,
    )
```

```python
import jax
import jax.numpy as jnp
from jax import lax
from jax.sharding import PartitionSpec as P
from jax.experimental import pallas as pl
from jax.experimental.pallas import tpu as pltpu

H = 16
DH = 64
MOSTB = 4


highest = lax.Precision.HIGHEST


def from_behind(value, axis, steps):
    count = lax.axis_size(axis)
    initial, last = (max(0, -steps), min(count, count - steps))
    return lax.ppermute(value, axis, [(source, source + steps) for source in range(initial, last)])


def features(values):
    return jnp.where(values > 0, values + 1.0, jnp.exp(jnp.minimum(values, 0.0)))


def slope(values):
    return jnp.where(values > 0, jnp.ones_like(values), jnp.exp(jnp.minimum(values, 0.0)))


def local_state(key_feat, val_round):
    rows = key_feat.shape[0]
    key_heads = key_feat.reshape(rows, H, DH)
    val_heads = val_round.reshape(rows, H, DH)
    outer = jnp.einsum(
        "thd,the->dhe", key_heads, val_heads, preferred_element_type=jnp.float32
    ).reshape(DH, H * DH)
    norm_row = jnp.sum(key_feat, axis=0, dtype=jnp.float32)
    return jnp.concatenate([outer, norm_row[None, :]], axis=0)


def complex_total(own, block_complex):
    position = lax.axis_index(("sec", "blk"))
    blocks = block_complex.shape[0]
    mine = jnp.take(block_complex, position)
    total = own
    for reach in range(1, MOSTB):
        lower = from_behind(own.astype(jnp.bfloat16), ("sec", "blk"), reach).astype(own.dtype)
        upper = from_behind(own.astype(jnp.bfloat16), ("sec", "blk"), -reach).astype(own.dtype)
        below = jnp.take(block_complex, jnp.maximum(position - reach, 0))
        above = jnp.take(block_complex, jnp.minimum(position + reach, blocks - 1))
        take_lower = jnp.logical_and(position - reach >= 0, below == mine)
        take_upper = jnp.logical_and(position + reach < blocks, above == mine)
        total = total + jnp.where(take_lower, lower, 0.0) + jnp.where(take_upper, upper, 0.0)
    return total


def send(value, axis, pairs):
    return lax.ppermute(value, axis, pairs)


def complex_sum(own, block_complex):
    axis = ("sec", "blk")
    count = lax.axis_size(axis)
    position = lax.axis_index(axis)
    last = block_complex.shape[0] - 1

    def complex_of(block):
        return jnp.take(block_complex, jnp.clip(block, 0, last))

    def kept(value, block, target):
        inside = jnp.logical_and(target >= 0, target <= last)
        return jnp.where(jnp.logical_and(inside, complex_of(block) == complex_of(target)), value, 0.0)

    narrow = own.astype(jnp.bfloat16)
    twin = position ^ 1
    sibling = send(narrow, axis, [(s, s ^ 1) for s in range(count)]).astype(own.dtype)
    odd = position % 2 == 1
    far_target = jnp.where(odd, position + 3, position - 3)
    far = send(
        kept(own, position, far_target).astype(jnp.bfloat16),
        axis,
        [(s, s + 3) for s in range(1, count - 3, 2)] + [(s, s - 3) for s in range(4, count, 2)],
    )
    low = jnp.where(odd, sibling, own)
    high = jnp.where(odd, own, sibling)
    first = position - position % 2

    def chip_part(target):
        return (kept(low, first, target) + kept(high, first + 1, target)).astype(jnp.bfloat16)

    even_chip = (position // 2) % 2 == 0
    pairs_a = [(s, s + 2 if (s // 2) % 2 == 0 else s - 2) for s in range(count)]
    pairs_b = [
        (s, s + 2 if (s // 2) % 2 else s - 2)
        for s in range(count)
        if 0 <= (s + 2 if (s // 2) % 2 else s - 2) < count
    ]
    up = send(
        chip_part(jnp.where(even_chip, position + 2, position - 2)), axis, pairs_a
    )
    down = send(
        chip_part(jnp.where(even_chip, position - 2, position + 2)), axis, pairs_b
    )
    total = own + kept(sibling, twin, position)
    return total + up.astype(own.dtype) + down.astype(own.dtype) + far.astype(own.dtype)


def pose_side(pose_rows, pair_rows, state, w_query, score_weight):
    count = pose_rows.shape[0]
    queries = jnp.dot(pose_rows, w_query, preferred_element_type=jnp.float32)
    query_heads = features(queries).reshape(count, H, DH)
    state_heads = state[:DH].reshape(DH, H, DH)
    norm_heads = state[DH].reshape(H, DH)
    numer = jnp.einsum("phd,dhe->phe", query_heads, state_heads, precision=highest)
    denom = jnp.sum(query_heads * norm_heads[None], axis=2)
    attended = numer / denom[:, :, None]
    weight_heads = score_weight.reshape(H, DH)
    scores = jnp.sum(attended * weight_heads[None], axis=(1, 2))
    slots = lax.broadcasted_iota(jnp.int32, (pair_rows.shape[0], count), 1)
    is_better = slots == pair_rows[:, 0:1]
    is_worse = slots == pair_rows[:, 1:2]
    better = jnp.sum(jnp.where(is_better, scores[None, :], 0.0), axis=1)
    worse = jnp.sum(jnp.where(is_worse, scores[None, :], 0.0), axis=1)
    delta = worse - better
    pair_loss = jax.nn.softplus(delta)
    push = jax.nn.sigmoid(delta)
    score_grad = jnp.sum(
        jnp.where(is_worse, push[:, None], 0.0) - jnp.where(is_better, push[:, None], 0.0),
        axis=0,
    )
    attended_grad = score_grad[:, None, None] * weight_heads[None]
    numer_grad = attended_grad / denom[:, :, None]
    denom_grad = -jnp.sum(attended_grad * attended, axis=2) / denom
    outer_grad = jnp.einsum("phd,phe->dhe", query_heads, numer_grad, precision=highest).reshape(
        DH, H * DH
    )
    norm_grad = jnp.sum(query_heads * denom_grad[:, :, None], axis=0).reshape(H * DH)
    pose_state = jnp.concatenate([outer_grad, norm_grad[None, :]], axis=0)
    feat_grad = (
        jnp.einsum("phe,dhe->phd", numer_grad, state_heads, precision=highest)
        + denom_grad[:, :, None] * norm_heads[None]
    )
    query_grad = (feat_grad.reshape(count, H * DH) * slope(queries)).astype(jnp.bfloat16)
    pose_grad = lax.dot_general(
        query_grad, w_query, (((1,), (1,)), ((), ())), preferred_element_type=jnp.float32
    )
    return (pair_loss, pose_grad.astype(jnp.bfloat16), pose_state)


def pose_kernel(pose_ref, pair_ref, state_ref, query_ref, weight_ref, loss_ref, grad_ref, back_ref, feat_ref):
    count, width = pose_ref.shape
    lanes = 2 * DH
    queries = jnp.dot(pose_ref[...], query_ref[...], preferred_element_type=jnp.float32)
    query_feat = features(queries)
    norm = state_ref[DH : DH + 1, :]
    weight = weight_ref[...]
    head_row = lax.broadcasted_iota(jnp.int32, (lanes, lanes), 0) // DH
    head_col = lax.broadcasted_iota(jnp.int32, (lanes, lanes), 1) // DH
    same = head_row == head_col
    ones = same.astype(jnp.float32)
    blocks, numers, denoms = [], [], []
    scores = jnp.zeros((count, 1), jnp.float32)
    for g in range(width // lanes):
        cols = slice(g * lanes, (g + 1) * lanes)
        part = state_ref[0:DH, cols]
        block = jnp.where(same, jnp.concatenate([part, part], axis=0), 0.0)
        feat = query_feat[:, cols]
        numer = jnp.dot(feat, block, precision=highest, preferred_element_type=jnp.float32)
        denom = jnp.dot(
            feat * norm[:, cols], ones, precision=highest, preferred_element_type=jnp.float32
        )
        attended = numer / denom
        scores = scores + jnp.sum(attended * weight[:, cols], axis=1, keepdims=True)
        blocks.append(block)
        numers.append(attended)
        denoms.append(denom)
    slots = lax.broadcasted_iota(jnp.int32, (count, pair_ref.shape[1]), 0)
    is_better = slots == pair_ref[0:1, :]
    is_worse = slots == pair_ref[1:2, :]
    better = jnp.sum(jnp.where(is_better, scores, 0.0), axis=0, keepdims=True)
    worse = jnp.sum(jnp.where(is_worse, scores, 0.0), axis=0, keepdims=True)
    delta = worse - better
    loss_ref[...] = jnp.maximum(delta, 0.0) + jnp.log1p(jnp.exp(-jnp.abs(delta)))
    push = 1.0 / (1.0 + jnp.exp(-delta))
    score_grad = jnp.sum(
        jnp.where(is_worse, push, 0.0) - jnp.where(is_better, push, 0.0), axis=1, keepdims=True
    )
    low = lax.broadcasted_iota(jnp.int32, (DH, lanes), 1) < DH
    for g in range(width // lanes):
        cols = slice(g * lanes, (g + 1) * lanes)
        feat = query_feat[:, cols]
        attended_grad = score_grad * weight[:, cols]
        numer_grad = attended_grad / denoms[g]
        denom_grad = -jnp.dot(
            attended_grad * numers[g], ones, precision=highest, preferred_element_type=jnp.float32
        ) / denoms[g]
        outer = jnp.dot(feat.T, numer_grad, precision=highest, preferred_element_type=jnp.float32)
        back_ref[0:DH, cols] = jnp.where(low, outer[:DH], outer[DH:])
        back_ref[DH : DH + 1, cols] = jnp.sum(feat * denom_grad, axis=0, keepdims=True)
        feat_grad = lax.dot_general(
            numer_grad,
            blocks[g],
            (((1,), (1,)), ((), ())),
            precision=highest,
            preferred_element_type=jnp.float32,
        ) + denom_grad * norm[:, cols]
        feat_ref[:, cols] = (feat_grad * slope(queries[:, cols])).astype(feat_ref.dtype)
    grad = lax.dot_general(
        feat_ref[...], query_ref[...], (((1,), (1,)), ((), ())), preferred_element_type=jnp.float32
    )
    grad_ref[...] = grad.astype(grad_ref.dtype)


def pose_fused(pose_rows, pair_rows, state, w_query, score_weight, interpret=False):
    count, width = pose_rows.shape
    pairs_t = pair_rows.T
    loss, grad, back = pl.pallas_call(
        pose_kernel,
        out_shape=(
            jax.ShapeDtypeStruct((1, pair_rows.shape[0]), jnp.float32),
            jax.ShapeDtypeStruct((count, width), jnp.bfloat16),
            jax.ShapeDtypeStruct(state.shape, jnp.float32),
        ),
        scratch_shapes=[pltpu.VMEM((count, width), jnp.bfloat16)],
        interpret=interpret,
    )(pose_rows, pairs_t, state, w_query, score_weight.reshape(1, width))
    return (loss.reshape(pair_rows.shape[0]), grad, back)


def back_kernel(feat_ref, val_ref, keys_ref, grad_ref, full_ref, out_ref, both_ref):
    width = feat_ref.shape[1]
    lanes = 2 * DH
    head_row = lax.broadcasted_iota(jnp.int32, (lanes, lanes), 0) // DH
    head_col = lax.broadcasted_iota(jnp.int32, (lanes, lanes), 1) // DH
    same = head_row == head_col
    for g in range(width // lanes):
        cols = slice(g * lanes, (g + 1) * lanes)
        part = grad_ref[0:DH, cols].astype(jnp.float32)
        block = jnp.where(same, jnp.concatenate([part, part], axis=0), 0.0).astype(jnp.bfloat16)
        feat_grad = lax.dot_general(
            val_ref[:, cols], block, (((1,), (1,)), ((), ())), preferred_element_type=jnp.float32
        ) + grad_ref[DH : DH + 1, cols].astype(jnp.float32)
        both_ref[:, cols] = (feat_grad * slope(keys_ref[:, cols])).astype(both_ref.dtype)
        value_grad = jnp.dot(feat_ref[:, cols], block, preferred_element_type=jnp.float32)
        both_ref[:, width + g * lanes : width + (g + 1) * lanes] = value_grad.astype(both_ref.dtype)
    total = lax.dot_general(
        both_ref[...], full_ref[...], (((1,), (1,)), ((), ())), preferred_element_type=jnp.float32
    )
    out_ref[...] = total.astype(out_ref.dtype)


def back_fused(key_feat, val_round, keys, state_grad, full_both, interpret=False):
    rows, width = key_feat.shape
    return pl.pallas_call(
        back_kernel,
        out_shape=jax.ShapeDtypeStruct((rows, width), jnp.bfloat16),
        scratch_shapes=[pltpu.VMEM((rows, 2 * width), jnp.bfloat16)],
        interpret=interpret,
    )(key_feat, val_round, keys, state_grad, full_both)


def gather_rows(shard):
    count = lax.axis_size("blk")
    if count != 8:
        return lax.all_gather(shard, "blk", axis=0, tiled=True), None
    position = lax.axis_index("blk")
    rows = shard.shape[0]
    odd = position % 2
    first = jnp.where(odd == 1, 4, 2)
    second = 6 - first
    swap = [(s, s ^ 1) for s in range(count)]
    twin_own = lax.ppermute(shard, "blk", swap)
    early = lax.ppermute(shard, "blk", [(s, s ^ (4 if s % 2 else 2)) for s in range(count)])
    twin_early = lax.ppermute(early, "blk", swap)
    late = lax.ppermute(
        jnp.stack([shard, early]), "blk", [(s, s ^ (2 if s % 2 else 4)) for s in range(count)]
    )
    twin_late = lax.ppermute(late, "blk", swap)
    twin = position ^ 1
    sources = [
        ([shard, twin_own, early, twin_early], [position, twin, position ^ first, twin ^ second]),
        ([late[0], late[1]], [position ^ second, position ^ 6]),
    ]
    full = jnp.zeros((count,) + shard.shape, shard.dtype)
    for pieces, where in sources:
        for k, at in enumerate(where):
            full = lax.dynamic_update_slice(full, pieces[k][None], (at, 0, 0))
    return full, (twin_late, [twin ^ first, twin ^ 6])


def shards(receptor, poses, pairs, block_complex, w_key, w_value, w_query, score_weight):
    rows = receptor.shape[0]
    width = receptor.shape[1]
    full_both, rest = gather_rows(jnp.concatenate([w_key, w_value], axis=1))
    if rest is None:
        both = jnp.dot(receptor, full_both, preferred_element_type=jnp.float32)
    else:
        pieces, where = rest
        part = full_both.shape[1]
        both = jnp.dot(
            receptor, full_both.reshape(-1, full_both.shape[2]), preferred_element_type=jnp.float32
        )
        picked = jnp.concatenate(
            [lax.dynamic_slice_in_dim(receptor, at * part, part, axis=1) for at in where], axis=1
        )
        both = both + jnp.dot(
            picked, pieces.reshape(-1, pieces.shape[2]), preferred_element_type=jnp.float32
        )
        for k, at in enumerate(where):
            full_both = lax.dynamic_update_slice(full_both, pieces[k][None], (at, 0, 0))
        full_both = full_both.reshape(-1, full_both.shape[2])
    keys = both[:, :width]
    values = both[:, width:]
    key_feat = features(keys).astype(jnp.bfloat16)
    val_round = values.astype(jnp.bfloat16)
    state = complex_sum(local_state(key_feat, val_round), block_complex)
    pair_loss, pose_grad, pose_state = pose_fused(poses, pairs, state, w_query, score_weight)
    state_grad = complex_sum(pose_state, block_complex).astype(jnp.bfloat16)
    total = back_fused(key_feat, val_round, keys, state_grad, full_both)
    return (pair_loss, pose_grad, total)


def solution(mesh):
    placed = (
        P(("sec", "blk"), None),
        P(("sec", "blk"), None),
        P(("sec", "blk"), None),
        P(),
        P("blk", None),
        P("blk", None),
        P(),
        P(),
    )
    return jax.shard_map(
        shards,
        mesh=mesh,
        in_specs=placed,
        out_specs=(P(("sec", "blk")), P(("sec", "blk"), None), P(("sec", "blk"), None)),
        check_vma=False,
    )
```

```python
import jax
import jax.numpy as jnp
from jax import lax
from jax.sharding import PartitionSpec as P
from jax.experimental import pallas as pl
from jax.experimental.pallas import tpu as pltpu

H = 16
DH = 64
MOSTB = 4


highest = lax.Precision.HIGHEST


def from_behind(value, axis, steps):
    count = lax.axis_size(axis)
    initial, last = (max(0, -steps), min(count, count - steps))
    return lax.ppermute(value, axis, [(source, source + steps) for source in range(initial, last)])


def features(values):
    return jnp.where(values > 0, values + 1.0, jnp.exp(jnp.minimum(values, 0.0)))


def slope(values):
    return jnp.where(values > 0, jnp.ones_like(values), jnp.exp(jnp.minimum(values, 0.0)))


def local_state(key_feat, val_round):
    rows = key_feat.shape[0]
    key_heads = key_feat.reshape(rows, H, DH)
    val_heads = val_round.reshape(rows, H, DH)
    outer = jnp.einsum(
        "thd,the->dhe", key_heads, val_heads, preferred_element_type=jnp.float32
    ).reshape(DH, H * DH)
    norm_row = jnp.sum(key_feat, axis=0, dtype=jnp.float32)
    return jnp.concatenate([outer, norm_row[None, :]], axis=0)


def complex_total(own, block_complex):
    position = lax.axis_index(("sec", "blk"))
    blocks = block_complex.shape[0]
    mine = jnp.take(block_complex, position)
    total = own
    for reach in range(1, MOSTB):
        lower = from_behind(own.astype(jnp.bfloat16), ("sec", "blk"), reach).astype(own.dtype)
        upper = from_behind(own.astype(jnp.bfloat16), ("sec", "blk"), -reach).astype(own.dtype)
        below = jnp.take(block_complex, jnp.maximum(position - reach, 0))
        above = jnp.take(block_complex, jnp.minimum(position + reach, blocks - 1))
        take_lower = jnp.logical_and(position - reach >= 0, below == mine)
        take_upper = jnp.logical_and(position + reach < blocks, above == mine)
        total = total + jnp.where(take_lower, lower, 0.0) + jnp.where(take_upper, upper, 0.0)
    return total


def send(value, axis, pairs):
    return lax.ppermute(value, axis, pairs)


def complex_sum(own, block_complex, narrow=None):
    axis = ("sec", "blk")
    count = lax.axis_size(axis)
    position = lax.axis_index(axis)
    last = block_complex.shape[0] - 1

    def complex_of(block):
        return jnp.take(block_complex, jnp.clip(block, 0, last))

    def kept(value, block, target):
        inside = jnp.logical_and(target >= 0, target <= last)
        return jnp.where(jnp.logical_and(inside, complex_of(block) == complex_of(target)), value, 0.0)

    if narrow is None:
        narrow = own.astype(jnp.bfloat16)
    twin = position ^ 1
    sibling = send(narrow, axis, [(s, s ^ 1) for s in range(count)]).astype(own.dtype)
    odd = position % 2 == 1
    far_target = jnp.where(odd, position + 3, position - 3)
    far = send(
        kept(own, position, far_target).astype(jnp.bfloat16),
        axis,
        [(s, s + 3) for s in range(1, count - 3, 2)] + [(s, s - 3) for s in range(4, count, 2)],
    )
    low = jnp.where(odd, sibling, own)
    high = jnp.where(odd, own, sibling)
    first = position - position % 2

    def chip_part(target):
        return (kept(low, first, target) + kept(high, first + 1, target)).astype(jnp.bfloat16)

    even_chip = (position // 2) % 2 == 0
    pairs_a = [(s, s + 2 if (s // 2) % 2 == 0 else s - 2) for s in range(count)]
    pairs_b = [
        (s, s + 2 if (s // 2) % 2 else s - 2)
        for s in range(count)
        if 0 <= (s + 2 if (s // 2) % 2 else s - 2) < count
    ]
    up = send(
        chip_part(jnp.where(even_chip, position + 2, position - 2)), axis, pairs_a
    )
    down = send(
        chip_part(jnp.where(even_chip, position - 2, position + 2)), axis, pairs_b
    )
    total = own + kept(sibling, twin, position)
    return total + up.astype(own.dtype) + down.astype(own.dtype) + far.astype(own.dtype)


def pose_side(pose_rows, pair_rows, state, w_query, score_weight):
    count = pose_rows.shape[0]
    queries = jnp.dot(pose_rows, w_query, preferred_element_type=jnp.float32)
    query_heads = features(queries).reshape(count, H, DH)
    state_heads = state[:DH].reshape(DH, H, DH)
    norm_heads = state[DH].reshape(H, DH)
    numer = jnp.einsum("phd,dhe->phe", query_heads, state_heads, precision=highest)
    denom = jnp.sum(query_heads * norm_heads[None], axis=2)
    attended = numer / denom[:, :, None]
    weight_heads = score_weight.reshape(H, DH)
    scores = jnp.sum(attended * weight_heads[None], axis=(1, 2))
    slots = lax.broadcasted_iota(jnp.int32, (pair_rows.shape[0], count), 1)
    is_better = slots == pair_rows[:, 0:1]
    is_worse = slots == pair_rows[:, 1:2]
    better = jnp.sum(jnp.where(is_better, scores[None, :], 0.0), axis=1)
    worse = jnp.sum(jnp.where(is_worse, scores[None, :], 0.0), axis=1)
    delta = worse - better
    pair_loss = jax.nn.softplus(delta)
    push = jax.nn.sigmoid(delta)
    score_grad = jnp.sum(
        jnp.where(is_worse, push[:, None], 0.0) - jnp.where(is_better, push[:, None], 0.0),
        axis=0,
    )
    attended_grad = score_grad[:, None, None] * weight_heads[None]
    numer_grad = attended_grad / denom[:, :, None]
    denom_grad = -jnp.sum(attended_grad * attended, axis=2) / denom
    outer_grad = jnp.einsum("phd,phe->dhe", query_heads, numer_grad, precision=highest).reshape(
        DH, H * DH
    )
    norm_grad = jnp.sum(query_heads * denom_grad[:, :, None], axis=0).reshape(H * DH)
    pose_state = jnp.concatenate([outer_grad, norm_grad[None, :]], axis=0)
    feat_grad = (
        jnp.einsum("phe,dhe->phd", numer_grad, state_heads, precision=highest)
        + denom_grad[:, :, None] * norm_heads[None]
    )
    query_grad = (feat_grad.reshape(count, H * DH) * slope(queries)).astype(jnp.bfloat16)
    pose_grad = lax.dot_general(
        query_grad, w_query, (((1,), (1,)), ((), ())), preferred_element_type=jnp.float32
    )
    return (pair_loss, pose_grad.astype(jnp.bfloat16), pose_state)


def pose_kernel(
    pose_ref, pair_ref, state_ref, query_ref, weight_ref, loss_ref, grad_ref, back_ref, narrow_ref,
    feat_ref,
):
    count, width = pose_ref.shape
    lanes = 2 * DH
    queries = jnp.dot(pose_ref[...], query_ref[...], preferred_element_type=jnp.float32)
    query_feat = features(queries)
    norm = state_ref[DH : DH + 1, :]
    weight = weight_ref[...]
    head_row = lax.broadcasted_iota(jnp.int32, (lanes, lanes), 0) // DH
    head_col = lax.broadcasted_iota(jnp.int32, (lanes, lanes), 1) // DH
    same = head_row == head_col
    ones = same.astype(jnp.float32)
    blocks, numers, denoms = [], [], []
    scores = jnp.zeros((count, 1), jnp.float32)
    for g in range(width // lanes):
        cols = slice(g * lanes, (g + 1) * lanes)
        part = state_ref[0:DH, cols]
        block = jnp.where(same, jnp.concatenate([part, part], axis=0), 0.0)
        feat = query_feat[:, cols]
        numer = jnp.dot(feat, block, precision=highest, preferred_element_type=jnp.float32)
        denom = jnp.dot(
            feat * norm[:, cols], ones, precision=highest, preferred_element_type=jnp.float32
        )
        attended = numer / denom
        scores = scores + jnp.sum(attended * weight[:, cols], axis=1, keepdims=True)
        blocks.append(block)
        numers.append(attended)
        denoms.append(denom)
    slots = lax.broadcasted_iota(jnp.int32, (count, pair_ref.shape[1]), 0)
    is_better = slots == pair_ref[0:1, :]
    is_worse = slots == pair_ref[1:2, :]
    better = jnp.sum(jnp.where(is_better, scores, 0.0), axis=0, keepdims=True)
    worse = jnp.sum(jnp.where(is_worse, scores, 0.0), axis=0, keepdims=True)
    delta = worse - better
    loss_ref[...] = jnp.maximum(delta, 0.0) + jnp.log1p(jnp.exp(-jnp.abs(delta)))
    push = 1.0 / (1.0 + jnp.exp(-delta))
    score_grad = jnp.sum(
        jnp.where(is_worse, push, 0.0) - jnp.where(is_better, push, 0.0), axis=1, keepdims=True
    )
    low = lax.broadcasted_iota(jnp.int32, (DH, lanes), 1) < DH
    for g in range(width // lanes):
        cols = slice(g * lanes, (g + 1) * lanes)
        feat = query_feat[:, cols]
        attended_grad = score_grad * weight[:, cols]
        numer_grad = attended_grad / denoms[g]
        denom_grad = -jnp.dot(
            attended_grad * numers[g], ones, precision=highest, preferred_element_type=jnp.float32
        ) / denoms[g]
        outer = jnp.dot(feat.T, numer_grad, precision=highest, preferred_element_type=jnp.float32)
        back_ref[0:DH, cols] = jnp.where(low, outer[:DH], outer[DH:])
        back_ref[DH : DH + 1, cols] = jnp.sum(feat * denom_grad, axis=0, keepdims=True)
        feat_grad = lax.dot_general(
            numer_grad,
            blocks[g],
            (((1,), (1,)), ((), ())),
            precision=highest,
            preferred_element_type=jnp.float32,
        ) + denom_grad * norm[:, cols]
        feat_ref[:, cols] = (feat_grad * slope(queries[:, cols])).astype(feat_ref.dtype)
    narrow_ref[...] = back_ref[...].astype(narrow_ref.dtype)
    grad = lax.dot_general(
        feat_ref[...], query_ref[...], (((1,), (1,)), ((), ())), preferred_element_type=jnp.float32
    )
    grad_ref[...] = grad.astype(grad_ref.dtype)


def pose_fused(pose_rows, pair_rows, state, w_query, score_weight, interpret=False):
    count, width = pose_rows.shape
    pairs_t = pair_rows.T
    loss, grad, back, narrow = pl.pallas_call(
        pose_kernel,
        out_shape=(
            jax.ShapeDtypeStruct((1, pair_rows.shape[0]), jnp.float32),
            jax.ShapeDtypeStruct((count, width), jnp.bfloat16),
            jax.ShapeDtypeStruct(state.shape, jnp.float32),
            jax.ShapeDtypeStruct(state.shape, jnp.bfloat16),
        ),
        scratch_shapes=[pltpu.VMEM((count, width), jnp.bfloat16)],
        interpret=interpret,
    )(pose_rows, pairs_t, state, w_query, score_weight.reshape(1, width))
    return (loss.reshape(pair_rows.shape[0]), grad, (back, narrow))


def back_kernel(feat_ref, val_ref, keys_ref, grad_ref, full_ref, out_ref, both_ref):
    width = feat_ref.shape[1]
    lanes = 2 * DH
    head_row = lax.broadcasted_iota(jnp.int32, (lanes, lanes), 0) // DH
    head_col = lax.broadcasted_iota(jnp.int32, (lanes, lanes), 1) // DH
    same = head_row == head_col
    for g in range(width // lanes):
        cols = slice(g * lanes, (g + 1) * lanes)
        part = grad_ref[0:DH, cols].astype(jnp.float32)
        block = jnp.where(same, jnp.concatenate([part, part], axis=0), 0.0).astype(jnp.bfloat16)
        feat_grad = lax.dot_general(
            val_ref[:, cols], block, (((1,), (1,)), ((), ())), preferred_element_type=jnp.float32
        ) + grad_ref[DH : DH + 1, cols].astype(jnp.float32)
        both_ref[:, cols] = (feat_grad * slope(keys_ref[:, cols])).astype(both_ref.dtype)
        value_grad = jnp.dot(feat_ref[:, cols], block, preferred_element_type=jnp.float32)
        both_ref[:, width + g * lanes : width + (g + 1) * lanes] = value_grad.astype(both_ref.dtype)
    total = lax.dot_general(
        both_ref[...], full_ref[...], (((1,), (1,)), ((), ())), preferred_element_type=jnp.float32
    )
    out_ref[...] = total.astype(out_ref.dtype)


def back_fused(key_feat, val_round, keys, state_grad, full_both, interpret=False):
    rows, width = key_feat.shape
    return pl.pallas_call(
        back_kernel,
        out_shape=jax.ShapeDtypeStruct((rows, width), jnp.bfloat16),
        scratch_shapes=[pltpu.VMEM((rows, 2 * width), jnp.bfloat16)],
        interpret=interpret,
    )(key_feat, val_round, keys, state_grad, full_both)


def gather_rows(shard):
    count = lax.axis_size("blk")
    if count != 8:
        return lax.all_gather(shard, "blk", axis=0, tiled=True), None
    position = lax.axis_index("blk")
    rows = shard.shape[0]
    odd = position % 2
    first = jnp.where(odd == 1, 4, 2)
    second = 6 - first
    swap = [(s, s ^ 1) for s in range(count)]
    twin_own = lax.ppermute(shard, "blk", swap)
    early = lax.ppermute(shard, "blk", [(s, s ^ (4 if s % 2 else 2)) for s in range(count)])
    twin_early = lax.ppermute(early, "blk", swap)
    late = lax.ppermute(
        jnp.stack([shard, early]), "blk", [(s, s ^ (2 if s % 2 else 4)) for s in range(count)]
    )
    twin_late = lax.ppermute(late, "blk", swap)
    twin = position ^ 1
    sources = [
        ([shard, twin_own, early, twin_early], [position, twin, position ^ first, twin ^ second]),
        ([late[0], late[1]], [position ^ second, position ^ 6]),
    ]
    full = jnp.zeros((count,) + shard.shape, shard.dtype)
    for pieces, where in sources:
        for k, at in enumerate(where):
            full = lax.dynamic_update_slice(full, pieces[k][None], (at, 0, 0))
    return full, (twin_late, [twin ^ first, twin ^ 6])


def shards(receptor, poses, pairs, block_complex, w_key, w_value, w_query, score_weight):
    rows = receptor.shape[0]
    width = receptor.shape[1]
    full_both, rest = gather_rows(jnp.concatenate([w_key, w_value], axis=1))
    if rest is None:
        both = jnp.dot(receptor, full_both, preferred_element_type=jnp.float32)
    else:
        pieces, where = rest
        part = full_both.shape[1]
        both = jnp.dot(
            receptor, full_both.reshape(-1, full_both.shape[2]), preferred_element_type=jnp.float32
        )
        picked = jnp.concatenate(
            [lax.dynamic_slice_in_dim(receptor, at * part, part, axis=1) for at in where], axis=1
        )
        both = both + jnp.dot(
            picked, pieces.reshape(-1, pieces.shape[2]), preferred_element_type=jnp.float32
        )
        for k, at in enumerate(where):
            full_both = lax.dynamic_update_slice(full_both, pieces[k][None], (at, 0, 0))
        full_both = full_both.reshape(-1, full_both.shape[2])
    keys = both[:, :width]
    values = both[:, width:]
    key_feat = features(keys).astype(jnp.bfloat16)
    val_round = values.astype(jnp.bfloat16)
    state = complex_sum(local_state(key_feat, val_round), block_complex)
    pair_loss, pose_grad, pose_state = pose_fused(poses, pairs, state, w_query, score_weight)
    state_grad = complex_sum(pose_state[0], block_complex, pose_state[1]).astype(jnp.bfloat16)
    total = back_fused(key_feat, val_round, keys, state_grad, full_both)
    return (pair_loss, pose_grad, total)


def solution(mesh):
    placed = (
        P(("sec", "blk"), None),
        P(("sec", "blk"), None),
        P(("sec", "blk"), None),
        P(),
        P("blk", None),
        P("blk", None),
        P(),
        P(),
    )
    return jax.shard_map(
        shards,
        mesh=mesh,
        in_specs=placed,
        out_specs=(P(("sec", "blk")), P(("sec", "blk"), None), P(("sec", "blk"), None)),
        check_vma=False,
    )
```

```python
import jax
import jax.numpy as jnp
from jax import lax
from jax.sharding import PartitionSpec as P
from jax.experimental import pallas as pl
from jax.experimental.pallas import tpu as pltpu

H = 16
DH = 64
MOSTB = 4


highest = lax.Precision.HIGHEST


def from_behind(value, axis, steps):
    count = lax.axis_size(axis)
    initial, last = (max(0, -steps), min(count, count - steps))
    return lax.ppermute(value, axis, [(source, source + steps) for source in range(initial, last)])


def features(values):
    return jnp.where(values > 0, values + 1.0, jnp.exp(jnp.minimum(values, 0.0)))


def slope(values):
    return jnp.where(values > 0, jnp.ones_like(values), jnp.exp(jnp.minimum(values, 0.0)))


def local_state(key_feat, val_round):
    rows = key_feat.shape[0]
    key_heads = key_feat.reshape(rows, H, DH)
    val_heads = val_round.reshape(rows, H, DH)
    outer = jnp.einsum(
        "thd,the->dhe", key_heads, val_heads, preferred_element_type=jnp.float32
    ).reshape(DH, H * DH)
    norm_row = jnp.sum(key_feat, axis=0, dtype=jnp.float32)
    return jnp.concatenate([outer, norm_row[None, :]], axis=0)


def complex_total(own, block_complex):
    position = lax.axis_index(("sec", "blk"))
    blocks = block_complex.shape[0]
    mine = jnp.take(block_complex, position)
    total = own
    for reach in range(1, MOSTB):
        lower = from_behind(own.astype(jnp.bfloat16), ("sec", "blk"), reach).astype(own.dtype)
        upper = from_behind(own.astype(jnp.bfloat16), ("sec", "blk"), -reach).astype(own.dtype)
        below = jnp.take(block_complex, jnp.maximum(position - reach, 0))
        above = jnp.take(block_complex, jnp.minimum(position + reach, blocks - 1))
        take_lower = jnp.logical_and(position - reach >= 0, below == mine)
        take_upper = jnp.logical_and(position + reach < blocks, above == mine)
        total = total + jnp.where(take_lower, lower, 0.0) + jnp.where(take_upper, upper, 0.0)
    return total


def send(value, axis, pairs):
    return lax.ppermute(value, axis, pairs)


def complex_sum(own, block_complex, narrow=None, split=False):
    axis = ("sec", "blk")
    count = lax.axis_size(axis)
    position = lax.axis_index(axis)
    last = block_complex.shape[0] - 1

    def complex_of(block):
        return jnp.take(block_complex, jnp.clip(block, 0, last))

    def kept(value, block, target):
        inside = jnp.logical_and(target >= 0, target <= last)
        return jnp.where(jnp.logical_and(inside, complex_of(block) == complex_of(target)), value, 0.0)

    if narrow is None:
        narrow = own.astype(jnp.bfloat16)
    twin = position ^ 1
    sibling = send(narrow, axis, [(s, s ^ 1) for s in range(count)]).astype(own.dtype)
    odd = position % 2 == 1
    far_target = jnp.where(odd, position + 3, position - 3)
    far = send(
        kept(own, position, far_target).astype(jnp.bfloat16),
        axis,
        [(s, s + 3) for s in range(1, count - 3, 2)] + [(s, s - 3) for s in range(4, count, 2)],
    )
    low = jnp.where(odd, sibling, own)
    high = jnp.where(odd, own, sibling)
    first = position - position % 2

    def chip_part(target):
        return (kept(low, first, target) + kept(high, first + 1, target)).astype(jnp.bfloat16)

    even_chip = (position // 2) % 2 == 0
    pairs_a = [(s, s + 2 if (s // 2) % 2 == 0 else s - 2) for s in range(count)]
    pairs_b = [
        (s, s + 2 if (s // 2) % 2 else s - 2)
        for s in range(count)
        if 0 <= (s + 2 if (s // 2) % 2 else s - 2) < count
    ]
    up = send(
        chip_part(jnp.where(even_chip, position + 2, position - 2)), axis, pairs_a
    )
    down = send(
        chip_part(jnp.where(even_chip, position - 2, position + 2)), axis, pairs_b
    )
    if split:
        alike = jnp.logical_and(twin <= last, complex_of(twin) == complex_of(position))
        return own, sibling, alike.astype(own.dtype).reshape(1, 1), up, down, far
    total = own + kept(sibling, twin, position)
    return total + up.astype(own.dtype) + down.astype(own.dtype) + far.astype(own.dtype)


def add_terms(own_ref, twin_ref, alike_ref, up_ref, down_ref, far_ref):
    total = own_ref[...] + twin_ref[...].astype(jnp.float32) * alike_ref[...]
    for ref in (up_ref, down_ref, far_ref):
        total = total + ref[...].astype(jnp.float32)
    return total


def pose_side(pose_rows, pair_rows, state, w_query, score_weight):
    count = pose_rows.shape[0]
    queries = jnp.dot(pose_rows, w_query, preferred_element_type=jnp.float32)
    query_heads = features(queries).reshape(count, H, DH)
    state_heads = state[:DH].reshape(DH, H, DH)
    norm_heads = state[DH].reshape(H, DH)
    numer = jnp.einsum("phd,dhe->phe", query_heads, state_heads, precision=highest)
    denom = jnp.sum(query_heads * norm_heads[None], axis=2)
    attended = numer / denom[:, :, None]
    weight_heads = score_weight.reshape(H, DH)
    scores = jnp.sum(attended * weight_heads[None], axis=(1, 2))
    slots = lax.broadcasted_iota(jnp.int32, (pair_rows.shape[0], count), 1)
    is_better = slots == pair_rows[:, 0:1]
    is_worse = slots == pair_rows[:, 1:2]
    better = jnp.sum(jnp.where(is_better, scores[None, :], 0.0), axis=1)
    worse = jnp.sum(jnp.where(is_worse, scores[None, :], 0.0), axis=1)
    delta = worse - better
    pair_loss = jax.nn.softplus(delta)
    push = jax.nn.sigmoid(delta)
    score_grad = jnp.sum(
        jnp.where(is_worse, push[:, None], 0.0) - jnp.where(is_better, push[:, None], 0.0),
        axis=0,
    )
    attended_grad = score_grad[:, None, None] * weight_heads[None]
    numer_grad = attended_grad / denom[:, :, None]
    denom_grad = -jnp.sum(attended_grad * attended, axis=2) / denom
    outer_grad = jnp.einsum("phd,phe->dhe", query_heads, numer_grad, precision=highest).reshape(
        DH, H * DH
    )
    norm_grad = jnp.sum(query_heads * denom_grad[:, :, None], axis=0).reshape(H * DH)
    pose_state = jnp.concatenate([outer_grad, norm_grad[None, :]], axis=0)
    feat_grad = (
        jnp.einsum("phe,dhe->phd", numer_grad, state_heads, precision=highest)
        + denom_grad[:, :, None] * norm_heads[None]
    )
    query_grad = (feat_grad.reshape(count, H * DH) * slope(queries)).astype(jnp.bfloat16)
    pose_grad = lax.dot_general(
        query_grad, w_query, (((1,), (1,)), ((), ())), preferred_element_type=jnp.float32
    )
    return (pair_loss, pose_grad.astype(jnp.bfloat16), pose_state)


def pose_kernel(
    pose_ref, pair_ref, state_ref, query_ref, weight_ref, loss_ref, grad_ref, back_ref, narrow_ref,
    feat_ref,
):
    count, width = pose_ref.shape
    lanes = 2 * DH
    queries = jnp.dot(pose_ref[...], query_ref[...], preferred_element_type=jnp.float32)
    query_feat = features(queries)
    norm = state_ref[DH : DH + 1, :]
    weight = weight_ref[...]
    head_row = lax.broadcasted_iota(jnp.int32, (lanes, lanes), 0) // DH
    head_col = lax.broadcasted_iota(jnp.int32, (lanes, lanes), 1) // DH
    same = head_row == head_col
    ones = same.astype(jnp.float32)
    blocks, numers, denoms = [], [], []
    scores = jnp.zeros((count, 1), jnp.float32)
    for g in range(width // lanes):
        cols = slice(g * lanes, (g + 1) * lanes)
        part = state_ref[0:DH, cols]
        block = jnp.where(same, jnp.concatenate([part, part], axis=0), 0.0)
        feat = query_feat[:, cols]
        numer = jnp.dot(feat, block, precision=highest, preferred_element_type=jnp.float32)
        denom = jnp.dot(
            feat * norm[:, cols], ones, precision=highest, preferred_element_type=jnp.float32
        )
        attended = numer / denom
        scores = scores + jnp.sum(attended * weight[:, cols], axis=1, keepdims=True)
        blocks.append(block)
        numers.append(attended)
        denoms.append(denom)
    slots = lax.broadcasted_iota(jnp.int32, (count, pair_ref.shape[1]), 0)
    is_better = slots == pair_ref[0:1, :]
    is_worse = slots == pair_ref[1:2, :]
    better = jnp.sum(jnp.where(is_better, scores, 0.0), axis=0, keepdims=True)
    worse = jnp.sum(jnp.where(is_worse, scores, 0.0), axis=0, keepdims=True)
    delta = worse - better
    loss_ref[...] = jnp.maximum(delta, 0.0) + jnp.log1p(jnp.exp(-jnp.abs(delta)))
    push = 1.0 / (1.0 + jnp.exp(-delta))
    score_grad = jnp.sum(
        jnp.where(is_worse, push, 0.0) - jnp.where(is_better, push, 0.0), axis=1, keepdims=True
    )
    low = lax.broadcasted_iota(jnp.int32, (DH, lanes), 1) < DH
    for g in range(width // lanes):
        cols = slice(g * lanes, (g + 1) * lanes)
        feat = query_feat[:, cols]
        attended_grad = score_grad * weight[:, cols]
        numer_grad = attended_grad / denoms[g]
        denom_grad = -jnp.dot(
            attended_grad * numers[g], ones, precision=highest, preferred_element_type=jnp.float32
        ) / denoms[g]
        outer = jnp.dot(feat.T, numer_grad, precision=highest, preferred_element_type=jnp.float32)
        back_ref[0:DH, cols] = jnp.where(low, outer[:DH], outer[DH:])
        back_ref[DH : DH + 1, cols] = jnp.sum(feat * denom_grad, axis=0, keepdims=True)
        feat_grad = lax.dot_general(
            numer_grad,
            blocks[g],
            (((1,), (1,)), ((), ())),
            precision=highest,
            preferred_element_type=jnp.float32,
        ) + denom_grad * norm[:, cols]
        feat_ref[:, cols] = (feat_grad * slope(queries[:, cols])).astype(feat_ref.dtype)
    narrow_ref[...] = back_ref[...].astype(narrow_ref.dtype)
    grad = lax.dot_general(
        feat_ref[...], query_ref[...], (((1,), (1,)), ((), ())), preferred_element_type=jnp.float32
    )
    grad_ref[...] = grad.astype(grad_ref.dtype)


def pose_fused(pose_rows, pair_rows, state, w_query, score_weight, interpret=False):
    count, width = pose_rows.shape
    pairs_t = pair_rows.T
    loss, grad, back, narrow = pl.pallas_call(
        pose_kernel,
        out_shape=(
            jax.ShapeDtypeStruct((1, pair_rows.shape[0]), jnp.float32),
            jax.ShapeDtypeStruct((count, width), jnp.bfloat16),
            jax.ShapeDtypeStruct(state.shape, jnp.float32),
            jax.ShapeDtypeStruct(state.shape, jnp.bfloat16),
        ),
        scratch_shapes=[pltpu.VMEM((count, width), jnp.bfloat16)],
        interpret=interpret,
    )(pose_rows, pairs_t, state, w_query, score_weight.reshape(1, width))
    return (loss.reshape(pair_rows.shape[0]), grad, (back, narrow))


def back_kernel(feat_ref, val_ref, keys_ref, *refs):
    terms = refs[:6]
    full_ref, out_ref, both_ref, grad_ref = refs[6:]
    grad_ref[...] = add_terms(*terms).astype(grad_ref.dtype)
    width = feat_ref.shape[1]
    lanes = 2 * DH
    head_row = lax.broadcasted_iota(jnp.int32, (lanes, lanes), 0) // DH
    head_col = lax.broadcasted_iota(jnp.int32, (lanes, lanes), 1) // DH
    same = head_row == head_col
    for g in range(width // lanes):
        cols = slice(g * lanes, (g + 1) * lanes)
        part = grad_ref[0:DH, cols].astype(jnp.float32)
        block = jnp.where(same, jnp.concatenate([part, part], axis=0), 0.0).astype(jnp.bfloat16)
        feat_grad = lax.dot_general(
            val_ref[:, cols], block, (((1,), (1,)), ((), ())), preferred_element_type=jnp.float32
        ) + grad_ref[DH : DH + 1, cols].astype(jnp.float32)
        both_ref[:, cols] = (feat_grad * slope(keys_ref[:, cols])).astype(both_ref.dtype)
        value_grad = jnp.dot(feat_ref[:, cols], block, preferred_element_type=jnp.float32)
        both_ref[:, width + g * lanes : width + (g + 1) * lanes] = value_grad.astype(both_ref.dtype)
    total = lax.dot_general(
        both_ref[...], full_ref[...], (((1,), (1,)), ((), ())), preferred_element_type=jnp.float32
    )
    out_ref[...] = total.astype(out_ref.dtype)


def back_fused(key_feat, val_round, keys, state_grad, full_both, interpret=False):
    rows, width = key_feat.shape
    return pl.pallas_call(
        back_kernel,
        out_shape=jax.ShapeDtypeStruct((rows, width), jnp.bfloat16),
        scratch_shapes=[
            pltpu.VMEM((rows, 2 * width), jnp.bfloat16),
            pltpu.VMEM(state_grad[0].shape, jnp.bfloat16),
        ],
        interpret=interpret,
    )(key_feat, val_round, keys, *state_grad, full_both)


def gather_rows(shard):
    count = lax.axis_size("blk")
    if count != 8:
        return lax.all_gather(shard, "blk", axis=0, tiled=True), None
    position = lax.axis_index("blk")
    rows = shard.shape[0]
    odd = position % 2
    first = jnp.where(odd == 1, 4, 2)
    second = 6 - first
    swap = [(s, s ^ 1) for s in range(count)]
    twin_own = lax.ppermute(shard, "blk", swap)
    early = lax.ppermute(shard, "blk", [(s, s ^ (4 if s % 2 else 2)) for s in range(count)])
    twin_early = lax.ppermute(early, "blk", swap)
    late = lax.ppermute(
        jnp.stack([shard, early]), "blk", [(s, s ^ (2 if s % 2 else 4)) for s in range(count)]
    )
    twin_late = lax.ppermute(late, "blk", swap)
    twin = position ^ 1
    sources = [
        ([shard, twin_own, early, twin_early], [position, twin, position ^ first, twin ^ second]),
        ([late[0], late[1]], [position ^ second, position ^ 6]),
    ]
    full = jnp.zeros((count,) + shard.shape, shard.dtype)
    for pieces, where in sources:
        for k, at in enumerate(where):
            full = lax.dynamic_update_slice(full, pieces[k][None], (at, 0, 0))
    return full, (twin_late, [twin ^ first, twin ^ 6])


def shards(receptor, poses, pairs, block_complex, w_key, w_value, w_query, score_weight):
    rows = receptor.shape[0]
    width = receptor.shape[1]
    full_both, rest = gather_rows(jnp.concatenate([w_key, w_value], axis=1))
    if rest is None:
        both = jnp.dot(receptor, full_both, preferred_element_type=jnp.float32)
    else:
        pieces, where = rest
        part = full_both.shape[1]
        both = jnp.dot(
            receptor, full_both.reshape(-1, full_both.shape[2]), preferred_element_type=jnp.float32
        )
        picked = jnp.concatenate(
            [lax.dynamic_slice_in_dim(receptor, at * part, part, axis=1) for at in where], axis=1
        )
        both = both + jnp.dot(
            picked, pieces.reshape(-1, pieces.shape[2]), preferred_element_type=jnp.float32
        )
        for k, at in enumerate(where):
            full_both = lax.dynamic_update_slice(full_both, pieces[k][None], (at, 0, 0))
        full_both = full_both.reshape(-1, full_both.shape[2])
    keys = both[:, :width]
    values = both[:, width:]
    key_feat = features(keys).astype(jnp.bfloat16)
    val_round = values.astype(jnp.bfloat16)
    state = complex_sum(local_state(key_feat, val_round), block_complex)
    pair_loss, pose_grad, pose_state = pose_fused(poses, pairs, state, w_query, score_weight)
    state_grad = complex_sum(pose_state[0], block_complex, pose_state[1], split=True)
    total = back_fused(key_feat, val_round, keys, state_grad, full_both)
    return (pair_loss, pose_grad, total)


def solution(mesh):
    placed = (
        P(("sec", "blk"), None),
        P(("sec", "blk"), None),
        P(("sec", "blk"), None),
        P(),
        P("blk", None),
        P("blk", None),
        P(),
        P(),
    )
    return jax.shard_map(
        shards,
        mesh=mesh,
        in_specs=placed,
        out_specs=(P(("sec", "blk")), P(("sec", "blk"), None), P(("sec", "blk"), None)),
        check_vma=False,
    )
```

```python
import jax
import jax.numpy as jnp
from jax import lax
from jax.sharding import PartitionSpec as P
from jax.experimental import pallas as pl
from jax.experimental.pallas import tpu as pltpu

H = 16
DH = 64
MOSTB = 4


highest = lax.Precision.HIGHEST


def from_behind(value, axis, steps):
    count = lax.axis_size(axis)
    initial, last = (max(0, -steps), min(count, count - steps))
    return lax.ppermute(value, axis, [(source, source + steps) for source in range(initial, last)])


def features(values):
    return jnp.where(values > 0, values + 1.0, jnp.exp(jnp.minimum(values, 0.0)))


def slope(values):
    return jnp.where(values > 0, jnp.ones_like(values), jnp.exp(jnp.minimum(values, 0.0)))


def local_state(key_feat, val_round):
    rows = key_feat.shape[0]
    key_heads = key_feat.reshape(rows, H, DH)
    val_heads = val_round.reshape(rows, H, DH)
    outer = jnp.einsum(
        "thd,the->dhe", key_heads, val_heads, preferred_element_type=jnp.float32
    ).reshape(DH, H * DH)
    norm_row = jnp.sum(key_feat, axis=0, dtype=jnp.float32)
    return jnp.concatenate([outer, norm_row[None, :]], axis=0)


def complex_total(own, block_complex):
    position = lax.axis_index(("sec", "blk"))
    blocks = block_complex.shape[0]
    mine = jnp.take(block_complex, position)
    total = own
    for reach in range(1, MOSTB):
        lower = from_behind(own.astype(jnp.bfloat16), ("sec", "blk"), reach).astype(own.dtype)
        upper = from_behind(own.astype(jnp.bfloat16), ("sec", "blk"), -reach).astype(own.dtype)
        below = jnp.take(block_complex, jnp.maximum(position - reach, 0))
        above = jnp.take(block_complex, jnp.minimum(position + reach, blocks - 1))
        take_lower = jnp.logical_and(position - reach >= 0, below == mine)
        take_upper = jnp.logical_and(position + reach < blocks, above == mine)
        total = total + jnp.where(take_lower, lower, 0.0) + jnp.where(take_upper, upper, 0.0)
    return total


def send(value, axis, pairs):
    return lax.ppermute(value, axis, pairs)


def complex_sum(own, block_complex, narrow=None):
    axis = ("sec", "blk")
    count = lax.axis_size(axis)
    position = lax.axis_index(axis)
    last = block_complex.shape[0] - 1

    def complex_of(block):
        return jnp.take(block_complex, jnp.clip(block, 0, last))

    def kept(value, block, target):
        inside = jnp.logical_and(target >= 0, target <= last)
        return jnp.where(jnp.logical_and(inside, complex_of(block) == complex_of(target)), value, 0.0)

    if narrow is None:
        narrow = own.astype(jnp.bfloat16)
    twin = position ^ 1
    sibling = send(narrow, axis, [(s, s ^ 1) for s in range(count)]).astype(own.dtype)
    odd = position % 2 == 1
    far_target = jnp.where(odd, position + 3, position - 3)
    far = send(
        kept(own, position, far_target).astype(jnp.bfloat16),
        axis,
        [(s, s + 3) for s in range(1, count - 3, 2)] + [(s, s - 3) for s in range(4, count, 2)],
    )
    low = jnp.where(odd, sibling, own)
    high = jnp.where(odd, own, sibling)
    first = position - position % 2

    def chip_part(target):
        return (kept(low, first, target) + kept(high, first + 1, target)).astype(jnp.bfloat16)

    even_chip = (position // 2) % 2 == 0
    pairs_a = [(s, s + 2 if (s // 2) % 2 == 0 else s - 2) for s in range(count)]
    pairs_b = [
        (s, s + 2 if (s // 2) % 2 else s - 2)
        for s in range(count)
        if 0 <= (s + 2 if (s // 2) % 2 else s - 2) < count
    ]
    up = send(
        chip_part(jnp.where(even_chip, position + 2, position - 2)), axis, pairs_a
    )
    down = send(
        chip_part(jnp.where(even_chip, position - 2, position + 2)), axis, pairs_b
    )
    total = own + kept(sibling, twin, position)
    return total + up.astype(own.dtype) + down.astype(own.dtype) + far.astype(own.dtype)


def pose_side(pose_rows, pair_rows, state, w_query, score_weight):
    count = pose_rows.shape[0]
    queries = jnp.dot(pose_rows, w_query, preferred_element_type=jnp.float32)
    query_heads = features(queries).reshape(count, H, DH)
    state_heads = state[:DH].reshape(DH, H, DH)
    norm_heads = state[DH].reshape(H, DH)
    numer = jnp.einsum("phd,dhe->phe", query_heads, state_heads, precision=highest)
    denom = jnp.sum(query_heads * norm_heads[None], axis=2)
    attended = numer / denom[:, :, None]
    weight_heads = score_weight.reshape(H, DH)
    scores = jnp.sum(attended * weight_heads[None], axis=(1, 2))
    slots = lax.broadcasted_iota(jnp.int32, (pair_rows.shape[0], count), 1)
    is_better = slots == pair_rows[:, 0:1]
    is_worse = slots == pair_rows[:, 1:2]
    better = jnp.sum(jnp.where(is_better, scores[None, :], 0.0), axis=1)
    worse = jnp.sum(jnp.where(is_worse, scores[None, :], 0.0), axis=1)
    delta = worse - better
    pair_loss = jax.nn.softplus(delta)
    push = jax.nn.sigmoid(delta)
    score_grad = jnp.sum(
        jnp.where(is_worse, push[:, None], 0.0) - jnp.where(is_better, push[:, None], 0.0),
        axis=0,
    )
    attended_grad = score_grad[:, None, None] * weight_heads[None]
    numer_grad = attended_grad / denom[:, :, None]
    denom_grad = -jnp.sum(attended_grad * attended, axis=2) / denom
    outer_grad = jnp.einsum("phd,phe->dhe", query_heads, numer_grad, precision=highest).reshape(
        DH, H * DH
    )
    norm_grad = jnp.sum(query_heads * denom_grad[:, :, None], axis=0).reshape(H * DH)
    pose_state = jnp.concatenate([outer_grad, norm_grad[None, :]], axis=0)
    feat_grad = (
        jnp.einsum("phe,dhe->phd", numer_grad, state_heads, precision=highest)
        + denom_grad[:, :, None] * norm_heads[None]
    )
    query_grad = (feat_grad.reshape(count, H * DH) * slope(queries)).astype(jnp.bfloat16)
    pose_grad = lax.dot_general(
        query_grad, w_query, (((1,), (1,)), ((), ())), preferred_element_type=jnp.float32
    )
    return (pair_loss, pose_grad.astype(jnp.bfloat16), pose_state)


def pose_kernel(
    pose_ref, pair_ref, state_ref, query_ref, weight_ref, loss_ref, grad_ref, back_ref, narrow_ref,
    feat_ref,
):
    count, width = pose_ref.shape
    lanes = 2 * DH
    queries = jnp.dot(pose_ref[...], query_ref[...], preferred_element_type=jnp.float32)
    query_feat = features(queries)
    norm = state_ref[DH : DH + 1, :]
    weight = weight_ref[...]
    head_row = lax.broadcasted_iota(jnp.int32, (lanes, lanes), 0) // DH
    head_col = lax.broadcasted_iota(jnp.int32, (lanes, lanes), 1) // DH
    same = head_row == head_col
    ones = same.astype(jnp.float32)
    blocks, numers, denoms = [], [], []
    scores = jnp.zeros((count, 1), jnp.float32)
    for g in range(width // lanes):
        cols = slice(g * lanes, (g + 1) * lanes)
        part = state_ref[0:DH, cols]
        block = jnp.where(same, jnp.concatenate([part, part], axis=0), 0.0)
        feat = query_feat[:, cols]
        numer = jnp.dot(feat, block, precision=highest, preferred_element_type=jnp.float32)
        denom = jnp.dot(
            feat * norm[:, cols], ones, precision=highest, preferred_element_type=jnp.float32
        )
        attended = numer / denom
        scores = scores + jnp.sum(attended * weight[:, cols], axis=1, keepdims=True)
        blocks.append(block)
        numers.append(attended)
        denoms.append(denom)
    slots = lax.broadcasted_iota(jnp.int32, (count, pair_ref.shape[1]), 0)
    is_better = slots == pair_ref[0:1, :]
    is_worse = slots == pair_ref[1:2, :]
    better = jnp.sum(jnp.where(is_better, scores, 0.0), axis=0, keepdims=True)
    worse = jnp.sum(jnp.where(is_worse, scores, 0.0), axis=0, keepdims=True)
    delta = worse - better
    loss_ref[...] = jnp.maximum(delta, 0.0) + jnp.log1p(jnp.exp(-jnp.abs(delta)))
    push = 1.0 / (1.0 + jnp.exp(-delta))
    score_grad = jnp.sum(
        jnp.where(is_worse, push, 0.0) - jnp.where(is_better, push, 0.0), axis=1, keepdims=True
    )
    low = lax.broadcasted_iota(jnp.int32, (DH, lanes), 1) < DH
    for g in range(width // lanes):
        cols = slice(g * lanes, (g + 1) * lanes)
        feat = query_feat[:, cols]
        attended_grad = score_grad * weight[:, cols]
        numer_grad = attended_grad / denoms[g]
        denom_grad = -jnp.dot(
            attended_grad * numers[g], ones, precision=highest, preferred_element_type=jnp.float32
        ) / denoms[g]
        outer = jnp.dot(feat.T, numer_grad, precision=highest, preferred_element_type=jnp.float32)
        back_ref[0:DH, cols] = jnp.where(low, outer[:DH], outer[DH:])
        back_ref[DH : DH + 1, cols] = jnp.sum(feat * denom_grad, axis=0, keepdims=True)
        feat_grad = lax.dot_general(
            numer_grad,
            blocks[g],
            (((1,), (1,)), ((), ())),
            precision=highest,
            preferred_element_type=jnp.float32,
        ) + denom_grad * norm[:, cols]
        feat_ref[:, cols] = (feat_grad * slope(queries[:, cols])).astype(feat_ref.dtype)
    narrow_ref[...] = back_ref[...].astype(narrow_ref.dtype)
    grad = lax.dot_general(
        feat_ref[...], query_ref[...], (((1,), (1,)), ((), ())), preferred_element_type=jnp.float32
    )
    grad_ref[...] = grad.astype(grad_ref.dtype)


def pose_fused(pose_rows, pair_rows, state, w_query, score_weight, interpret=False):
    count, width = pose_rows.shape
    pairs_t = pair_rows.T
    loss, grad, back, narrow = pl.pallas_call(
        pose_kernel,
        out_shape=(
            jax.ShapeDtypeStruct((1, pair_rows.shape[0]), jnp.float32),
            jax.ShapeDtypeStruct((count, width), jnp.bfloat16),
            jax.ShapeDtypeStruct(state.shape, jnp.float32),
            jax.ShapeDtypeStruct(state.shape, jnp.bfloat16),
        ),
        scratch_shapes=[pltpu.VMEM((count, width), jnp.bfloat16)],
        interpret=interpret,
    )(pose_rows, pairs_t, state, w_query, score_weight.reshape(1, width))
    return (loss.reshape(pair_rows.shape[0]), grad, (back, narrow))


def back_kernel(feat_ref, val_ref, keys_ref, grad_ref, full_ref, out_ref, both_ref):
    width = feat_ref.shape[1]
    lanes = 2 * DH
    head_row = lax.broadcasted_iota(jnp.int32, (lanes, lanes), 0) // DH
    head_col = lax.broadcasted_iota(jnp.int32, (lanes, lanes), 1) // DH
    same = head_row == head_col
    for g in range(width // lanes):
        cols = slice(g * lanes, (g + 1) * lanes)
        part = grad_ref[0:DH, cols].astype(jnp.float32)
        block = jnp.where(same, jnp.concatenate([part, part], axis=0), 0.0).astype(jnp.bfloat16)
        feat_grad = lax.dot_general(
            val_ref[:, cols], block, (((1,), (1,)), ((), ())), preferred_element_type=jnp.float32
        ) + grad_ref[DH : DH + 1, cols].astype(jnp.float32)
        both_ref[:, cols] = (feat_grad * slope(keys_ref[:, cols])).astype(both_ref.dtype)
        value_grad = jnp.dot(feat_ref[:, cols], block, preferred_element_type=jnp.float32)
        both_ref[:, width + g * lanes : width + (g + 1) * lanes] = value_grad.astype(both_ref.dtype)
    total = lax.dot_general(
        both_ref[...], full_ref[...], (((1,), (1,)), ((), ())), preferred_element_type=jnp.float32
    )
    out_ref[...] = total.astype(out_ref.dtype)


def back_fused(key_feat, val_round, keys, state_grad, full_both, interpret=False):
    rows, width = key_feat.shape
    return pl.pallas_call(
        back_kernel,
        out_shape=jax.ShapeDtypeStruct((rows, width), jnp.bfloat16),
        scratch_shapes=[pltpu.VMEM((rows, 2 * width), jnp.bfloat16)],
        interpret=interpret,
    )(key_feat, val_round, keys, state_grad, full_both)


def gather_rows(shard, halves):
    count = lax.axis_size("blk")
    if count != 8:
        return lax.all_gather(shard, "blk", axis=0, tiled=True), None
    position = lax.axis_index("blk")
    rows = shard.shape[0]
    odd = position % 2
    first = jnp.where(odd == 1, 4, 2)
    second = 6 - first
    swap = [(s, s ^ 1) for s in range(count)]
    twin_own = lax.ppermute(shard, "blk", swap)
    early = jnp.concatenate(
        lax.ppermute(halves, "blk", [(s, s ^ (4 if s % 2 else 2)) for s in range(count)]), axis=1
    )
    twin_early = lax.ppermute(early, "blk", swap)
    late = lax.ppermute(
        jnp.stack([shard, early]), "blk", [(s, s ^ (2 if s % 2 else 4)) for s in range(count)]
    )
    twin_late = lax.ppermute(late, "blk", swap)
    twin = position ^ 1
    sources = [
        ([shard, twin_own, early, twin_early], [position, twin, position ^ first, twin ^ second]),
        ([late[0], late[1]], [position ^ second, position ^ 6]),
    ]
    full = jnp.zeros((count,) + shard.shape, shard.dtype)
    for pieces, where in sources:
        for k, at in enumerate(where):
            full = lax.dynamic_update_slice(full, pieces[k][None], (at, 0, 0))
    return full, (twin_late, [twin ^ first, twin ^ 6])


def shards(receptor, poses, pairs, block_complex, w_key, w_value, w_query, score_weight):
    rows = receptor.shape[0]
    width = receptor.shape[1]
    full_both, rest = gather_rows(jnp.concatenate([w_key, w_value], axis=1), (w_key, w_value))
    if rest is None:
        both = jnp.dot(receptor, full_both, preferred_element_type=jnp.float32)
    else:
        pieces, where = rest
        part = full_both.shape[1]
        both = jnp.dot(
            receptor, full_both.reshape(-1, full_both.shape[2]), preferred_element_type=jnp.float32
        )
        picked = jnp.concatenate(
            [lax.dynamic_slice_in_dim(receptor, at * part, part, axis=1) for at in where], axis=1
        )
        both = both + jnp.dot(
            picked, pieces.reshape(-1, pieces.shape[2]), preferred_element_type=jnp.float32
        )
        for k, at in enumerate(where):
            full_both = lax.dynamic_update_slice(full_both, pieces[k][None], (at, 0, 0))
        full_both = full_both.reshape(-1, full_both.shape[2])
    keys = both[:, :width]
    values = both[:, width:]
    key_feat = features(keys).astype(jnp.bfloat16)
    val_round = values.astype(jnp.bfloat16)
    state = complex_sum(local_state(key_feat, val_round), block_complex)
    pair_loss, pose_grad, pose_state = pose_fused(poses, pairs, state, w_query, score_weight)
    state_grad = complex_sum(pose_state[0], block_complex, pose_state[1]).astype(jnp.bfloat16)
    total = back_fused(key_feat, val_round, keys, state_grad, full_both)
    return (pair_loss, pose_grad, total)


def solution(mesh):
    placed = (
        P(("sec", "blk"), None),
        P(("sec", "blk"), None),
        P(("sec", "blk"), None),
        P(),
        P("blk", None),
        P("blk", None),
        P(),
        P(),
    )
    return jax.shard_map(
        shards,
        mesh=mesh,
        in_specs=placed,
        out_specs=(P(("sec", "blk")), P(("sec", "blk"), None), P(("sec", "blk"), None)),
        check_vma=False,
    )
```
